32 devices in a mesh: light: 4 (over z), view: 4 (over x, core), across: 2 (over y).
Axes of the slice: x: 2, y: 2, z: 4, core: 2. Of those that a mesh axis runs over, the one named last changes fastest.
Arguments:
- density: float32 [64, 64, 512], P('light', 'across', 'view'), may hold values from 0 to 1
- labels: int32 [64, 64, 512], P('light', 'across', 'view'), may hold values from 0 to 15
- sunlight: float32 [3, 64, 512], P(None, 'across', 'view'), may hold values from 0.18 to 2.8
- opacity_table: float32 [16], replicated, may hold values from 0.5 to 8
- extinction_table: float32 [3, 16], replicated, may hold values from 0.02 to 4
- albedo_table: float32 [3, 16], replicated, may hold values from 0.2 to 1
Outputs:
- image: float32 [4, 64, 64], P(None, ('light', 'view'), 'across')
The draws below stay inside these ranges and needn't reach their ends.
All inputs are finite; a program needn't handle non-finite values.
Results may differ from the reference program's by a relative error of at most 0.0003.
Values sent between devices are 32-bit elements; how exact they have to be, the bound alone decides.
No kernel may reach another device: no remote copies, remote signals or barrier semaphores. Data moves between devices by JAX's collectives and lax.ppermute only.
A program may use at most 64 MiB of HBM per device.

```python
import math
import jax
import jax.numpy as jnp
import numpy as np
from jax import lax

BA = 32
BV = 128
SLABS = 8
MATS = 16
NL = 64
NA = 64
NV = 512
N_LIGHT = 4


def spread_blocks(levels):
    return jnp.repeat(jnp.repeat(levels, BA, axis=0), BV, axis=1)


def block_pattern(key):
    shared = jax.random.fold_in(key, 11)
    parity_key, density_key, bright_key = jax.random.split(shared, 3)
    blocks_across = NA // BA
    blocks_view = NV // BV
    phase_bit = jax.random.randint(parity_key, (), 0, 2)
    parity = (jnp.arange(blocks_across, dtype=jnp.int32)[:, None] + jnp.arange(blocks_view, dtype=jnp.int32)[None, :] + phase_bit) % 2
    dense_block = parity == 1
    density_mix = jax.random.uniform(density_key, (blocks_across, blocks_view), jnp.float32)
    bright_mix = jax.random.uniform(bright_key, (blocks_across, blocks_view), jnp.float32)
    density_level = jnp.where(dense_block, 0.8 + 0.2 * density_mix, 0.06 + 0.09 * density_mix)
    sun_level = jnp.where(dense_block, 0.3 + 0.3 * bright_mix, 1.5 + 0.5 * bright_mix)
    return (spread_blocks(density_level), spread_blocks(sun_level))


def draw_density(key, part):
    density_level, sun_level = block_pattern(key)
    rough_key = jax.random.fold_in(key, 23)
    uniform_cells = jax.random.uniform(rough_key, (NL, NA, NV), jnp.float32)
    factor = 0.3 + 0.7 * uniform_cells
    return density_level[None] * factor


def draw_sunlight(key, part):
    density_level, sun_level = block_pattern(key)
    rough_key = jax.random.fold_in(key, 37)
    uniform_cells = jax.random.uniform(rough_key, (3, NA, NV), jnp.float32)
    factor = 0.6 + 0.8 * uniform_cells
    return sun_level[None] * factor


def touch_ends(array, rng, least, top_value):
    dims = array.shape
    index_at = [jax.random.randint(jax.random.fold_in(rng, axis), (), 0, dims[axis]) for axis in range(len(dims))]
    array = array.at[tuple(index_at)].set(least)
    longest = dims.index(max(dims))
    index_at[longest] = (index_at[longest] + 1) % dims[longest]
    return array.at[tuple(index_at)].set(top_value)


def rank_table(count, slope):
    loads = [(1 << 20) // math.isqrt(rank ** slope) + 1 for rank in range(1, count + 1)]
    width = 1 + sum(loads) // (1 << 30)
    return np.cumsum(np.array([max(1, weight // width) for weight in loads]))


def ranked_ids(rng, dims, number_of, slope):
    listing = rank_table(number_of, slope)
    pick = jax.random.randint(jax.random.fold_in(rng, 1), dims, 0, int(listing[number_of - 1]))
    grade = jnp.searchsorted(jnp.asarray(listing, jnp.int32), pick, side="right")
    return jax.random.permutation(jax.random.fold_in(rng, 2), number_of)[grade].astype(jnp.int32)


def setup_inputs(seed: int = 0) -> dict:
    streams_of = jax.random.split(jax.random.key(seed), 7)
    return {
        "density": draw_density(jax.random.fold_in(streams_of[6], 71), 0),
        "labels": touch_ends(ranked_ids(streams_of[1], (NL, NA, NV), MATS, 1), jax.random.fold_in(streams_of[1], 3), 0, MATS - 1).astype(jnp.int32),
        "sunlight": draw_sunlight(jax.random.fold_in(streams_of[6], 71), 0),
        "opacity_table": jnp.clip(jnp.exp(jax.random.uniform(streams_of[3], (MATS,), jnp.float32, math.log(0.5), math.log(8.0))), 0.5, 8.0),
        "extinction_table": jnp.clip(jnp.exp(jax.random.uniform(streams_of[4], (3, MATS), jnp.float32, math.log(0.02), math.log(4.0))), 0.02, 4.0),
        "albedo_table": jnp.clip(jax.random.uniform(streams_of[5], (3, MATS), jnp.float32, 0.2, 1.0), 0.2, 1.0),
    }


BLUR = 0.24
AMBIENT = 0.1
SOFTEN = 0.05


def shade_from(tensor):
    centre = tensor[:, 1:-1, 1:-1, 1:-1]
    smooth = (2.0 * centre + tensor[:, 2:, 1:-1, 1:-1] + tensor[:, :-2, 1:-1, 1:-1]
              + tensor[:, 1:-1, 2:, 1:-1] + tensor[:, 1:-1, :-2, 1:-1]
              + tensor[:, 1:-1, 1:-1, 2:] + tensor[:, 1:-1, 1:-1, :-2]) * 0.125
    aligned = (0.64 * smooth[0] + 0.1296 * smooth[1] + 0.2304 * smooth[2]
               + 0.576 * smooth[3] + 0.768 * smooth[4] + 0.3456 * smooth[5])
    trace_sum = smooth[0] + smooth[1] + smooth[2]
    return 0.25 + aligned / (trace_sum + SOFTEN)


def structure(window):
    slope_light = (window[2:, 1:-1, 1:-1] - window[:-2, 1:-1, 1:-1]) * 0.5
    slope_across = (window[1:-1, 2:, 1:-1] - window[1:-1, :-2, 1:-1]) * 0.5
    slope_view = (window[1:-1, 1:-1, 2:] - window[1:-1, 1:-1, :-2]) * 0.5
    return jnp.stack([slope_light * slope_light, slope_across * slope_across, slope_view * slope_view,
                      slope_light * slope_across, slope_light * slope_view, slope_across * slope_view])


def blur_plane(plane_in):
    padded = jnp.pad(plane_in, ((0, 0), (1, 1), (1, 1)))
    return plane_in + BLUR * (padded[:, :-2, 1:-1] + padded[:, 2:, 1:-1] + padded[:, 1:-1, :-2]
                              + padded[:, 1:-1, 2:] - 4.0 * plane_in)


def reference(density, labels, sunlight, opacity_table, extinction_table, albedo_table):
    layer_rows = NL // (N_LIGHT * SLABS)
    slab_count = NL // layer_rows
    padded = jnp.pad(density, 2)
    light_step = 10.0 / NL
    view_step = 2.0 / NV
    across_index = jnp.arange(NA + 2)
    keep_across = ((across_index >= 1) & (across_index <= NA)).astype(jnp.float32)
    view_index = jnp.arange(NV + 2)
    keep_view = ((view_index >= 1) & (view_index <= NV)).astype(jnp.float32)

    def one_slab(plane_in, slab_num):
        first_row = (slab_num * layer_rows).astype(jnp.int32)
        zero = jnp.zeros((), jnp.int32)
        window = lax.dynamic_slice(padded, (first_row, zero, zero), (layer_rows + 4, NA + 4, NV + 4))
        row_index = first_row - 1 + jnp.arange(layer_rows + 2, dtype=jnp.int32)
        keep_rows = ((row_index >= 0) & (row_index < NL)).astype(jnp.float32)
        inside = keep_rows[:, None, None] * keep_across[None, :, None] * keep_view[None, None, :]
        tensor = structure(window) * inside[None]
        shading = shade_from(tensor)
        cells = lax.dynamic_slice(density, (first_row, zero, zero), (layer_rows, NA, NV))
        material = lax.dynamic_slice(labels, (first_row, zero, zero), (layer_rows, NA, NV))
        extinct = extinction_table[:, material] * cells[None]
        running = jnp.cumsum(extinct, axis=1) - extinct
        lighting = plane_in[:, None] * jnp.exp(-light_step * running)
        slab_depth = jnp.sum(extinct, axis=1)
        plane_next = blur_plane(plane_in * jnp.exp(-light_step * slab_depth))
        optical = opacity_table[material] * cells * view_step
        colour = (1.0 - jnp.exp(-optical))[None] * albedo_table[:, material] * (shading[None] * lighting + AMBIENT)
        before = jnp.cumsum(optical, axis=-1) - optical
        colour_sum = jnp.sum(colour * jnp.exp(-before)[None], axis=-1)
        opacity = 1.0 - jnp.exp(-jnp.sum(optical, axis=-1))
        return plane_next, jnp.concatenate([colour_sum, opacity[None]], axis=0)

    final_plane, images = lax.scan(one_slab, sunlight, jnp.arange(slab_count, dtype=jnp.int32))
    return images.transpose(1, 0, 2, 3).reshape(4, NL, NA)
```

```python
import jax
import jax.numpy as jnp
from jax import lax
from jax.sharding import PartitionSpec as P

SLABS = 8


BLUR = 0.24
AMBIENT = 0.1
SOFTEN = 0.05


def padded_2(block, sides, width):
    for axis, dim in sides:
        count = lax.axis_size(axis)
        forward = [(i, i + 1) for i in range(count - 1)]
        backward = [(target, source) for source, target in forward]
        low = lax.ppermute(
            lax.slice_in_dim(block, block.shape[dim] - width, None, axis=dim), axis, forward
        )
        high = lax.ppermute(lax.slice_in_dim(block, 0, width, axis=dim), axis, backward)
        block = jnp.concatenate([low, block, high], axis=dim)
    return block


def from_behind(value, axis, steps):
    count = lax.axis_size(axis)
    leading, last = (max(0, -steps), min(count, count - steps))
    return lax.ppermute(value, axis, [(source, source + steps) for source in range(leading, last)])


def from_partner(block, axis, apart):
    count = lax.axis_size(axis)
    route = []
    for low in range(count):
        high = low | 1 << apart
        if high != low and high < count:
            route += [(low, high), (high, low)]
    return lax.ppermute(block, axis, route)


def shade_from(tensor):
    centre = tensor[:, 1:-1, 1:-1, 1:-1]
    smooth = (
        2.0 * centre
        + tensor[:, 2:, 1:-1, 1:-1]
        + tensor[:, :-2, 1:-1, 1:-1]
        + tensor[:, 1:-1, 2:, 1:-1]
        + tensor[:, 1:-1, :-2, 1:-1]
        + tensor[:, 1:-1, 1:-1, 2:]
        + tensor[:, 1:-1, 1:-1, :-2]
    ) * 0.125
    aligned = (
        0.64 * smooth[0]
        + 0.1296 * smooth[1]
        + 0.2304 * smooth[2]
        + 0.576 * smooth[3]
        + 0.768 * smooth[4]
        + 0.3456 * smooth[5]
    )
    trace_sum = smooth[0] + smooth[1] + smooth[2]
    return 0.25 + aligned / (trace_sum + SOFTEN)


def structure(window):
    slope_light = (window[2:, 1:-1, 1:-1] - window[:-2, 1:-1, 1:-1]) * 0.5
    slope_across = (window[1:-1, 2:, 1:-1] - window[1:-1, :-2, 1:-1]) * 0.5
    slope_view = (window[1:-1, 1:-1, 2:] - window[1:-1, 1:-1, :-2]) * 0.5
    return jnp.stack(
        [
            slope_light * slope_light,
            slope_across * slope_across,
            slope_view * slope_view,
            slope_light * slope_across,
            slope_light * slope_view,
            slope_across * slope_view,
        ]
    )


def rim_mask(position, devices, width, border):
    places = position * width - border + jnp.arange(width + 2 * border, dtype=jnp.int32)
    return ((places >= 0) & (places < devices * width)).astype(jnp.float32)


def propagate(current, depth_rim, plane_inside, brick_a, brick_v, light_step):
    starts = []
    for slab_num in range(SLABS):
        border = SLABS - slab_num
        starts.append(current[:, border : border + brick_a, border : border + brick_v])
        depth_here = depth_rim[
            :,
            slab_num,
            slab_num : slab_num + brick_a + 2 * border,
            slab_num : slab_num + brick_v + 2 * border,
        ]
        current = current * jnp.exp(-light_step * depth_here)
        centre = current[:, 1:-1, 1:-1]
        current = centre + BLUR * (
            current[:, :-2, 1:-1]
            + current[:, 2:, 1:-1]
            + current[:, 1:-1, :-2]
            + current[:, 1:-1, 2:]
            - 4.0 * centre
        )
        inner = border - 1
        current = (
            current
            * plane_inside[
                slab_num + 1 : slab_num + 1 + brick_a + 2 * inner,
                slab_num + 1 : slab_num + 1 + brick_v + 2 * inner,
            ][None]
        )
    return (current, jnp.stack(starts, axis=1))


def shards(density, labels, sunlight, opacity_table, extinction_table, albedo_table):
    brick_l, brick_a, brick_v = density.shape
    n_light = lax.axis_size("light")
    n_view = lax.axis_size("view")
    n_across = lax.axis_size("across")
    full_l = brick_l * n_light
    full_v = brick_v * n_view
    light_step = 10.0 / full_l
    view_step = 2.0 / full_v
    layer_rows = brick_l // SLABS
    light_idx = lax.axis_index("light")
    view_idx = lax.axis_index("view")
    across_idx = lax.axis_index("across")
    padded = padded_2(density, (("light", 0), ("view", 2), ("across", 1)), 2)
    inside = (
        rim_mask(light_idx, n_light, brick_l, 1)[:, None, None]
        * rim_mask(across_idx, n_across, brick_a, 1)[None, :, None]
        * rim_mask(view_idx, n_view, brick_v, 1)[None, None, :]
    )
    tensor_rim = structure(padded) * inside[None]
    shading = shade_from(tensor_rim)
    table_all = jnp.concatenate([opacity_table[None], extinction_table, albedo_table], axis=0)
    looked = jnp.broadcast_to(table_all[:, 0, None, None, None], (7,) + labels.shape)
    for material in range(1, table_all.shape[1]):
        looked = jnp.where(
            (labels == material)[None], table_all[:, material, None, None, None], looked
        )
    extinct = looked[1:4] * density[None]
    extinct_slabs = extinct.reshape(3, SLABS, layer_rows, brick_a, brick_v)
    running = jnp.cumsum(extinct_slabs, axis=2) - extinct_slabs
    slab_depth = jnp.sum(extinct_slabs, axis=2)
    depth_rim = padded_2(slab_depth, (("view", 3), ("across", 2)), SLABS)
    plane_inside = (
        rim_mask(across_idx, n_across, brick_a, SLABS)[:, None]
        * rim_mask(view_idx, n_view, brick_v, SLABS)[None, :]
    )
    starts = None
    incoming = sunlight
    for section_num in range(n_light):
        current = padded_2(incoming, (("view", 2), ("across", 1)), SLABS)
        outgoing, starts = propagate(current, depth_rim, plane_inside, brick_a, brick_v, light_step)
        if section_num + 1 < n_light:
            arrived = from_behind(outgoing, "light", 1)
            incoming = jnp.where(light_idx == 0, sunlight, arrived)
    lighting = (starts[:, :, None] * jnp.exp(-light_step * running)).reshape(
        3, brick_l, brick_a, brick_v
    )
    optical = looked[0] * density * view_step
    colour = (1.0 - jnp.exp(-optical))[None] * looked[4:7] * (shading[None] * lighting + AMBIENT)
    upper = (jnp.arange(brick_v)[:, None] < jnp.arange(brick_v)[None, :]).astype(jnp.float32)
    before = jnp.dot(optical.reshape(-1, brick_v), upper, precision=lax.Precision.HIGHEST).reshape(
        brick_l, brick_a, brick_v
    )
    colour_sum = jnp.sum(colour * jnp.exp(-before)[None], axis=-1)
    transmit = jnp.exp(-jnp.sum(optical, axis=-1))
    pixels = brick_l * brick_a
    piece_len = pixels // n_view
    colour_now = colour_sum.reshape(3, n_view, piece_len)
    transmit_now = transmit.reshape(1, n_view, piece_len)
    bit_count = n_view.bit_length() - 1
    for bit_num in range(bit_count):
        kept = colour_now.shape[1]
        colour_pairs = colour_now.reshape(3, kept // 2, 2, piece_len)
        transmit_pairs = transmit_now.reshape(1, kept // 2, 2, piece_len)
        my_bit = view_idx // 2**bit_num % 2
        first_half = my_bit == 0
        keep_colour = jnp.where(first_half, colour_pairs[:, :, 0], colour_pairs[:, :, 1])
        send_colour = jnp.where(first_half, colour_pairs[:, :, 1], colour_pairs[:, :, 0])
        keep_transmit = jnp.where(first_half, transmit_pairs[:, :, 0], transmit_pairs[:, :, 1])
        send_transmit = jnp.where(first_half, transmit_pairs[:, :, 1], transmit_pairs[:, :, 0])
        got_colour, got_transmit = from_partner((send_colour, send_transmit), "view", bit_num)
        front_colour = jnp.where(first_half, keep_colour, got_colour)
        back_colour = jnp.where(first_half, got_colour, keep_colour)
        front_transmit = jnp.where(first_half, keep_transmit, got_transmit)
        colour_now = front_colour + front_transmit * back_colour
        transmit_now = keep_transmit * got_transmit
    final_colour = colour_now[:, 0]
    final_transmit = transmit_now[:, 0]
    rows_out = brick_l // n_view
    opacity = 1.0 - final_transmit.reshape(1, rows_out, brick_a)
    return jnp.concatenate([final_colour.reshape(3, rows_out, brick_a), opacity], axis=0)


def solution(mesh):
    in_specs = (
        P("light", "across", "view"),
        P("light", "across", "view"),
        P(None, "across", "view"),
        P(),
        P(),
        P(),
    )
    out_specs = P(None, ("light", "view"), "across")
    return jax.shard_map(shards, mesh=mesh, in_specs=in_specs, out_specs=out_specs, check_vma=False)
```

```python
import jax
import jax.numpy as jnp
from jax import lax
from jax.sharding import PartitionSpec as P

SLABS = 8


BLUR = 0.24
AMBIENT = 0.1
SOFTEN = 0.05


def padded_2(block, sides, width):
    for axis, dim in sides:
        count = lax.axis_size(axis)
        forward = [(i, i + 1) for i in range(count - 1)]
        backward = [(target, source) for source, target in forward]
        low = lax.ppermute(
            lax.slice_in_dim(block, block.shape[dim] - width, None, axis=dim), axis, forward
        )
        high = lax.ppermute(lax.slice_in_dim(block, 0, width, axis=dim), axis, backward)
        block = jnp.concatenate([low, block, high], axis=dim)
    return block


def from_behind(value, axis, steps):
    count = lax.axis_size(axis)
    leading, last = (max(0, -steps), min(count, count - steps))
    return lax.ppermute(value, axis, [(source, source + steps) for source in range(leading, last)])


def from_partner(block, axis, apart):
    count = lax.axis_size(axis)
    route = []
    for low in range(count):
        high = low | 1 << apart
        if high != low and high < count:
            route += [(low, high), (high, low)]
    return lax.ppermute(block, axis, route)


def shade_from(tensor):
    centre = tensor[:, 1:-1, 1:-1, 1:-1]
    smooth = (
        2.0 * centre
        + tensor[:, 2:, 1:-1, 1:-1]
        + tensor[:, :-2, 1:-1, 1:-1]
        + tensor[:, 1:-1, 2:, 1:-1]
        + tensor[:, 1:-1, :-2, 1:-1]
        + tensor[:, 1:-1, 1:-1, 2:]
        + tensor[:, 1:-1, 1:-1, :-2]
    ) * 0.125
    aligned = (
        0.64 * smooth[0]
        + 0.1296 * smooth[1]
        + 0.2304 * smooth[2]
        + 0.576 * smooth[3]
        + 0.768 * smooth[4]
        + 0.3456 * smooth[5]
    )
    trace_sum = smooth[0] + smooth[1] + smooth[2]
    return 0.25 + aligned / (trace_sum + SOFTEN)


def structure(window):
    slope_light = (window[2:, 1:-1, 1:-1] - window[:-2, 1:-1, 1:-1]) * 0.5
    slope_across = (window[1:-1, 2:, 1:-1] - window[1:-1, :-2, 1:-1]) * 0.5
    slope_view = (window[1:-1, 1:-1, 2:] - window[1:-1, 1:-1, :-2]) * 0.5
    return jnp.stack(
        [
            slope_light * slope_light,
            slope_across * slope_across,
            slope_view * slope_view,
            slope_light * slope_across,
            slope_light * slope_view,
            slope_across * slope_view,
        ]
    )


def rim_mask(position, devices, width, border):
    places = position * width - border + jnp.arange(width + 2 * border, dtype=jnp.int32)
    return ((places >= 0) & (places < devices * width)).astype(jnp.float32)


def halo(block, axis, dim, width):
    count = lax.axis_size(axis)
    size = block.shape[dim]
    lows, highs = [], []
    for hop in range(1, count):
        need = min(size, width - (hop - 1) * size)
        if need <= 0:
            break
        forward = [(i, i + hop) for i in range(count - hop)]
        backward = [(target, source) for source, target in forward]
        low = lax.slice_in_dim(block, size - need, None, axis=dim)
        lows.insert(0, lax.ppermute(low, axis, forward))
        highs.append(lax.ppermute(lax.slice_in_dim(block, 0, need, axis=dim), axis, backward))
    block = jnp.concatenate(lows + [block] + highs, axis=dim)
    missing = width - sum(part.shape[dim] for part in lows)
    if missing > 0:
        widths = [(0, 0)] * block.ndim
        widths[dim] = (missing, missing)
        block = jnp.pad(block, widths)
    return block


def propagate(current, border_in, depth_rim, plane_inside, brick_a, brick_v, light_step):
    widest = (depth_rim.shape[2] - brick_a) // 2
    starts = []
    for slab_num in range(SLABS):
        border = border_in - slab_num
        starts.append(current[:, border : border + brick_a, border : border + brick_v])
        offset = widest - border
        depth_here = depth_rim[
            :,
            slab_num,
            offset : offset + brick_a + 2 * border,
            offset : offset + brick_v + 2 * border,
        ]
        current = current * jnp.exp(-light_step * depth_here)
        centre = current[:, 1:-1, 1:-1]
        current = centre + BLUR * (
            current[:, :-2, 1:-1]
            + current[:, 2:, 1:-1]
            + current[:, 1:-1, :-2]
            + current[:, 1:-1, 2:]
            - 4.0 * centre
        )
        inner = border - 1
        offset = widest - inner
        current = (
            current
            * plane_inside[
                offset : offset + brick_a + 2 * inner,
                offset : offset + brick_v + 2 * inner,
            ][None]
        )
    return (current, jnp.stack(starts, axis=1))


def shards(density, labels, sunlight, opacity_table, extinction_table, albedo_table):
    brick_l, brick_a, brick_v = density.shape
    n_light = lax.axis_size("light")
    n_view = lax.axis_size("view")
    n_across = lax.axis_size("across")
    full_l = brick_l * n_light
    full_v = brick_v * n_view
    light_step = 10.0 / full_l
    view_step = 2.0 / full_v
    layer_rows = brick_l // SLABS
    light_idx = lax.axis_index("light")
    view_idx = lax.axis_index("view")
    across_idx = lax.axis_index("across")
    padded = padded_2(density, (("light", 0), ("view", 2), ("across", 1)), 2)
    inside = (
        rim_mask(light_idx, n_light, brick_l, 1)[:, None, None]
        * rim_mask(across_idx, n_across, brick_a, 1)[None, :, None]
        * rim_mask(view_idx, n_view, brick_v, 1)[None, None, :]
    )
    tensor_rim = structure(padded) * inside[None]
    shading = shade_from(tensor_rim)
    table_all = jnp.concatenate([opacity_table[None], extinction_table, albedo_table], axis=0)
    looked = jnp.broadcast_to(table_all[:, 0, None, None, None], (7,) + labels.shape)
    for material in range(1, table_all.shape[1]):
        looked = jnp.where(
            (labels == material)[None], table_all[:, material, None, None, None], looked
        )
    extinct = looked[1:4] * density[None]
    extinct_slabs = extinct.reshape(3, SLABS, layer_rows, brick_a, brick_v)
    running = jnp.cumsum(extinct_slabs, axis=2) - extinct_slabs
    slab_depth = jnp.sum(extinct_slabs, axis=2)
    widest = SLABS * n_light
    depth_rim = halo(halo(slab_depth, "across", 2, widest), "view", 3, widest)
    sun_rim = halo(halo(sunlight, "across", 1, widest), "view", 2, widest)
    plane_inside = (
        rim_mask(across_idx, n_across, brick_a, widest)[:, None]
        * rim_mask(view_idx, n_view, brick_v, widest)[None, :]
    )
    starts = None
    incoming = sun_rim
    for section_num in range(n_light):
        border = SLABS * (n_light - section_num)
        outgoing, starts = propagate(
            incoming, border, depth_rim, plane_inside, brick_a, brick_v, light_step
        )
        if section_num + 1 < n_light:
            arrived = from_behind(outgoing, "light", 1)
            cut = widest - border + SLABS
            sun_here = sun_rim[:, cut : cut + brick_a + 2 * (border - SLABS), cut : cut + brick_v + 2 * (border - SLABS)]
            incoming = jnp.where(light_idx == 0, sun_here, arrived)
    lighting = (starts[:, :, None] * jnp.exp(-light_step * running)).reshape(
        3, brick_l, brick_a, brick_v
    )
    optical = looked[0] * density * view_step
    colour = (1.0 - jnp.exp(-optical))[None] * looked[4:7] * (shading[None] * lighting + AMBIENT)
    upper = (jnp.arange(brick_v)[:, None] < jnp.arange(brick_v)[None, :]).astype(jnp.float32)
    before = jnp.dot(optical.reshape(-1, brick_v), upper, precision=lax.Precision.HIGHEST).reshape(
        brick_l, brick_a, brick_v
    )
    colour_sum = jnp.sum(colour * jnp.exp(-before)[None], axis=-1)
    transmit = jnp.exp(-jnp.sum(optical, axis=-1))
    pixels = brick_l * brick_a
    piece_len = pixels // n_view
    colour_now = colour_sum.reshape(3, n_view, piece_len)
    transmit_now = transmit.reshape(1, n_view, piece_len)
    bit_count = n_view.bit_length() - 1
    for bit_num in range(bit_count):
        kept = colour_now.shape[1]
        colour_pairs = colour_now.reshape(3, kept // 2, 2, piece_len)
        transmit_pairs = transmit_now.reshape(1, kept // 2, 2, piece_len)
        my_bit = view_idx // 2**bit_num % 2
        first_half = my_bit == 0
        keep_colour = jnp.where(first_half, colour_pairs[:, :, 0], colour_pairs[:, :, 1])
        send_colour = jnp.where(first_half, colour_pairs[:, :, 1], colour_pairs[:, :, 0])
        keep_transmit = jnp.where(first_half, transmit_pairs[:, :, 0], transmit_pairs[:, :, 1])
        send_transmit = jnp.where(first_half, transmit_pairs[:, :, 1], transmit_pairs[:, :, 0])
        got_colour, got_transmit = from_partner((send_colour, send_transmit), "view", bit_num)
        front_colour = jnp.where(first_half, keep_colour, got_colour)
        back_colour = jnp.where(first_half, got_colour, keep_colour)
        front_transmit = jnp.where(first_half, keep_transmit, got_transmit)
        colour_now = front_colour + front_transmit * back_colour
        transmit_now = keep_transmit * got_transmit
    final_colour = colour_now[:, 0]
    final_transmit = transmit_now[:, 0]
    rows_out = brick_l // n_view
    opacity = 1.0 - final_transmit.reshape(1, rows_out, brick_a)
    return jnp.concatenate([final_colour.reshape(3, rows_out, brick_a), opacity], axis=0)


def solution(mesh):
    in_specs = (
        P("light", "across", "view"),
        P("light", "across", "view"),
        P(None, "across", "view"),
        P(),
        P(),
        P(),
    )
    out_specs = P(None, ("light", "view"), "across")
    return jax.shard_map(shards, mesh=mesh, in_specs=in_specs, out_specs=out_specs, check_vma=False)
```

```python
import jax
import jax.numpy as jnp
from jax import lax
from jax.sharding import PartitionSpec as P

SLABS = 8


BLUR = 0.24
AMBIENT = 0.1
SOFTEN = 0.05


def padded_2(block, sides, width):
    for axis, dim in sides:
        count = lax.axis_size(axis)
        forward = [(i, i + 1) for i in range(count - 1)]
        backward = [(target, source) for source, target in forward]
        low = lax.ppermute(
            lax.slice_in_dim(block, block.shape[dim] - width, None, axis=dim), axis, forward
        )
        high = lax.ppermute(lax.slice_in_dim(block, 0, width, axis=dim), axis, backward)
        block = jnp.concatenate([low, block, high], axis=dim)
    return block


def from_behind(value, axis, steps):
    count = lax.axis_size(axis)
    leading, last = (max(0, -steps), min(count, count - steps))
    return lax.ppermute(value, axis, [(source, source + steps) for source in range(leading, last)])


def from_partner(block, axis, apart):
    count = lax.axis_size(axis)
    route = []
    for low in range(count):
        high = low | 1 << apart
        if high != low and high < count:
            route += [(low, high), (high, low)]
    return lax.ppermute(block, axis, route)


def shade_from(tensor):
    centre = tensor[:, 1:-1, 1:-1, 1:-1]
    smooth = (
        2.0 * centre
        + tensor[:, 2:, 1:-1, 1:-1]
        + tensor[:, :-2, 1:-1, 1:-1]
        + tensor[:, 1:-1, 2:, 1:-1]
        + tensor[:, 1:-1, :-2, 1:-1]
        + tensor[:, 1:-1, 1:-1, 2:]
        + tensor[:, 1:-1, 1:-1, :-2]
    ) * 0.125
    aligned = (
        0.64 * smooth[0]
        + 0.1296 * smooth[1]
        + 0.2304 * smooth[2]
        + 0.576 * smooth[3]
        + 0.768 * smooth[4]
        + 0.3456 * smooth[5]
    )
    trace_sum = smooth[0] + smooth[1] + smooth[2]
    return 0.25 + aligned / (trace_sum + SOFTEN)


def structure(window):
    slope_light = (window[2:, 1:-1, 1:-1] - window[:-2, 1:-1, 1:-1]) * 0.5
    slope_across = (window[1:-1, 2:, 1:-1] - window[1:-1, :-2, 1:-1]) * 0.5
    slope_view = (window[1:-1, 1:-1, 2:] - window[1:-1, 1:-1, :-2]) * 0.5
    return jnp.stack(
        [
            slope_light * slope_light,
            slope_across * slope_across,
            slope_view * slope_view,
            slope_light * slope_across,
            slope_light * slope_view,
            slope_across * slope_view,
        ]
    )


def rim_mask(position, devices, width, border):
    places = position * width - border + jnp.arange(width + 2 * border, dtype=jnp.int32)
    return ((places >= 0) & (places < devices * width)).astype(jnp.float32)


def halo(block, axis, dim, width):
    count = lax.axis_size(axis)
    size = block.shape[dim]
    lows, highs = [], []
    for hop in range(1, count):
        need = min(size, width - (hop - 1) * size)
        if need <= 0:
            break
        forward = [(i, i + hop) for i in range(count - hop)]
        backward = [(target, source) for source, target in forward]
        low = lax.slice_in_dim(block, size - need, None, axis=dim)
        lows.insert(0, lax.ppermute(low, axis, forward))
        highs.append(lax.ppermute(lax.slice_in_dim(block, 0, need, axis=dim), axis, backward))
    block = jnp.concatenate(lows + [block] + highs, axis=dim)
    missing = width - sum(part.shape[dim] for part in lows)
    if missing > 0:
        widths = [(0, 0)] * block.ndim
        widths[dim] = (missing, missing)
        block = jnp.pad(block, widths)
    return block


def plane_mask(border, brick_a, brick_v):
    return (
        rim_mask(lax.axis_index("across"), lax.axis_size("across"), brick_a, border)[:, None]
        * rim_mask(lax.axis_index("view"), lax.axis_size("view"), brick_v, border)[None, :]
    )


def propagate(current, border_in, depth_rim, brick_a, brick_v, light_step):
    widest = (depth_rim.shape[2] - brick_a) // 2
    starts = []
    for slab_num in range(SLABS):
        border = border_in - slab_num
        starts.append(current[:, border : border + brick_a, border : border + brick_v])
        offset = widest - border
        depth_here = depth_rim[
            :,
            slab_num,
            offset : offset + brick_a + 2 * border,
            offset : offset + brick_v + 2 * border,
        ]
        current = current * jnp.exp(-light_step * depth_here)
        centre = current[:, 1:-1, 1:-1]
        current = centre + BLUR * (
            current[:, :-2, 1:-1]
            + current[:, 2:, 1:-1]
            + current[:, 1:-1, :-2]
            + current[:, 1:-1, 2:]
            - 4.0 * centre
        )
        current = current * plane_mask(border - 1, brick_a, brick_v)[None]
    return (current, jnp.stack(starts, axis=1))


def shards(density, labels, sunlight, opacity_table, extinction_table, albedo_table):
    brick_l, brick_a, brick_v = density.shape
    n_light = lax.axis_size("light")
    n_view = lax.axis_size("view")
    n_across = lax.axis_size("across")
    full_l = brick_l * n_light
    full_v = brick_v * n_view
    light_step = 10.0 / full_l
    view_step = 2.0 / full_v
    layer_rows = brick_l // SLABS
    light_idx = lax.axis_index("light")
    view_idx = lax.axis_index("view")
    across_idx = lax.axis_index("across")
    padded = padded_2(density, (("light", 0), ("view", 2), ("across", 1)), 2)
    inside = (
        rim_mask(light_idx, n_light, brick_l, 1)[:, None, None]
        * rim_mask(across_idx, n_across, brick_a, 1)[None, :, None]
        * rim_mask(view_idx, n_view, brick_v, 1)[None, None, :]
    )
    tensor_rim = structure(padded) * inside[None]
    shading = shade_from(tensor_rim)
    table_all = jnp.concatenate([opacity_table[None], extinction_table, albedo_table], axis=0)
    looked = jnp.broadcast_to(table_all[:, 0, None, None, None], (7,) + labels.shape)
    for material in range(1, table_all.shape[1]):
        looked = jnp.where(
            (labels == material)[None], table_all[:, material, None, None, None], looked
        )
    extinct = looked[1:4] * density[None]
    extinct_slabs = extinct.reshape(3, SLABS, layer_rows, brick_a, brick_v)
    running = jnp.cumsum(extinct_slabs, axis=2) - extinct_slabs
    slab_depth = jnp.sum(extinct_slabs, axis=2)
    widest = SLABS * n_light
    both = jnp.concatenate([slab_depth, sunlight[:, None]], axis=1)
    both_rim = halo(halo(both, "across", 2, widest), "view", 3, widest)
    depth_rim = both_rim[:, :SLABS]
    sun_rim = both_rim[:, SLABS]
    starts = None
    incoming = sun_rim
    for section_num in range(n_light):
        border = SLABS * (n_light - section_num)
        outgoing, starts = propagate(
            incoming, border, depth_rim, brick_a, brick_v, light_step
        )
        if section_num + 1 < n_light:
            arrived = from_behind(outgoing, "light", 1)
            cut = widest - border + SLABS
            sun_here = sun_rim[:, cut : cut + brick_a + 2 * (border - SLABS), cut : cut + brick_v + 2 * (border - SLABS)]
            incoming = jnp.where(light_idx == 0, sun_here, arrived)
    lighting = (starts[:, :, None] * jnp.exp(-light_step * running)).reshape(
        3, brick_l, brick_a, brick_v
    )
    optical = looked[0] * density * view_step
    colour = (1.0 - jnp.exp(-optical))[None] * looked[4:7] * (shading[None] * lighting + AMBIENT)
    upper = (jnp.arange(brick_v)[:, None] < jnp.arange(brick_v)[None, :]).astype(jnp.float32)
    before = jnp.dot(optical.reshape(-1, brick_v), upper, precision=lax.Precision.HIGHEST).reshape(
        brick_l, brick_a, brick_v
    )
    colour_sum = jnp.sum(colour * jnp.exp(-before)[None], axis=-1)
    transmit = jnp.exp(-jnp.sum(optical, axis=-1))
    pixels = brick_l * brick_a
    piece_len = pixels // n_view
    colour_now = colour_sum.reshape(3, n_view, piece_len)
    transmit_now = transmit.reshape(1, n_view, piece_len)
    bit_count = n_view.bit_length() - 1
    for bit_num in range(bit_count):
        kept = colour_now.shape[1]
        colour_pairs = colour_now.reshape(3, kept // 2, 2, piece_len)
        transmit_pairs = transmit_now.reshape(1, kept // 2, 2, piece_len)
        my_bit = view_idx // 2**bit_num % 2
        first_half = my_bit == 0
        keep_colour = jnp.where(first_half, colour_pairs[:, :, 0], colour_pairs[:, :, 1])
        send_colour = jnp.where(first_half, colour_pairs[:, :, 1], colour_pairs[:, :, 0])
        keep_transmit = jnp.where(first_half, transmit_pairs[:, :, 0], transmit_pairs[:, :, 1])
        send_transmit = jnp.where(first_half, transmit_pairs[:, :, 1], transmit_pairs[:, :, 0])
        got_colour, got_transmit = from_partner((send_colour, send_transmit), "view", bit_num)
        front_colour = jnp.where(first_half, keep_colour, got_colour)
        back_colour = jnp.where(first_half, got_colour, keep_colour)
        front_transmit = jnp.where(first_half, keep_transmit, got_transmit)
        colour_now = front_colour + front_transmit * back_colour
        transmit_now = keep_transmit * got_transmit
    final_colour = colour_now[:, 0]
    final_transmit = transmit_now[:, 0]
    rows_out = brick_l // n_view
    opacity = 1.0 - final_transmit.reshape(1, rows_out, brick_a)
    return jnp.concatenate([final_colour.reshape(3, rows_out, brick_a), opacity], axis=0)


def solution(mesh):
    in_specs = (
        P("light", "across", "view"),
        P("light", "across", "view"),
        P(None, "across", "view"),
        P(),
        P(),
        P(),
    )
    out_specs = P(None, ("light", "view"), "across")
    return jax.shard_map(shards, mesh=mesh, in_specs=in_specs, out_specs=out_specs, check_vma=False)
```

```python
import jax
import jax.numpy as jnp
from jax import lax
from jax.sharding import PartitionSpec as P

SLABS = 8


BLUR = 0.24
AMBIENT = 0.1
SOFTEN = 0.05


def padded_2(block, sides, width):
    for axis, dim in sides:
        count = lax.axis_size(axis)
        forward = [(i, i + 1) for i in range(count - 1)]
        backward = [(target, source) for source, target in forward]
        low = lax.ppermute(
            lax.slice_in_dim(block, block.shape[dim] - width, None, axis=dim), axis, forward
        )
        high = lax.ppermute(lax.slice_in_dim(block, 0, width, axis=dim), axis, backward)
        block = jnp.concatenate([low, block, high], axis=dim)
    return block


def from_behind(value, axis, steps):
    count = lax.axis_size(axis)
    leading, last = (max(0, -steps), min(count, count - steps))
    return lax.ppermute(value, axis, [(source, source + steps) for source in range(leading, last)])


def from_partner(block, axis, apart):
    count = lax.axis_size(axis)
    route = []
    for low in range(count):
        high = low | 1 << apart
        if high != low and high < count:
            route += [(low, high), (high, low)]
    return lax.ppermute(block, axis, route)


def shade_from(tensor):
    centre = tensor[:, 1:-1, 1:-1, 1:-1]
    smooth = (
        2.0 * centre
        + tensor[:, 2:, 1:-1, 1:-1]
        + tensor[:, :-2, 1:-1, 1:-1]
        + tensor[:, 1:-1, 2:, 1:-1]
        + tensor[:, 1:-1, :-2, 1:-1]
        + tensor[:, 1:-1, 1:-1, 2:]
        + tensor[:, 1:-1, 1:-1, :-2]
    ) * 0.125
    aligned = (
        0.64 * smooth[0]
        + 0.1296 * smooth[1]
        + 0.2304 * smooth[2]
        + 0.576 * smooth[3]
        + 0.768 * smooth[4]
        + 0.3456 * smooth[5]
    )
    trace_sum = smooth[0] + smooth[1] + smooth[2]
    return 0.25 + aligned / (trace_sum + SOFTEN)


def structure(window):
    slope_light = (window[2:, 1:-1, 1:-1] - window[:-2, 1:-1, 1:-1]) * 0.5
    slope_across = (window[1:-1, 2:, 1:-1] - window[1:-1, :-2, 1:-1]) * 0.5
    slope_view = (window[1:-1, 1:-1, 2:] - window[1:-1, 1:-1, :-2]) * 0.5
    return jnp.stack(
        [
            slope_light * slope_light,
            slope_across * slope_across,
            slope_view * slope_view,
            slope_light * slope_across,
            slope_light * slope_view,
            slope_across * slope_view,
        ]
    )


def rim_mask(position, devices, width, border):
    places = position * width - border + jnp.arange(width + 2 * border, dtype=jnp.int32)
    return ((places >= 0) & (places < devices * width)).astype(jnp.float32)


def halo(block, axis, dim, width):
    count = lax.axis_size(axis)
    size = block.shape[dim]
    lows, highs = [], []
    for hop in range(1, count):
        need = min(size, width - (hop - 1) * size)
        if need <= 0:
            break
        forward = [(i, i + hop) for i in range(count - hop)]
        backward = [(target, source) for source, target in forward]
        low = lax.slice_in_dim(block, size - need, None, axis=dim)
        lows.insert(0, lax.ppermute(low, axis, forward))
        highs.append(lax.ppermute(lax.slice_in_dim(block, 0, need, axis=dim), axis, backward))
    block = jnp.concatenate(lows + [block] + highs, axis=dim)
    missing = width - sum(part.shape[dim] for part in lows)
    if missing > 0:
        widths = [(0, 0)] * block.ndim
        widths[dim] = (missing, missing)
        block = jnp.pad(block, widths)
    return block


def plane_mask(border, brick_a, brick_v):
    return (
        rim_mask(lax.axis_index("across"), lax.axis_size("across"), brick_a, border)[:, None]
        * rim_mask(lax.axis_index("view"), lax.axis_size("view"), brick_v, border)[None, :]
    )


def propagate(current, border_in, fade_rim, brick_a, brick_v):
    widest = (fade_rim.shape[2] - brick_a) // 2
    starts = []
    for slab_num in range(SLABS):
        border = border_in - slab_num
        starts.append(current[:, border : border + brick_a, border : border + brick_v])
        offset = widest - border
        fade_here = fade_rim[
            :,
            slab_num,
            offset : offset + brick_a + 2 * border,
            offset : offset + brick_v + 2 * border,
        ]
        current = current * fade_here
        centre = current[:, 1:-1, 1:-1]
        current = centre + BLUR * (
            current[:, :-2, 1:-1]
            + current[:, 2:, 1:-1]
            + current[:, 1:-1, :-2]
            + current[:, 1:-1, 2:]
            - 4.0 * centre
        )
    return (current, jnp.stack(starts, axis=1))


def shards(density, labels, sunlight, opacity_table, extinction_table, albedo_table):
    brick_l, brick_a, brick_v = density.shape
    n_light = lax.axis_size("light")
    n_view = lax.axis_size("view")
    n_across = lax.axis_size("across")
    full_l = brick_l * n_light
    full_v = brick_v * n_view
    light_step = 10.0 / full_l
    view_step = 2.0 / full_v
    layer_rows = brick_l // SLABS
    light_idx = lax.axis_index("light")
    view_idx = lax.axis_index("view")
    across_idx = lax.axis_index("across")
    padded = padded_2(density, (("light", 0), ("view", 2), ("across", 1)), 2)
    inside = (
        rim_mask(light_idx, n_light, brick_l, 1)[:, None, None]
        * rim_mask(across_idx, n_across, brick_a, 1)[None, :, None]
        * rim_mask(view_idx, n_view, brick_v, 1)[None, None, :]
    )
    tensor_rim = structure(padded) * inside[None]
    shading = shade_from(tensor_rim)
    table_all = jnp.concatenate([opacity_table[None], extinction_table, albedo_table], axis=0)
    looked = jnp.broadcast_to(table_all[:, 0, None, None, None], (7,) + labels.shape)
    for material in range(1, table_all.shape[1]):
        looked = jnp.where(
            (labels == material)[None], table_all[:, material, None, None, None], looked
        )
    extinct = looked[1:4] * density[None]
    extinct_slabs = extinct.reshape(3, SLABS, layer_rows, brick_a, brick_v)
    running = jnp.cumsum(extinct_slabs, axis=2) - extinct_slabs
    slab_depth = jnp.sum(extinct_slabs, axis=2)
    widest = SLABS * n_light
    both = jnp.concatenate([slab_depth, sunlight[:, None]], axis=1)
    both_rim = halo(halo(both, "across", 2, widest), "view", 3, widest)
    sun_rim = both_rim[:, SLABS]
    fade_rim = jnp.exp(-light_step * both_rim[:, :SLABS]) * plane_mask(widest, brick_a, brick_v)
    starts = None
    incoming = sun_rim
    for section_num in range(n_light):
        border = SLABS * (n_light - section_num)
        outgoing, starts = propagate(
            incoming, border, fade_rim, brick_a, brick_v
        )
        if section_num + 1 < n_light:
            arrived = from_behind(outgoing, "light", 1)
            cut = widest - border + SLABS
            sun_here = sun_rim[:, cut : cut + brick_a + 2 * (border - SLABS), cut : cut + brick_v + 2 * (border - SLABS)]
            incoming = jnp.where(light_idx == 0, sun_here, arrived)
    lighting = (starts[:, :, None] * jnp.exp(-light_step * running)).reshape(
        3, brick_l, brick_a, brick_v
    )
    optical = looked[0] * density * view_step
    colour = (1.0 - jnp.exp(-optical))[None] * looked[4:7] * (shading[None] * lighting + AMBIENT)
    upper = (jnp.arange(brick_v)[:, None] < jnp.arange(brick_v)[None, :]).astype(jnp.float32)
    before = jnp.dot(optical.reshape(-1, brick_v), upper, precision=lax.Precision.HIGHEST).reshape(
        brick_l, brick_a, brick_v
    )
    colour_sum = jnp.sum(colour * jnp.exp(-before)[None], axis=-1)
    transmit = jnp.exp(-jnp.sum(optical, axis=-1))
    pixels = brick_l * brick_a
    piece_len = pixels // n_view
    colour_now = colour_sum.reshape(3, n_view, piece_len)
    transmit_now = transmit.reshape(1, n_view, piece_len)
    bit_count = n_view.bit_length() - 1
    for bit_num in range(bit_count):
        kept = colour_now.shape[1]
        colour_pairs = colour_now.reshape(3, kept // 2, 2, piece_len)
        transmit_pairs = transmit_now.reshape(1, kept // 2, 2, piece_len)
        my_bit = view_idx // 2**bit_num % 2
        first_half = my_bit == 0
        keep_colour = jnp.where(first_half, colour_pairs[:, :, 0], colour_pairs[:, :, 1])
        send_colour = jnp.where(first_half, colour_pairs[:, :, 1], colour_pairs[:, :, 0])
        keep_transmit = jnp.where(first_half, transmit_pairs[:, :, 0], transmit_pairs[:, :, 1])
        send_transmit = jnp.where(first_half, transmit_pairs[:, :, 1], transmit_pairs[:, :, 0])
        got_colour, got_transmit = from_partner((send_colour, send_transmit), "view", bit_num)
        front_colour = jnp.where(first_half, keep_colour, got_colour)
        back_colour = jnp.where(first_half, got_colour, keep_colour)
        front_transmit = jnp.where(first_half, keep_transmit, got_transmit)
        colour_now = front_colour + front_transmit * back_colour
        transmit_now = keep_transmit * got_transmit
    final_colour = colour_now[:, 0]
    final_transmit = transmit_now[:, 0]
    rows_out = brick_l // n_view
    opacity = 1.0 - final_transmit.reshape(1, rows_out, brick_a)
    return jnp.concatenate([final_colour.reshape(3, rows_out, brick_a), opacity], axis=0)


def solution(mesh):
    in_specs = (
        P("light", "across", "view"),
        P("light", "across", "view"),
        P(None, "across", "view"),
        P(),
        P(),
        P(),
    )
    out_specs = P(None, ("light", "view"), "across")
    return jax.shard_map(shards, mesh=mesh, in_specs=in_specs, out_specs=out_specs, check_vma=False)
```

```python
import jax
import jax.numpy as jnp
from jax import lax
from jax.sharding import PartitionSpec as P

SLABS = 8


BLUR = 0.24
AMBIENT = 0.1
SOFTEN = 0.05


def padded_2(block, sides, width):
    for axis, dim in sides:
        count = lax.axis_size(axis)
        forward = [(i, i + 1) for i in range(count - 1)]
        backward = [(target, source) for source, target in forward]
        low = lax.ppermute(
            lax.slice_in_dim(block, block.shape[dim] - width, None, axis=dim), axis, forward
        )
        high = lax.ppermute(lax.slice_in_dim(block, 0, width, axis=dim), axis, backward)
        block = jnp.concatenate([low, block, high], axis=dim)
    return block


def from_behind(value, axis, steps):
    count = lax.axis_size(axis)
    leading, last = (max(0, -steps), min(count, count - steps))
    return lax.ppermute(value, axis, [(source, source + steps) for source in range(leading, last)])


def from_partner(block, axis, apart):
    count = lax.axis_size(axis)
    route = []
    for low in range(count):
        high = low | 1 << apart
        if high != low and high < count:
            route += [(low, high), (high, low)]
    return lax.ppermute(block, axis, route)


def smooth(field):
    centre = field[1:-1, 1:-1, 1:-1]
    return (
        2.0 * centre
        + field[2:, 1:-1, 1:-1]
        + field[:-2, 1:-1, 1:-1]
        + field[1:-1, 2:, 1:-1]
        + field[1:-1, :-2, 1:-1]
        + field[1:-1, 1:-1, 2:]
        + field[1:-1, 1:-1, :-2]
    ) * 0.125


def shade_from(window, inside):
    slope_light = (window[2:, 1:-1, 1:-1] - window[:-2, 1:-1, 1:-1]) * 0.5
    slope_across = (window[1:-1, 2:, 1:-1] - window[1:-1, :-2, 1:-1]) * 0.5
    slope_view = (window[1:-1, 1:-1, 2:] - window[1:-1, 1:-1, :-2]) * 0.5
    along = 0.8 * slope_light + 0.36 * slope_across + 0.48 * slope_view
    aligned = along * along * inside
    trace = (slope_light * slope_light + slope_across * slope_across + slope_view * slope_view) * inside
    return 0.25 + smooth(aligned) / (smooth(trace) + SOFTEN)


def rim_mask(position, devices, width, border):
    places = position * width - border + jnp.arange(width + 2 * border, dtype=jnp.int32)
    return ((places >= 0) & (places < devices * width)).astype(jnp.float32)


def halo(block, axis, dim, width):
    count = lax.axis_size(axis)
    size = block.shape[dim]
    lows, highs = [], []
    for hop in range(1, count):
        need = min(size, width - (hop - 1) * size)
        if need <= 0:
            break
        forward = [(i, i + hop) for i in range(count - hop)]
        backward = [(target, source) for source, target in forward]
        low = lax.slice_in_dim(block, size - need, None, axis=dim)
        lows.insert(0, lax.ppermute(low, axis, forward))
        highs.append(lax.ppermute(lax.slice_in_dim(block, 0, need, axis=dim), axis, backward))
    block = jnp.concatenate(lows + [block] + highs, axis=dim)
    missing = width - sum(part.shape[dim] for part in lows)
    if missing > 0:
        widths = [(0, 0)] * block.ndim
        widths[dim] = (missing, missing)
        block = jnp.pad(block, widths)
    return block


def plane_mask(border, brick_a, brick_v):
    return (
        rim_mask(lax.axis_index("across"), lax.axis_size("across"), brick_a, border)[:, None]
        * rim_mask(lax.axis_index("view"), lax.axis_size("view"), brick_v, border)[None, :]
    )


def propagate(current, border_in, fade_rim, brick_a, brick_v):
    widest = (fade_rim.shape[2] - brick_a) // 2
    starts = []
    for slab_num in range(SLABS):
        border = border_in - slab_num
        starts.append(current[:, border : border + brick_a, border : border + brick_v])
        offset = widest - border
        fade_here = fade_rim[
            :,
            slab_num,
            offset : offset + brick_a + 2 * border,
            offset : offset + brick_v + 2 * border,
        ]
        current = current * fade_here
        centre = current[:, 1:-1, 1:-1]
        current = centre + BLUR * (
            current[:, :-2, 1:-1]
            + current[:, 2:, 1:-1]
            + current[:, 1:-1, :-2]
            + current[:, 1:-1, 2:]
            - 4.0 * centre
        )
    return (current, jnp.stack(starts, axis=1))


def shards(density, labels, sunlight, opacity_table, extinction_table, albedo_table):
    brick_l, brick_a, brick_v = density.shape
    n_light = lax.axis_size("light")
    n_view = lax.axis_size("view")
    n_across = lax.axis_size("across")
    full_l = brick_l * n_light
    full_v = brick_v * n_view
    light_step = 10.0 / full_l
    view_step = 2.0 / full_v
    layer_rows = brick_l // SLABS
    light_idx = lax.axis_index("light")
    view_idx = lax.axis_index("view")
    across_idx = lax.axis_index("across")
    padded = padded_2(density, (("light", 0), ("view", 2), ("across", 1)), 2)
    inside = (
        rim_mask(light_idx, n_light, brick_l, 1)[:, None, None]
        * rim_mask(across_idx, n_across, brick_a, 1)[None, :, None]
        * rim_mask(view_idx, n_view, brick_v, 1)[None, None, :]
    )
    shading = shade_from(padded, inside)
    table_all = jnp.concatenate([opacity_table[None], extinction_table, albedo_table], axis=0)
    looked = jnp.broadcast_to(table_all[:, 0, None, None, None], (7,) + labels.shape)
    for material in range(1, table_all.shape[1]):
        looked = jnp.where(
            (labels == material)[None], table_all[:, material, None, None, None], looked
        )
    extinct = looked[1:4] * density[None]
    extinct_slabs = extinct.reshape(3, SLABS, layer_rows, brick_a, brick_v)
    running = jnp.cumsum(extinct_slabs, axis=2) - extinct_slabs
    slab_depth = jnp.sum(extinct_slabs, axis=2)
    widest = SLABS * n_light
    both = jnp.concatenate([slab_depth, sunlight[:, None]], axis=1)
    both_rim = halo(halo(both, "across", 2, widest), "view", 3, widest)
    sun_rim = both_rim[:, SLABS]
    fade_rim = jnp.exp(-light_step * both_rim[:, :SLABS]) * plane_mask(widest, brick_a, brick_v)
    starts = None
    incoming = sun_rim
    for section_num in range(n_light):
        border = SLABS * (n_light - section_num)
        outgoing, starts = propagate(
            incoming, border, fade_rim, brick_a, brick_v
        )
        if section_num + 1 < n_light:
            arrived = from_behind(outgoing, "light", 1)
            cut = widest - border + SLABS
            sun_here = sun_rim[:, cut : cut + brick_a + 2 * (border - SLABS), cut : cut + brick_v + 2 * (border - SLABS)]
            incoming = jnp.where(light_idx == 0, sun_here, arrived)
    lighting = (starts[:, :, None] * jnp.exp(-light_step * running)).reshape(
        3, brick_l, brick_a, brick_v
    )
    optical = looked[0] * density * view_step
    colour = (1.0 - jnp.exp(-optical))[None] * looked[4:7] * (shading[None] * lighting + AMBIENT)
    upper = (jnp.arange(brick_v)[:, None] < jnp.arange(brick_v)[None, :]).astype(jnp.float32)
    before = jnp.dot(optical.reshape(-1, brick_v), upper, precision=lax.Precision.HIGHEST).reshape(
        brick_l, brick_a, brick_v
    )
    colour_sum = jnp.sum(colour * jnp.exp(-before)[None], axis=-1)
    transmit = jnp.exp(-jnp.sum(optical, axis=-1))
    pixels = brick_l * brick_a
    piece_len = pixels // n_view
    colour_now = colour_sum.reshape(3, n_view, piece_len)
    transmit_now = transmit.reshape(1, n_view, piece_len)
    bit_count = n_view.bit_length() - 1
    for bit_num in range(bit_count):
        kept = colour_now.shape[1]
        colour_pairs = colour_now.reshape(3, kept // 2, 2, piece_len)
        transmit_pairs = transmit_now.reshape(1, kept // 2, 2, piece_len)
        my_bit = view_idx // 2**bit_num % 2
        first_half = my_bit == 0
        keep_colour = jnp.where(first_half, colour_pairs[:, :, 0], colour_pairs[:, :, 1])
        send_colour = jnp.where(first_half, colour_pairs[:, :, 1], colour_pairs[:, :, 0])
        keep_transmit = jnp.where(first_half, transmit_pairs[:, :, 0], transmit_pairs[:, :, 1])
        send_transmit = jnp.where(first_half, transmit_pairs[:, :, 1], transmit_pairs[:, :, 0])
        got_colour, got_transmit = from_partner((send_colour, send_transmit), "view", bit_num)
        front_colour = jnp.where(first_half, keep_colour, got_colour)
        back_colour = jnp.where(first_half, got_colour, keep_colour)
        front_transmit = jnp.where(first_half, keep_transmit, got_transmit)
        colour_now = front_colour + front_transmit * back_colour
        transmit_now = keep_transmit * got_transmit
    final_colour = colour_now[:, 0]
    final_transmit = transmit_now[:, 0]
    rows_out = brick_l // n_view
    opacity = 1.0 - final_transmit.reshape(1, rows_out, brick_a)
    return jnp.concatenate([final_colour.reshape(3, rows_out, brick_a), opacity], axis=0)


def solution(mesh):
    in_specs = (
        P("light", "across", "view"),
        P("light", "across", "view"),
        P(None, "across", "view"),
        P(),
        P(),
        P(),
    )
    out_specs = P(None, ("light", "view"), "across")
    return jax.shard_map(shards, mesh=mesh, in_specs=in_specs, out_specs=out_specs, check_vma=False)
```

```python
import jax
import jax.numpy as jnp
from jax import lax
from jax.sharding import PartitionSpec as P

SLABS = 8


BLUR = 0.24
AMBIENT = 0.1
SOFTEN = 0.05


def padded_2(block, sides, width):
    for axis, dim in sides:
        count = lax.axis_size(axis)
        forward = [(i, i + 1) for i in range(count - 1)]
        backward = [(target, source) for source, target in forward]
        low = lax.ppermute(
            lax.slice_in_dim(block, block.shape[dim] - width, None, axis=dim), axis, forward
        )
        high = lax.ppermute(lax.slice_in_dim(block, 0, width, axis=dim), axis, backward)
        block = jnp.concatenate([low, block, high], axis=dim)
    return block


def from_behind(value, axis, steps):
    count = lax.axis_size(axis)
    leading, last = (max(0, -steps), min(count, count - steps))
    return lax.ppermute(value, axis, [(source, source + steps) for source in range(leading, last)])


def from_partner(block, axis, apart):
    count = lax.axis_size(axis)
    route = []
    for low in range(count):
        high = low | 1 << apart
        if high != low and high < count:
            route += [(low, high), (high, low)]
    return lax.ppermute(block, axis, route)


def smooth(field):
    centre = field[1:-1, 1:-1, 1:-1]
    return (
        2.0 * centre
        + field[2:, 1:-1, 1:-1]
        + field[:-2, 1:-1, 1:-1]
        + field[1:-1, 2:, 1:-1]
        + field[1:-1, :-2, 1:-1]
        + field[1:-1, 1:-1, 2:]
        + field[1:-1, 1:-1, :-2]
    ) * 0.125


def shade_from(window, inside):
    slope_light = (window[2:, 1:-1, 1:-1] - window[:-2, 1:-1, 1:-1]) * 0.5
    slope_across = (window[1:-1, 2:, 1:-1] - window[1:-1, :-2, 1:-1]) * 0.5
    slope_view = (window[1:-1, 1:-1, 2:] - window[1:-1, 1:-1, :-2]) * 0.5
    along = 0.8 * slope_light + 0.36 * slope_across + 0.48 * slope_view
    aligned = along * along * inside
    trace = (slope_light * slope_light + slope_across * slope_across + slope_view * slope_view) * inside
    return 0.25 + smooth(aligned) / (smooth(trace) + SOFTEN)


def rim_mask(position, devices, width, border):
    places = position * width - border + jnp.arange(width + 2 * border, dtype=jnp.int32)
    return ((places >= 0) & (places < devices * width)).astype(jnp.float32)


def halo(block, axis, dim, width):
    count = lax.axis_size(axis)
    size = block.shape[dim]
    lows, highs = [], []
    for hop in range(1, count):
        need = min(size, width - (hop - 1) * size)
        if need <= 0:
            break
        forward = [(i, i + hop) for i in range(count - hop)]
        backward = [(target, source) for source, target in forward]
        low = lax.slice_in_dim(block, size - need, None, axis=dim)
        lows.insert(0, lax.ppermute(low, axis, forward))
        highs.append(lax.ppermute(lax.slice_in_dim(block, 0, need, axis=dim), axis, backward))
    block = jnp.concatenate(lows + [block] + highs, axis=dim)
    missing = width - sum(part.shape[dim] for part in lows)
    if missing > 0:
        widths = [(0, 0)] * block.ndim
        widths[dim] = (missing, missing)
        block = jnp.pad(block, widths)
    return block


def plane_mask(border, brick_a, brick_v):
    return (
        rim_mask(lax.axis_index("across"), lax.axis_size("across"), brick_a, border)[:, None]
        * rim_mask(lax.axis_index("view"), lax.axis_size("view"), brick_v, border)[None, :]
    )


def propagate(current, border_in, fade_rim, brick_a, brick_v):
    widest = (fade_rim.shape[2] - brick_a) // 2
    starts = []
    for slab_num in range(SLABS):
        border = border_in - slab_num
        starts.append(current[:, border : border + brick_a, border : border + brick_v])
        offset = widest - border
        fade_here = fade_rim[
            :,
            slab_num,
            offset : offset + brick_a + 2 * border,
            offset : offset + brick_v + 2 * border,
        ]
        current = current * fade_here
        centre = current[:, 1:-1, 1:-1]
        current = centre + BLUR * (
            current[:, :-2, 1:-1]
            + current[:, 2:, 1:-1]
            + current[:, 1:-1, :-2]
            + current[:, 1:-1, 2:]
            - 4.0 * centre
        )
    return (current, jnp.stack(starts, axis=1))


def shards(density, labels, sunlight, opacity_table, extinction_table, albedo_table):
    brick_l, brick_a, brick_v = density.shape
    n_light = lax.axis_size("light")
    n_view = lax.axis_size("view")
    n_across = lax.axis_size("across")
    full_l = brick_l * n_light
    full_v = brick_v * n_view
    light_step = 10.0 / full_l
    view_step = 2.0 / full_v
    layer_rows = brick_l // SLABS
    light_idx = lax.axis_index("light")
    view_idx = lax.axis_index("view")
    across_idx = lax.axis_index("across")
    table_all = jnp.concatenate([opacity_table[None], extinction_table, albedo_table], axis=0)
    looked = jnp.broadcast_to(table_all[:, 0, None, None, None], (7,) + labels.shape)
    for material in range(1, table_all.shape[1]):
        looked = jnp.where(
            (labels == material)[None], table_all[:, material, None, None, None], looked
        )
    extinct = looked[1:4] * density[None]
    extinct_slabs = extinct.reshape(3, SLABS, layer_rows, brick_a, brick_v)
    running = jnp.cumsum(extinct_slabs, axis=2) - extinct_slabs
    slab_depth = jnp.sum(extinct_slabs, axis=2)
    widest = SLABS * n_light
    stack = jnp.concatenate(
        [density, slab_depth.reshape(3 * SLABS, brick_a, brick_v), sunlight], axis=0
    )
    stack_rim = halo(halo(stack, "view", 2, widest), "across", 1, widest)
    rim_a = brick_a + 2 * widest
    rim_v = brick_v + 2 * widest
    depth_rim = stack_rim[brick_l : brick_l + 3 * SLABS].reshape(3, SLABS, rim_a, rim_v)
    sun_rim = stack_rim[brick_l + 3 * SLABS :]
    fade_rim = jnp.exp(-light_step * depth_rim) * plane_mask(widest, brick_a, brick_v)
    density_side = stack_rim[
        :brick_l, widest - 2 : widest + brick_a + 2, widest - 2 : widest + brick_v + 2
    ]
    padded = padded_2(density_side, (("light", 0),), 2)
    inside = (
        rim_mask(light_idx, n_light, brick_l, 1)[:, None, None]
        * rim_mask(across_idx, n_across, brick_a, 1)[None, :, None]
        * rim_mask(view_idx, n_view, brick_v, 1)[None, None, :]
    )
    shading = shade_from(padded, inside)
    starts = None
    incoming = sun_rim
    for section_num in range(n_light):
        border = SLABS * (n_light - section_num)
        outgoing, starts = propagate(
            incoming, border, fade_rim, brick_a, brick_v
        )
        if section_num + 1 < n_light:
            arrived = from_behind(outgoing, "light", 1)
            cut = widest - border + SLABS
            sun_here = sun_rim[:, cut : cut + brick_a + 2 * (border - SLABS), cut : cut + brick_v + 2 * (border - SLABS)]
            incoming = jnp.where(light_idx == 0, sun_here, arrived)
    lighting = (starts[:, :, None] * jnp.exp(-light_step * running)).reshape(
        3, brick_l, brick_a, brick_v
    )
    optical = looked[0] * density * view_step
    colour = (1.0 - jnp.exp(-optical))[None] * looked[4:7] * (shading[None] * lighting + AMBIENT)
    upper = (jnp.arange(brick_v)[:, None] < jnp.arange(brick_v)[None, :]).astype(jnp.float32)
    before = jnp.dot(optical.reshape(-1, brick_v), upper, precision=lax.Precision.HIGHEST).reshape(
        brick_l, brick_a, brick_v
    )
    colour_sum = jnp.sum(colour * jnp.exp(-before)[None], axis=-1)
    transmit = jnp.exp(-jnp.sum(optical, axis=-1))
    pixels = brick_l * brick_a
    piece_len = pixels // n_view
    image_now = jnp.concatenate(
        [colour_sum.reshape(3, n_view, piece_len), transmit.reshape(1, n_view, piece_len)], axis=0
    )
    bit_count = n_view.bit_length() - 1
    for bit_num in range(bit_count):
        kept = image_now.shape[1]
        pairs = image_now.reshape(4, kept // 2, 2, piece_len)
        my_bit = view_idx // 2**bit_num % 2
        first_half = my_bit == 0
        keep = jnp.where(first_half, pairs[:, :, 0], pairs[:, :, 1])
        send = jnp.where(first_half, pairs[:, :, 1], pairs[:, :, 0])
        got = from_partner(send, "view", bit_num)
        front = jnp.where(first_half, keep, got)
        back = jnp.where(first_half, got, keep)
        image_now = jnp.concatenate(
            [front[:3] + front[3:] * back[:3], keep[3:] * got[3:]], axis=0
        )
    final_colour = image_now[:3, 0]
    final_transmit = image_now[3:, 0]
    rows_out = brick_l // n_view
    opacity = 1.0 - final_transmit.reshape(1, rows_out, brick_a)
    return jnp.concatenate([final_colour.reshape(3, rows_out, brick_a), opacity], axis=0)


def solution(mesh):
    in_specs = (
        P("light", "across", "view"),
        P("light", "across", "view"),
        P(None, "across", "view"),
        P(),
        P(),
        P(),
    )
    out_specs = P(None, ("light", "view"), "across")
    return jax.shard_map(shards, mesh=mesh, in_specs=in_specs, out_specs=out_specs, check_vma=False)
```

```python
import jax
import jax.numpy as jnp
from jax import lax
from jax.sharding import PartitionSpec as P

SLABS = 8


BLUR = 0.24
AMBIENT = 0.1
SOFTEN = 0.05


def padded_2(block, sides, width):
    for axis, dim in sides:
        count = lax.axis_size(axis)
        forward = [(i, i + 1) for i in range(count - 1)]
        backward = [(target, source) for source, target in forward]
        low = lax.ppermute(
            lax.slice_in_dim(block, block.shape[dim] - width, None, axis=dim), axis, forward
        )
        high = lax.ppermute(lax.slice_in_dim(block, 0, width, axis=dim), axis, backward)
        block = jnp.concatenate([low, block, high], axis=dim)
    return block


def from_behind(value, axis, steps):
    count = lax.axis_size(axis)
    leading, last = (max(0, -steps), min(count, count - steps))
    return lax.ppermute(value, axis, [(source, source + steps) for source in range(leading, last)])


def from_partner(block, axis, apart):
    count = lax.axis_size(axis)
    route = []
    for low in range(count):
        high = low | 1 << apart
        if high != low and high < count:
            route += [(low, high), (high, low)]
    return lax.ppermute(block, axis, route)


def smooth(field):
    centre = field[1:-1, 1:-1, 1:-1]
    return (
        2.0 * centre
        + field[2:, 1:-1, 1:-1]
        + field[:-2, 1:-1, 1:-1]
        + field[1:-1, 2:, 1:-1]
        + field[1:-1, :-2, 1:-1]
        + field[1:-1, 1:-1, 2:]
        + field[1:-1, 1:-1, :-2]
    ) * 0.125


def shade_from(window, inside):
    slope_light = (window[2:, 1:-1, 1:-1] - window[:-2, 1:-1, 1:-1]) * 0.5
    slope_across = (window[1:-1, 2:, 1:-1] - window[1:-1, :-2, 1:-1]) * 0.5
    slope_view = (window[1:-1, 1:-1, 2:] - window[1:-1, 1:-1, :-2]) * 0.5
    along = 0.8 * slope_light + 0.36 * slope_across + 0.48 * slope_view
    aligned = along * along * inside
    trace = (slope_light * slope_light + slope_across * slope_across + slope_view * slope_view) * inside
    return 0.25 + smooth(aligned) / (smooth(trace) + SOFTEN)


def rim_mask(position, devices, width, border):
    places = position * width - border + jnp.arange(width + 2 * border, dtype=jnp.int32)
    return ((places >= 0) & (places < devices * width)).astype(jnp.float32)


def halo(block, axis, dim, width):
    count = lax.axis_size(axis)
    size = block.shape[dim]
    lows, highs = [], []
    for hop in range(1, count):
        need = min(size, width - (hop - 1) * size)
        if need <= 0:
            break
        forward = [(i, i + hop) for i in range(count - hop)]
        backward = [(target, source) for source, target in forward]
        low = lax.slice_in_dim(block, size - need, None, axis=dim)
        lows.insert(0, lax.ppermute(low, axis, forward))
        highs.append(lax.ppermute(lax.slice_in_dim(block, 0, need, axis=dim), axis, backward))
    block = jnp.concatenate(lows + [block] + highs, axis=dim)
    missing = width - sum(part.shape[dim] for part in lows)
    if missing > 0:
        widths = [(0, 0)] * block.ndim
        widths[dim] = (missing, missing)
        block = jnp.pad(block, widths)
    return block


def plane_mask(border, brick_a, brick_v):
    return (
        rim_mask(lax.axis_index("across"), lax.axis_size("across"), brick_a, border)[:, None]
        * rim_mask(lax.axis_index("view"), lax.axis_size("view"), brick_v, border)[None, :]
    )


def propagate(current, border_in, fade_rim, brick_a, brick_v):
    widest = (fade_rim.shape[2] - brick_a) // 2
    starts = []
    for slab_num in range(SLABS):
        border = border_in - slab_num
        starts.append(current[:, border : border + brick_a, border : border + brick_v])
        offset = widest - border
        fade_here = fade_rim[
            :,
            slab_num,
            offset : offset + brick_a + 2 * border,
            offset : offset + brick_v + 2 * border,
        ]
        current = current * fade_here
        centre = current[:, 1:-1, 1:-1]
        current = centre + BLUR * (
            current[:, :-2, 1:-1]
            + current[:, 2:, 1:-1]
            + current[:, 1:-1, :-2]
            + current[:, 1:-1, 2:]
            - 4.0 * centre
        )
    return (current, jnp.stack(starts, axis=1))


def shards(density, labels, sunlight, opacity_table, extinction_table, albedo_table):
    brick_l, brick_a, brick_v = density.shape
    n_light = lax.axis_size("light")
    n_view = lax.axis_size("view")
    n_across = lax.axis_size("across")
    full_l = brick_l * n_light
    full_v = brick_v * n_view
    light_step = 10.0 / full_l
    view_step = 2.0 / full_v
    layer_rows = brick_l // SLABS
    light_idx = lax.axis_index("light")
    view_idx = lax.axis_index("view")
    across_idx = lax.axis_index("across")
    padded = padded_2(density, (("light", 0), ("view", 2), ("across", 1)), 2)
    inside = (
        rim_mask(light_idx, n_light, brick_l, 1)[:, None, None]
        * rim_mask(across_idx, n_across, brick_a, 1)[None, :, None]
        * rim_mask(view_idx, n_view, brick_v, 1)[None, None, :]
    )
    shading = shade_from(padded, inside)
    table_all = jnp.concatenate([opacity_table[None], extinction_table, albedo_table], axis=0)
    looked = jnp.broadcast_to(table_all[:, 0, None, None, None], (7,) + labels.shape)
    for material in range(1, table_all.shape[1]):
        looked = jnp.where(
            (labels == material)[None], table_all[:, material, None, None, None], looked
        )
    extinct = looked[1:4] * density[None]
    extinct_slabs = extinct.reshape(3, SLABS, layer_rows, brick_a, brick_v)
    running = jnp.cumsum(extinct_slabs, axis=2) - extinct_slabs
    slab_depth = jnp.sum(extinct_slabs, axis=2)
    widest = SLABS * n_light
    both = jnp.concatenate([slab_depth, sunlight[:, None]], axis=1)
    both_rim = halo(halo(both, "across", 2, widest), "view", 3, widest)
    sun_rim = both_rim[:, SLABS]
    fade_rim = jnp.exp(-light_step * both_rim[:, :SLABS]) * plane_mask(widest, brick_a, brick_v)
    starts = None
    incoming = sun_rim
    for section_num in range(n_light):
        border = SLABS * (n_light - section_num)
        outgoing, starts = propagate(
            incoming, border, fade_rim, brick_a, brick_v
        )
        if section_num + 1 < n_light:
            arrived = from_behind(outgoing, "light", 1)
            cut = widest - border + SLABS
            sun_here = sun_rim[:, cut : cut + brick_a + 2 * (border - SLABS), cut : cut + brick_v + 2 * (border - SLABS)]
            incoming = jnp.where(light_idx == 0, sun_here, arrived)
    lighting = (starts[:, :, None] * jnp.exp(-light_step * running)).reshape(
        3, brick_l, brick_a, brick_v
    )
    optical = looked[0] * density * view_step
    colour = (1.0 - jnp.exp(-optical))[None] * looked[4:7] * (shading[None] * lighting + AMBIENT)
    upper = (jnp.arange(brick_v)[:, None] < jnp.arange(brick_v)[None, :]).astype(jnp.float32)
    before = jnp.dot(optical.reshape(-1, brick_v), upper, precision=lax.Precision.HIGHEST).reshape(
        brick_l, brick_a, brick_v
    )
    colour_sum = jnp.sum(colour * jnp.exp(-before)[None], axis=-1)
    transmit = jnp.exp(-jnp.sum(optical, axis=-1))
    pixels = brick_l * brick_a
    piece_len = pixels // n_view
    image_now = jnp.concatenate(
        [colour_sum.reshape(3, n_view, piece_len), transmit.reshape(1, n_view, piece_len)], axis=0
    )
    bit_count = n_view.bit_length() - 1
    for bit_num in range(bit_count):
        kept = image_now.shape[1]
        pairs = image_now.reshape(4, kept // 2, 2, piece_len)
        my_bit = view_idx // 2**bit_num % 2
        first_half = my_bit == 0
        keep = jnp.where(first_half, pairs[:, :, 0], pairs[:, :, 1])
        send = jnp.where(first_half, pairs[:, :, 1], pairs[:, :, 0])
        got = from_partner(send, "view", bit_num)
        front = jnp.where(first_half, keep, got)
        back = jnp.where(first_half, got, keep)
        image_now = jnp.concatenate(
            [front[:3] + front[3:] * back[:3], keep[3:] * got[3:]], axis=0
        )
    final_colour = image_now[:3, 0]
    final_transmit = image_now[3:, 0]
    rows_out = brick_l // n_view
    opacity = 1.0 - final_transmit.reshape(1, rows_out, brick_a)
    return jnp.concatenate([final_colour.reshape(3, rows_out, brick_a), opacity], axis=0)


def solution(mesh):
    in_specs = (
        P("light", "across", "view"),
        P("light", "across", "view"),
        P(None, "across", "view"),
        P(),
        P(),
        P(),
    )
    out_specs = P(None, ("light", "view"), "across")
    return jax.shard_map(shards, mesh=mesh, in_specs=in_specs, out_specs=out_specs, check_vma=False)
```

```python
import jax
import jax.numpy as jnp
from jax import lax
from jax.sharding import PartitionSpec as P

SLABS = 8


BLUR = 0.24
AMBIENT = 0.1
SOFTEN = 0.05


def padded_2(block, sides, width):
    for axis, dim in sides:
        count = lax.axis_size(axis)
        forward = [(i, i + 1) for i in range(count - 1)]
        backward = [(target, source) for source, target in forward]
        low = lax.ppermute(
            lax.slice_in_dim(block, block.shape[dim] - width, None, axis=dim), axis, forward
        )
        high = lax.ppermute(lax.slice_in_dim(block, 0, width, axis=dim), axis, backward)
        block = jnp.concatenate([low, block, high], axis=dim)
    return block


def from_behind(value, axis, steps):
    count = lax.axis_size(axis)
    leading, last = (max(0, -steps), min(count, count - steps))
    return lax.ppermute(value, axis, [(source, source + steps) for source in range(leading, last)])


def from_partner(block, axis, apart):
    count = lax.axis_size(axis)
    route = []
    for low in range(count):
        high = low | 1 << apart
        if high != low and high < count:
            route += [(low, high), (high, low)]
    return lax.ppermute(block, axis, route)


def smooth(field):
    centre = field[1:-1, 1:-1, 1:-1]
    return (
        2.0 * centre
        + field[2:, 1:-1, 1:-1]
        + field[:-2, 1:-1, 1:-1]
        + field[1:-1, 2:, 1:-1]
        + field[1:-1, :-2, 1:-1]
        + field[1:-1, 1:-1, 2:]
        + field[1:-1, 1:-1, :-2]
    ) * 0.125


def shade_from(window, inside):
    slope_light = (window[2:, 1:-1, 1:-1] - window[:-2, 1:-1, 1:-1]) * 0.5
    slope_across = (window[1:-1, 2:, 1:-1] - window[1:-1, :-2, 1:-1]) * 0.5
    slope_view = (window[1:-1, 1:-1, 2:] - window[1:-1, 1:-1, :-2]) * 0.5
    along = 0.8 * slope_light + 0.36 * slope_across + 0.48 * slope_view
    aligned = along * along * inside
    trace = (slope_light * slope_light + slope_across * slope_across + slope_view * slope_view) * inside
    return 0.25 + smooth(aligned) / (smooth(trace) + SOFTEN)


def rim_mask(position, devices, width, border):
    places = position * width - border + jnp.arange(width + 2 * border, dtype=jnp.int32)
    return ((places >= 0) & (places < devices * width)).astype(jnp.float32)


def halo(block, axis, dim, width):
    count = lax.axis_size(axis)
    size = block.shape[dim]
    lows, highs = [], []
    for hop in range(1, count):
        need = min(size, width - (hop - 1) * size)
        if need <= 0:
            break
        forward = [(i, i + hop) for i in range(count - hop)]
        backward = [(target, source) for source, target in forward]
        low = lax.slice_in_dim(block, size - need, None, axis=dim)
        lows.insert(0, lax.ppermute(low, axis, forward))
        highs.append(lax.ppermute(lax.slice_in_dim(block, 0, need, axis=dim), axis, backward))
    block = jnp.concatenate(lows + [block] + highs, axis=dim)
    missing = width - sum(part.shape[dim] for part in lows)
    if missing > 0:
        widths = [(0, 0)] * block.ndim
        widths[dim] = (missing, missing)
        block = jnp.pad(block, widths)
    return block


def plane_mask(border, brick_a, brick_v):
    return (
        rim_mask(lax.axis_index("across"), lax.axis_size("across"), brick_a, border)[:, None]
        * rim_mask(lax.axis_index("view"), lax.axis_size("view"), brick_v, border)[None, :]
    )


def propagate(current, border_in, fade_rim, brick_a, brick_v):
    widest = (fade_rim.shape[2] - brick_a) // 2
    starts = []
    for slab_num in range(SLABS):
        border = border_in - slab_num
        starts.append(current[:, border : border + brick_a, border : border + brick_v])
        offset = widest - border
        fade_here = fade_rim[
            :,
            slab_num,
            offset : offset + brick_a + 2 * border,
            offset : offset + brick_v + 2 * border,
        ]
        current = current * fade_here
        centre = current[:, 1:-1, 1:-1]
        current = centre + BLUR * (
            current[:, :-2, 1:-1]
            + current[:, 2:, 1:-1]
            + current[:, 1:-1, :-2]
            + current[:, 1:-1, 2:]
            - 4.0 * centre
        )
    return (current, jnp.stack(starts, axis=1))


def shards(density, labels, sunlight, opacity_table, extinction_table, albedo_table):
    brick_l, brick_a, brick_v = density.shape
    n_light = lax.axis_size("light")
    n_view = lax.axis_size("view")
    n_across = lax.axis_size("across")
    full_l = brick_l * n_light
    full_v = brick_v * n_view
    light_step = 10.0 / full_l
    view_step = 2.0 / full_v
    layer_rows = brick_l // SLABS
    light_idx = lax.axis_index("light")
    view_idx = lax.axis_index("view")
    across_idx = lax.axis_index("across")
    widest = SLABS * n_light
    stack = jnp.concatenate([density, labels.astype(jnp.float32), sunlight], axis=0)
    stack_rim = halo(halo(stack, "across", 1, widest), "view", 2, widest)
    density_rim = stack_rim[:brick_l]
    labels_rim = stack_rim[brick_l : 2 * brick_l]
    sun_rim = stack_rim[2 * brick_l :]
    density_side = density_rim[
        :, widest - 2 : widest + brick_a + 2, widest - 2 : widest + brick_v + 2
    ]
    padded = padded_2(density_side, (("light", 0),), 2)
    inside = (
        rim_mask(light_idx, n_light, brick_l, 1)[:, None, None]
        * rim_mask(across_idx, n_across, brick_a, 1)[None, :, None]
        * rim_mask(view_idx, n_view, brick_v, 1)[None, None, :]
    )
    shading = shade_from(padded, inside)
    table_all = jnp.concatenate([opacity_table[None], albedo_table], axis=0)
    looked = jnp.broadcast_to(table_all[:, 0, None, None, None], (4,) + labels.shape)
    for material in range(1, table_all.shape[1]):
        looked = jnp.where(
            (labels == material)[None], table_all[:, material, None, None, None], looked
        )
    extinct_rim = jnp.broadcast_to(extinction_table[:, 0, None, None, None], (3,) + labels_rim.shape)
    for material in range(1, extinction_table.shape[1]):
        extinct_rim = jnp.where(
            (labels_rim == material)[None], extinction_table[:, material, None, None, None], extinct_rim
        )
    extinct_rim = extinct_rim * density_rim[None]
    rim_a = brick_a + 2 * widest
    rim_v = brick_v + 2 * widest
    slab_depth = jnp.sum(extinct_rim.reshape(3, SLABS, layer_rows, rim_a, rim_v), axis=2)
    extinct = extinct_rim[:, :, widest : widest + brick_a, widest : widest + brick_v]
    extinct_slabs = extinct.reshape(3, SLABS, layer_rows, brick_a, brick_v)
    running = jnp.cumsum(extinct_slabs, axis=2) - extinct_slabs
    fade_rim = jnp.exp(-light_step * slab_depth) * plane_mask(widest, brick_a, brick_v)
    starts = None
    incoming = sun_rim
    for section_num in range(n_light):
        border = SLABS * (n_light - section_num)
        outgoing, starts = propagate(
            incoming, border, fade_rim, brick_a, brick_v
        )
        if section_num + 1 < n_light:
            arrived = from_behind(outgoing, "light", 1)
            cut = widest - border + SLABS
            sun_here = sun_rim[:, cut : cut + brick_a + 2 * (border - SLABS), cut : cut + brick_v + 2 * (border - SLABS)]
            incoming = jnp.where(light_idx == 0, sun_here, arrived)
    lighting = (starts[:, :, None] * jnp.exp(-light_step * running)).reshape(
        3, brick_l, brick_a, brick_v
    )
    optical = looked[0] * density * view_step
    colour = (1.0 - jnp.exp(-optical))[None] * looked[1:4] * (shading[None] * lighting + AMBIENT)
    upper = (jnp.arange(brick_v)[:, None] < jnp.arange(brick_v)[None, :]).astype(jnp.float32)
    before = jnp.dot(optical.reshape(-1, brick_v), upper, precision=lax.Precision.HIGHEST).reshape(
        brick_l, brick_a, brick_v
    )
    colour_sum = jnp.sum(colour * jnp.exp(-before)[None], axis=-1)
    transmit = jnp.exp(-jnp.sum(optical, axis=-1))
    pixels = brick_l * brick_a
    piece_len = pixels // n_view
    image_now = jnp.concatenate(
        [colour_sum.reshape(3, n_view, piece_len), transmit.reshape(1, n_view, piece_len)], axis=0
    )
    bit_count = n_view.bit_length() - 1
    for bit_num in range(bit_count):
        kept = image_now.shape[1]
        pairs = image_now.reshape(4, kept // 2, 2, piece_len)
        my_bit = view_idx // 2**bit_num % 2
        first_half = my_bit == 0
        keep = jnp.where(first_half, pairs[:, :, 0], pairs[:, :, 1])
        send = jnp.where(first_half, pairs[:, :, 1], pairs[:, :, 0])
        got = from_partner(send, "view", bit_num)
        front = jnp.where(first_half, keep, got)
        back = jnp.where(first_half, got, keep)
        image_now = jnp.concatenate(
            [front[:3] + front[3:] * back[:3], keep[3:] * got[3:]], axis=0
        )
    final_colour = image_now[:3, 0]
    final_transmit = image_now[3:, 0]
    rows_out = brick_l // n_view
    opacity = 1.0 - final_transmit.reshape(1, rows_out, brick_a)
    return jnp.concatenate([final_colour.reshape(3, rows_out, brick_a), opacity], axis=0)


def solution(mesh):
    in_specs = (
        P("light", "across", "view"),
        P("light", "across", "view"),
        P(None, "across", "view"),
        P(),
        P(),
        P(),
    )
    out_specs = P(None, ("light", "view"), "across")
    return jax.shard_map(shards, mesh=mesh, in_specs=in_specs, out_specs=out_specs, check_vma=False)
```

```python
import jax
import jax.numpy as jnp
from jax import lax
from jax.experimental import pallas as pl
from jax.experimental.pallas import tpu as pltpu
from jax.sharding import PartitionSpec as P

SLABS = 8


BLUR = 0.24
AMBIENT = 0.1
SOFTEN = 0.05


def padded_2(block, sides, width):
    for axis, dim in sides:
        count = lax.axis_size(axis)
        forward = [(i, i + 1) for i in range(count - 1)]
        backward = [(target, source) for source, target in forward]
        low = lax.ppermute(
            lax.slice_in_dim(block, block.shape[dim] - width, None, axis=dim), axis, forward
        )
        high = lax.ppermute(lax.slice_in_dim(block, 0, width, axis=dim), axis, backward)
        block = jnp.concatenate([low, block, high], axis=dim)
    return block


def from_behind(value, axis, steps):
    count = lax.axis_size(axis)
    leading, last = (max(0, -steps), min(count, count - steps))
    return lax.ppermute(value, axis, [(source, source + steps) for source in range(leading, last)])


def from_partner(block, axis, apart):
    count = lax.axis_size(axis)
    route = []
    for low in range(count):
        high = low | 1 << apart
        if high != low and high < count:
            route += [(low, high), (high, low)]
    return lax.ppermute(block, axis, route)


def smooth(field):
    centre = field[1:-1, 1:-1, 1:-1]
    return (
        2.0 * centre
        + field[2:, 1:-1, 1:-1]
        + field[:-2, 1:-1, 1:-1]
        + field[1:-1, 2:, 1:-1]
        + field[1:-1, :-2, 1:-1]
        + field[1:-1, 1:-1, 2:]
        + field[1:-1, 1:-1, :-2]
    ) * 0.125


def shade_from(window, inside):
    slope_light = (window[2:, 1:-1, 1:-1] - window[:-2, 1:-1, 1:-1]) * 0.5
    slope_across = (window[1:-1, 2:, 1:-1] - window[1:-1, :-2, 1:-1]) * 0.5
    slope_view = (window[1:-1, 1:-1, 2:] - window[1:-1, 1:-1, :-2]) * 0.5
    along = 0.8 * slope_light + 0.36 * slope_across + 0.48 * slope_view
    aligned = along * along * inside
    trace = (slope_light * slope_light + slope_across * slope_across + slope_view * slope_view) * inside
    return 0.25 + smooth(aligned) / (smooth(trace) + SOFTEN)


def rim_mask(position, devices, width, border):
    places = position * width - border + jnp.arange(width + 2 * border, dtype=jnp.int32)
    return ((places >= 0) & (places < devices * width)).astype(jnp.float32)


def halo(block, axis, dim, width):
    count = lax.axis_size(axis)
    size = block.shape[dim]
    lows, highs = [], []
    for hop in range(1, count):
        need = min(size, width - (hop - 1) * size)
        if need <= 0:
            break
        forward = [(i, i + hop) for i in range(count - hop)]
        backward = [(target, source) for source, target in forward]
        low = lax.slice_in_dim(block, size - need, None, axis=dim)
        lows.insert(0, lax.ppermute(low, axis, forward))
        highs.append(lax.ppermute(lax.slice_in_dim(block, 0, need, axis=dim), axis, backward))
    block = jnp.concatenate(lows + [block] + highs, axis=dim)
    missing = width - sum(part.shape[dim] for part in lows)
    if missing > 0:
        widths = [(0, 0)] * block.ndim
        widths[dim] = (missing, missing)
        block = jnp.pad(block, widths)
    return block


def plane_mask(border, brick_a, brick_v):
    return (
        rim_mask(lax.axis_index("across"), lax.axis_size("across"), brick_a, border)[:, None]
        * rim_mask(lax.axis_index("view"), lax.axis_size("view"), brick_v, border)[None, :]
    )


def propagate(current, border_in, fade_rim, brick_a, brick_v):
    widest = (fade_rim.shape[2] - brick_a) // 2
    starts = []
    for slab_num in range(SLABS):
        border = border_in - slab_num
        starts.append(current[:, border : border + brick_a, border : border + brick_v])
        offset = widest - border
        fade_here = fade_rim[
            :,
            slab_num,
            offset : offset + brick_a + 2 * border,
            offset : offset + brick_v + 2 * border,
        ]
        current = current * fade_here
        centre = current[:, 1:-1, 1:-1]
        current = centre + BLUR * (
            current[:, :-2, 1:-1]
            + current[:, 2:, 1:-1]
            + current[:, 1:-1, :-2]
            + current[:, 1:-1, 2:]
            - 4.0 * centre
        )
    return (current, jnp.stack(starts, axis=1))


def fade_rim_of(extinction_table, density_rim, labels_rim, mask, light_step):
    rows, rim_a, rim_v = density_rim.shape
    layer_rows = rows // SLABS
    colours, materials = extinction_table.shape
    chunk = 8 if rim_a % 8 == 0 else rim_a

    def kernel(table_ref, density_ref, labels_ref, mask_ref, out_ref):
        def one_slab(slab_num, carry):
            for first in range(0, rim_a, chunk):
                part = slice(first, first + chunk)
                depth = [None] * colours
                for row in range(layer_rows):
                    row_num = slab_num * layer_rows + row
                    here = labels_ref[row_num, part, :]
                    cells = density_ref[row_num, part, :]
                    looked = [jnp.full(here.shape, table_ref[c, 0]) for c in range(colours)]
                    for material in range(1, materials):
                        match = here == float(material)
                        looked = [
                            jnp.where(match, table_ref[c, material], looked[c]) for c in range(colours)
                        ]
                    for c in range(colours):
                        term = looked[c] * cells
                        depth[c] = term if depth[c] is None else depth[c] + term
                for c in range(colours):
                    out_ref[c, slab_num, part, :] = (
                        jnp.exp(-light_step * depth[c]) * mask_ref[part, :]
                    )
            return carry

        lax.fori_loop(0, SLABS, one_slab, 0)

    return pl.pallas_call(
        kernel,
        out_shape=jax.ShapeDtypeStruct((colours, SLABS, rim_a, rim_v), jnp.float32),
        in_specs=[
            pl.BlockSpec(memory_space=pltpu.SMEM),
            pl.BlockSpec(memory_space=pltpu.VMEM),
            pl.BlockSpec(memory_space=pltpu.VMEM),
            pl.BlockSpec(memory_space=pltpu.VMEM),
        ],
        out_specs=pl.BlockSpec(memory_space=pltpu.VMEM),
    )(extinction_table, density_rim, labels_rim, mask)


def shards(density, labels, sunlight, opacity_table, extinction_table, albedo_table):
    brick_l, brick_a, brick_v = density.shape
    n_light = lax.axis_size("light")
    n_view = lax.axis_size("view")
    n_across = lax.axis_size("across")
    full_l = brick_l * n_light
    full_v = brick_v * n_view
    light_step = 10.0 / full_l
    view_step = 2.0 / full_v
    layer_rows = brick_l // SLABS
    light_idx = lax.axis_index("light")
    view_idx = lax.axis_index("view")
    across_idx = lax.axis_index("across")
    widest = SLABS * n_light
    stack = jnp.concatenate([density, labels.astype(jnp.float32), sunlight], axis=0)
    stack_rim = halo(halo(stack, "across", 1, widest), "view", 2, widest)
    density_rim = stack_rim[:brick_l]
    labels_rim = stack_rim[brick_l : 2 * brick_l]
    sun_rim = stack_rim[2 * brick_l :]
    density_side = density_rim[
        :, widest - 2 : widest + brick_a + 2, widest - 2 : widest + brick_v + 2
    ]
    padded = padded_2(density_side, (("light", 0),), 2)
    inside = (
        rim_mask(light_idx, n_light, brick_l, 1)[:, None, None]
        * rim_mask(across_idx, n_across, brick_a, 1)[None, :, None]
        * rim_mask(view_idx, n_view, brick_v, 1)[None, None, :]
    )
    shading = shade_from(padded, inside)
    table_all = jnp.concatenate([opacity_table[None], extinction_table, albedo_table], axis=0)
    looked = jnp.broadcast_to(table_all[:, 0, None, None, None], (7,) + labels.shape)
    for material in range(1, table_all.shape[1]):
        looked = jnp.where(
            (labels == material)[None], table_all[:, material, None, None, None], looked
        )
    extinct = looked[1:4] * density[None]
    extinct_slabs = extinct.reshape(3, SLABS, layer_rows, brick_a, brick_v)
    running = jnp.cumsum(extinct_slabs, axis=2) - extinct_slabs
    fade_rim = fade_rim_of(
        extinction_table, density_rim, labels_rim, plane_mask(widest, brick_a, brick_v), light_step
    )
    starts = None
    incoming = sun_rim
    for section_num in range(n_light):
        border = SLABS * (n_light - section_num)
        outgoing, starts = propagate(
            incoming, border, fade_rim, brick_a, brick_v
        )
        if section_num + 1 < n_light:
            arrived = from_behind(outgoing, "light", 1)
            cut = widest - border + SLABS
            sun_here = sun_rim[:, cut : cut + brick_a + 2 * (border - SLABS), cut : cut + brick_v + 2 * (border - SLABS)]
            incoming = jnp.where(light_idx == 0, sun_here, arrived)
    lighting = (starts[:, :, None] * jnp.exp(-light_step * running)).reshape(
        3, brick_l, brick_a, brick_v
    )
    optical = looked[0] * density * view_step
    colour = (1.0 - jnp.exp(-optical))[None] * looked[4:7] * (shading[None] * lighting + AMBIENT)
    upper = (jnp.arange(brick_v)[:, None] < jnp.arange(brick_v)[None, :]).astype(jnp.float32)
    before = jnp.dot(optical.reshape(-1, brick_v), upper, precision=lax.Precision.HIGHEST).reshape(
        brick_l, brick_a, brick_v
    )
    colour_sum = jnp.sum(colour * jnp.exp(-before)[None], axis=-1)
    transmit = jnp.exp(-jnp.sum(optical, axis=-1))
    pixels = brick_l * brick_a
    piece_len = pixels // n_view
    image_now = jnp.concatenate(
        [colour_sum.reshape(3, n_view, piece_len), transmit.reshape(1, n_view, piece_len)], axis=0
    )
    bit_count = n_view.bit_length() - 1
    for bit_num in range(bit_count):
        kept = image_now.shape[1]
        pairs = image_now.reshape(4, kept // 2, 2, piece_len)
        my_bit = view_idx // 2**bit_num % 2
        first_half = my_bit == 0
        keep = jnp.where(first_half, pairs[:, :, 0], pairs[:, :, 1])
        send = jnp.where(first_half, pairs[:, :, 1], pairs[:, :, 0])
        got = from_partner(send, "view", bit_num)
        front = jnp.where(first_half, keep, got)
        back = jnp.where(first_half, got, keep)
        image_now = jnp.concatenate(
            [front[:3] + front[3:] * back[:3], keep[3:] * got[3:]], axis=0
        )
    final_colour = image_now[:3, 0]
    final_transmit = image_now[3:, 0]
    rows_out = brick_l // n_view
    opacity = 1.0 - final_transmit.reshape(1, rows_out, brick_a)
    return jnp.concatenate([final_colour.reshape(3, rows_out, brick_a), opacity], axis=0)


def solution(mesh):
    in_specs = (
        P("light", "across", "view"),
        P("light", "across", "view"),
        P(None, "across", "view"),
        P(),
        P(),
        P(),
    )
    out_specs = P(None, ("light", "view"), "across")
    return jax.shard_map(shards, mesh=mesh, in_specs=in_specs, out_specs=out_specs, check_vma=False)
```

```python
import jax
import jax.numpy as jnp
from jax import lax
from jax.experimental import pallas as pl
from jax.experimental.pallas import tpu as pltpu
from jax.sharding import PartitionSpec as P

SLABS = 8


BLUR = 0.24
AMBIENT = 0.1
SOFTEN = 0.05


def padded_2(block, sides, width):
    for axis, dim in sides:
        count = lax.axis_size(axis)
        forward = [(i, i + 1) for i in range(count - 1)]
        backward = [(target, source) for source, target in forward]
        low = lax.ppermute(
            lax.slice_in_dim(block, block.shape[dim] - width, None, axis=dim), axis, forward
        )
        high = lax.ppermute(lax.slice_in_dim(block, 0, width, axis=dim), axis, backward)
        block = jnp.concatenate([low, block, high], axis=dim)
    return block


def from_behind(value, axis, steps):
    count = lax.axis_size(axis)
    leading, last = (max(0, -steps), min(count, count - steps))
    return lax.ppermute(value, axis, [(source, source + steps) for source in range(leading, last)])


def from_partner(block, axis, apart):
    count = lax.axis_size(axis)
    route = []
    for low in range(count):
        high = low | 1 << apart
        if high != low and high < count:
            route += [(low, high), (high, low)]
    return lax.ppermute(block, axis, route)


def smooth(field):
    centre = field[1:-1, 1:-1, 1:-1]
    return (
        2.0 * centre
        + field[2:, 1:-1, 1:-1]
        + field[:-2, 1:-1, 1:-1]
        + field[1:-1, 2:, 1:-1]
        + field[1:-1, :-2, 1:-1]
        + field[1:-1, 1:-1, 2:]
        + field[1:-1, 1:-1, :-2]
    ) * 0.125


def shade_from(window, inside):
    slope_light = (window[2:, 1:-1, 1:-1] - window[:-2, 1:-1, 1:-1]) * 0.5
    slope_across = (window[1:-1, 2:, 1:-1] - window[1:-1, :-2, 1:-1]) * 0.5
    slope_view = (window[1:-1, 1:-1, 2:] - window[1:-1, 1:-1, :-2]) * 0.5
    along = 0.8 * slope_light + 0.36 * slope_across + 0.48 * slope_view
    aligned = along * along * inside
    trace = (slope_light * slope_light + slope_across * slope_across + slope_view * slope_view) * inside
    return 0.25 + smooth(aligned) / (smooth(trace) + SOFTEN)


def rim_mask(position, devices, width, border):
    places = position * width - border + jnp.arange(width + 2 * border, dtype=jnp.int32)
    return ((places >= 0) & (places < devices * width)).astype(jnp.float32)


def halo(block, axis, dim, width):
    count = lax.axis_size(axis)
    size = block.shape[dim]
    lows, highs = [], []
    for hop in range(1, count):
        need = min(size, width - (hop - 1) * size)
        if need <= 0:
            break
        forward = [(i, i + hop) for i in range(count - hop)]
        backward = [(target, source) for source, target in forward]
        low = lax.slice_in_dim(block, size - need, None, axis=dim)
        lows.insert(0, lax.ppermute(low, axis, forward))
        highs.append(lax.ppermute(lax.slice_in_dim(block, 0, need, axis=dim), axis, backward))
    block = jnp.concatenate(lows + [block] + highs, axis=dim)
    missing = width - sum(part.shape[dim] for part in lows)
    if missing > 0:
        widths = [(0, 0)] * block.ndim
        widths[dim] = (missing, missing)
        block = jnp.pad(block, widths)
    return block


def plane_mask(border, brick_a, brick_v):
    return (
        rim_mask(lax.axis_index("across"), lax.axis_size("across"), brick_a, border)[:, None]
        * rim_mask(lax.axis_index("view"), lax.axis_size("view"), brick_v, border)[None, :]
    )


def propagate(current, border_in, fade_rim, brick_a, brick_v):
    widest = (fade_rim.shape[2] - brick_a) // 2
    starts = []
    for slab_num in range(SLABS):
        border = border_in - slab_num
        starts.append(current[:, border : border + brick_a, border : border + brick_v])
        offset = widest - border
        fade_here = fade_rim[
            :,
            slab_num,
            offset : offset + brick_a + 2 * border,
            offset : offset + brick_v + 2 * border,
        ]
        current = current * fade_here
        centre = current[:, 1:-1, 1:-1]
        current = centre + BLUR * (
            current[:, :-2, 1:-1]
            + current[:, 2:, 1:-1]
            + current[:, 1:-1, :-2]
            + current[:, 1:-1, 2:]
            - 4.0 * centre
        )
    return (current, jnp.stack(starts, axis=1))


def fade_rim_of(extinction_table, density_rim, labels_rim, mask, light_step):
    rows, rim_a, rim_v = density_rim.shape
    layer_rows = rows // SLABS
    colours, materials = extinction_table.shape
    chunk = 8 if rim_a % 8 == 0 else rim_a

    def kernel(table_ref, density_ref, labels_ref, mask_ref, out_ref):
        def one_slab(slab_num, carry):
            for first in range(0, rim_a, chunk):
                part = slice(first, first + chunk)
                depth = [None] * colours
                for row in range(layer_rows):
                    row_num = slab_num * layer_rows + row
                    here = labels_ref[row_num, part, :]
                    cells = density_ref[row_num, part, :]
                    looked = [jnp.full(here.shape, table_ref[c, 0]) for c in range(colours)]
                    for material in range(1, materials):
                        match = here == float(material)
                        looked = [
                            jnp.where(match, table_ref[c, material], looked[c]) for c in range(colours)
                        ]
                    for c in range(colours):
                        term = looked[c] * cells
                        depth[c] = term if depth[c] is None else depth[c] + term
                for c in range(colours):
                    out_ref[c, slab_num, part, :] = (
                        jnp.exp(-light_step * depth[c]) * mask_ref[part, :]
                    )
            return carry

        lax.fori_loop(0, SLABS, one_slab, 0)

    return pl.pallas_call(
        kernel,
        out_shape=jax.ShapeDtypeStruct((colours, SLABS, rim_a, rim_v), jnp.float32),
        in_specs=[
            pl.BlockSpec(memory_space=pltpu.SMEM),
            pl.BlockSpec(memory_space=pltpu.VMEM),
            pl.BlockSpec(memory_space=pltpu.VMEM),
            pl.BlockSpec(memory_space=pltpu.VMEM),
        ],
        out_specs=pl.BlockSpec(memory_space=pltpu.VMEM),
    )(extinction_table, density_rim, labels_rim, mask)


def shards(density, labels, sunlight, opacity_table, extinction_table, albedo_table):
    brick_l, brick_a, brick_v = density.shape
    n_light = lax.axis_size("light")
    n_view = lax.axis_size("view")
    n_across = lax.axis_size("across")
    full_l = brick_l * n_light
    full_v = brick_v * n_view
    light_step = 10.0 / full_l
    view_step = 2.0 / full_v
    layer_rows = brick_l // SLABS
    light_idx = lax.axis_index("light")
    view_idx = lax.axis_index("view")
    across_idx = lax.axis_index("across")
    widest = SLABS * n_light
    stack = jnp.concatenate([density, labels.astype(jnp.float32), sunlight], axis=0)
    stack_rim = halo(halo(stack, "across", 1, widest), "view", 2, widest)
    density_rim = stack_rim[:brick_l]
    labels_rim = stack_rim[brick_l : 2 * brick_l]
    sun_rim = stack_rim[2 * brick_l :]
    density_side = density_rim[
        :, widest - 2 : widest + brick_a + 2, widest - 2 : widest + brick_v + 2
    ]
    table_all = jnp.concatenate([opacity_table[None], extinction_table, albedo_table], axis=0)
    looked = jnp.broadcast_to(table_all[:, 0, None, None, None], (7,) + labels.shape)
    for material in range(1, table_all.shape[1]):
        looked = jnp.where(
            (labels == material)[None], table_all[:, material, None, None, None], looked
        )
    extinct = looked[1:4] * density[None]
    extinct_slabs = extinct.reshape(3, SLABS, layer_rows, brick_a, brick_v)
    running = jnp.cumsum(extinct_slabs, axis=2) - extinct_slabs
    fade_rim = fade_rim_of(
        extinction_table, density_rim, labels_rim, plane_mask(widest, brick_a, brick_v), light_step
    )
    starts = None
    incoming = sun_rim
    for section_num in range(n_light):
        border = SLABS * (n_light - section_num)
        outgoing, starts = propagate(
            incoming, border, fade_rim, brick_a, brick_v
        )
        if section_num == 0:
            outgoing, density_side = lax.optimization_barrier((outgoing, density_side))
        if section_num + 1 < n_light:
            arrived = from_behind(outgoing, "light", 1)
            cut = widest - border + SLABS
            sun_here = sun_rim[:, cut : cut + brick_a + 2 * (border - SLABS), cut : cut + brick_v + 2 * (border - SLABS)]
            incoming = jnp.where(light_idx == 0, sun_here, arrived)
    padded = padded_2(density_side, (("light", 0),), 2)
    inside = (
        rim_mask(light_idx, n_light, brick_l, 1)[:, None, None]
        * rim_mask(across_idx, n_across, brick_a, 1)[None, :, None]
        * rim_mask(view_idx, n_view, brick_v, 1)[None, None, :]
    )
    shading = shade_from(padded, inside)
    lighting = (starts[:, :, None] * jnp.exp(-light_step * running)).reshape(
        3, brick_l, brick_a, brick_v
    )
    optical = looked[0] * density * view_step
    colour = (1.0 - jnp.exp(-optical))[None] * looked[4:7] * (shading[None] * lighting + AMBIENT)
    upper = (jnp.arange(brick_v)[:, None] < jnp.arange(brick_v)[None, :]).astype(jnp.float32)
    before = jnp.dot(optical.reshape(-1, brick_v), upper, precision=lax.Precision.HIGHEST).reshape(
        brick_l, brick_a, brick_v
    )
    colour_sum = jnp.sum(colour * jnp.exp(-before)[None], axis=-1)
    transmit = jnp.exp(-jnp.sum(optical, axis=-1))
    pixels = brick_l * brick_a
    piece_len = pixels // n_view
    image_now = jnp.concatenate(
        [colour_sum.reshape(3, n_view, piece_len), transmit.reshape(1, n_view, piece_len)], axis=0
    )
    bit_count = n_view.bit_length() - 1
    for bit_num in range(bit_count):
        kept = image_now.shape[1]
        pairs = image_now.reshape(4, kept // 2, 2, piece_len)
        my_bit = view_idx // 2**bit_num % 2
        first_half = my_bit == 0
        keep = jnp.where(first_half, pairs[:, :, 0], pairs[:, :, 1])
        send = jnp.where(first_half, pairs[:, :, 1], pairs[:, :, 0])
        got = from_partner(send, "view", bit_num)
        front = jnp.where(first_half, keep, got)
        back = jnp.where(first_half, got, keep)
        image_now = jnp.concatenate(
            [front[:3] + front[3:] * back[:3], keep[3:] * got[3:]], axis=0
        )
    final_colour = image_now[:3, 0]
    final_transmit = image_now[3:, 0]
    rows_out = brick_l // n_view
    opacity = 1.0 - final_transmit.reshape(1, rows_out, brick_a)
    return jnp.concatenate([final_colour.reshape(3, rows_out, brick_a), opacity], axis=0)


def solution(mesh):
    in_specs = (
        P("light", "across", "view"),
        P("light", "across", "view"),
        P(None, "across", "view"),
        P(),
        P(),
        P(),
    )
    out_specs = P(None, ("light", "view"), "across")
    return jax.shard_map(shards, mesh=mesh, in_specs=in_specs, out_specs=out_specs, check_vma=False)
```

```python
import jax
import jax.numpy as jnp
from jax import lax
from jax.experimental import pallas as pl
from jax.experimental.pallas import tpu as pltpu
from jax.sharding import PartitionSpec as P

SLABS = 8


BLUR = 0.24
AMBIENT = 0.1
SOFTEN = 0.05


def padded_2(block, sides, width):
    for axis, dim in sides:
        count = lax.axis_size(axis)
        forward = [(i, i + 1) for i in range(count - 1)]
        backward = [(target, source) for source, target in forward]
        low = lax.ppermute(
            lax.slice_in_dim(block, block.shape[dim] - width, None, axis=dim), axis, forward
        )
        high = lax.ppermute(lax.slice_in_dim(block, 0, width, axis=dim), axis, backward)
        block = jnp.concatenate([low, block, high], axis=dim)
    return block


def from_behind(value, axis, steps):
    count = lax.axis_size(axis)
    leading, last = (max(0, -steps), min(count, count - steps))
    return lax.ppermute(value, axis, [(source, source + steps) for source in range(leading, last)])


def from_partner(block, axis, apart):
    count = lax.axis_size(axis)
    route = []
    for low in range(count):
        high = low | 1 << apart
        if high != low and high < count:
            route += [(low, high), (high, low)]
    return lax.ppermute(block, axis, route)


def smooth(field):
    centre = field[1:-1, 1:-1, 1:-1]
    return (
        2.0 * centre
        + field[2:, 1:-1, 1:-1]
        + field[:-2, 1:-1, 1:-1]
        + field[1:-1, 2:, 1:-1]
        + field[1:-1, :-2, 1:-1]
        + field[1:-1, 1:-1, 2:]
        + field[1:-1, 1:-1, :-2]
    ) * 0.125


def shade_from(window, inside):
    slope_light = (window[2:, 1:-1, 1:-1] - window[:-2, 1:-1, 1:-1]) * 0.5
    slope_across = (window[1:-1, 2:, 1:-1] - window[1:-1, :-2, 1:-1]) * 0.5
    slope_view = (window[1:-1, 1:-1, 2:] - window[1:-1, 1:-1, :-2]) * 0.5
    along = 0.8 * slope_light + 0.36 * slope_across + 0.48 * slope_view
    aligned = along * along * inside
    trace = (slope_light * slope_light + slope_across * slope_across + slope_view * slope_view) * inside
    return 0.25 + smooth(aligned) / (smooth(trace) + SOFTEN)


def rim_mask(position, devices, width, border):
    places = position * width - border + jnp.arange(width + 2 * border, dtype=jnp.int32)
    return ((places >= 0) & (places < devices * width)).astype(jnp.float32)


def halo(block, axis, dim, width):
    count = lax.axis_size(axis)
    size = block.shape[dim]
    lows, highs = [], []
    if count == 2:
        need = min(size, width)
        first = lax.axis_index(axis) == 0
        send = block
        if need < size:
            send = jnp.where(
                first,
                lax.slice_in_dim(block, size - need, None, axis=dim),
                lax.slice_in_dim(block, 0, need, axis=dim),
            )
        got = lax.ppermute(send, axis, [(0, 1), (1, 0)])
        lows = [jnp.where(first, jnp.zeros_like(got), got)]
        highs = [jnp.where(first, got, jnp.zeros_like(got))]
        count = 0
    for hop in range(1, count):
        need = min(size, width - (hop - 1) * size)
        if need <= 0:
            break
        forward = [(i, i + hop) for i in range(count - hop)]
        backward = [(target, source) for source, target in forward]
        low = lax.slice_in_dim(block, size - need, None, axis=dim)
        lows.insert(0, lax.ppermute(low, axis, forward))
        highs.append(lax.ppermute(lax.slice_in_dim(block, 0, need, axis=dim), axis, backward))
    block = jnp.concatenate(lows + [block] + highs, axis=dim)
    missing = width - sum(part.shape[dim] for part in lows)
    if missing > 0:
        widths = [(0, 0)] * block.ndim
        widths[dim] = (missing, missing)
        block = jnp.pad(block, widths)
    return block


def plane_mask(border, brick_a, brick_v):
    return (
        rim_mask(lax.axis_index("across"), lax.axis_size("across"), brick_a, border)[:, None]
        * rim_mask(lax.axis_index("view"), lax.axis_size("view"), brick_v, border)[None, :]
    )


def propagate(current, border_in, fade_rim, brick_a, brick_v):
    widest = (fade_rim.shape[2] - brick_a) // 2
    starts = []
    for slab_num in range(SLABS):
        border = border_in - slab_num
        starts.append(current[:, border : border + brick_a, border : border + brick_v])
        offset = widest - border
        fade_here = fade_rim[
            :,
            slab_num,
            offset : offset + brick_a + 2 * border,
            offset : offset + brick_v + 2 * border,
        ]
        current = current * fade_here
        centre = current[:, 1:-1, 1:-1]
        current = centre + BLUR * (
            current[:, :-2, 1:-1]
            + current[:, 2:, 1:-1]
            + current[:, 1:-1, :-2]
            + current[:, 1:-1, 2:]
            - 4.0 * centre
        )
    return (current, jnp.stack(starts, axis=1))


def fade_rim_of(extinction_table, density_rim, labels_rim, mask, light_step):
    rows, rim_a, rim_v = density_rim.shape
    layer_rows = rows // SLABS
    colours, materials = extinction_table.shape
    chunk = 8 if rim_a % 8 == 0 else rim_a

    def kernel(table_ref, density_ref, labels_ref, mask_ref, out_ref):
        def one_slab(slab_num, carry):
            for first in range(0, rim_a, chunk):
                part = slice(first, first + chunk)
                depth = [None] * colours
                for row in range(layer_rows):
                    row_num = slab_num * layer_rows + row
                    here = labels_ref[row_num, part, :]
                    cells = density_ref[row_num, part, :]
                    looked = [jnp.full(here.shape, table_ref[c, 0]) for c in range(colours)]
                    for material in range(1, materials):
                        match = here == float(material)
                        looked = [
                            jnp.where(match, table_ref[c, material], looked[c]) for c in range(colours)
                        ]
                    for c in range(colours):
                        term = looked[c] * cells
                        depth[c] = term if depth[c] is None else depth[c] + term
                for c in range(colours):
                    out_ref[c, slab_num, part, :] = (
                        jnp.exp(-light_step * depth[c]) * mask_ref[part, :]
                    )
            return carry

        lax.fori_loop(0, SLABS, one_slab, 0)

    return pl.pallas_call(
        kernel,
        out_shape=jax.ShapeDtypeStruct((colours, SLABS, rim_a, rim_v), jnp.float32),
        in_specs=[
            pl.BlockSpec(memory_space=pltpu.SMEM),
            pl.BlockSpec(memory_space=pltpu.VMEM),
            pl.BlockSpec(memory_space=pltpu.VMEM),
            pl.BlockSpec(memory_space=pltpu.VMEM),
        ],
        out_specs=pl.BlockSpec(memory_space=pltpu.VMEM),
    )(extinction_table, density_rim, labels_rim, mask)


def shards(density, labels, sunlight, opacity_table, extinction_table, albedo_table):
    brick_l, brick_a, brick_v = density.shape
    n_light = lax.axis_size("light")
    n_view = lax.axis_size("view")
    n_across = lax.axis_size("across")
    full_l = brick_l * n_light
    full_v = brick_v * n_view
    light_step = 10.0 / full_l
    view_step = 2.0 / full_v
    layer_rows = brick_l // SLABS
    light_idx = lax.axis_index("light")
    view_idx = lax.axis_index("view")
    across_idx = lax.axis_index("across")
    widest = SLABS * n_light
    stack = jnp.concatenate([density, labels.astype(jnp.float32), sunlight], axis=0)
    stack_rim = halo(halo(stack, "across", 1, widest), "view", 2, widest)
    density_rim = stack_rim[:brick_l]
    labels_rim = stack_rim[brick_l : 2 * brick_l]
    sun_rim = stack_rim[2 * brick_l :]
    density_side = density_rim[
        :, widest - 2 : widest + brick_a + 2, widest - 2 : widest + brick_v + 2
    ]
    table_all = jnp.concatenate([opacity_table[None], extinction_table, albedo_table], axis=0)
    looked = jnp.broadcast_to(table_all[:, 0, None, None, None], (7,) + labels.shape)
    for material in range(1, table_all.shape[1]):
        looked = jnp.where(
            (labels == material)[None], table_all[:, material, None, None, None], looked
        )
    extinct = looked[1:4] * density[None]
    extinct_slabs = extinct.reshape(3, SLABS, layer_rows, brick_a, brick_v)
    running = jnp.cumsum(extinct_slabs, axis=2) - extinct_slabs
    fade_rim = fade_rim_of(
        extinction_table, density_rim, labels_rim, plane_mask(widest, brick_a, brick_v), light_step
    )
    starts = None
    incoming = sun_rim
    for section_num in range(n_light):
        border = SLABS * (n_light - section_num)
        outgoing, starts = propagate(
            incoming, border, fade_rim, brick_a, brick_v
        )
        if section_num == 0:
            outgoing, density_side = lax.optimization_barrier((outgoing, density_side))
        if section_num + 1 < n_light:
            arrived = from_behind(outgoing, "light", 1)
            cut = widest - border + SLABS
            sun_here = sun_rim[:, cut : cut + brick_a + 2 * (border - SLABS), cut : cut + brick_v + 2 * (border - SLABS)]
            incoming = jnp.where(light_idx == 0, sun_here, arrived)
    padded = padded_2(density_side, (("light", 0),), 2)
    inside = (
        rim_mask(light_idx, n_light, brick_l, 1)[:, None, None]
        * rim_mask(across_idx, n_across, brick_a, 1)[None, :, None]
        * rim_mask(view_idx, n_view, brick_v, 1)[None, None, :]
    )
    shading = shade_from(padded, inside)
    lighting = (starts[:, :, None] * jnp.exp(-light_step * running)).reshape(
        3, brick_l, brick_a, brick_v
    )
    optical = looked[0] * density * view_step
    colour = (1.0 - jnp.exp(-optical))[None] * looked[4:7] * (shading[None] * lighting + AMBIENT)
    upper = (jnp.arange(brick_v)[:, None] < jnp.arange(brick_v)[None, :]).astype(jnp.float32)
    before = jnp.dot(optical.reshape(-1, brick_v), upper, precision=lax.Precision.HIGHEST).reshape(
        brick_l, brick_a, brick_v
    )
    colour_sum = jnp.sum(colour * jnp.exp(-before)[None], axis=-1)
    transmit = jnp.exp(-jnp.sum(optical, axis=-1))
    pixels = brick_l * brick_a
    piece_len = pixels // n_view
    image_now = jnp.concatenate(
        [colour_sum.reshape(3, n_view, piece_len), transmit.reshape(1, n_view, piece_len)], axis=0
    )
    segments = lax.all_to_all(image_now, "view", 1, 1, tiled=True)
    final_colour = segments[:3, n_view - 1]
    final_transmit = segments[3:, n_view - 1]
    for segment in range(n_view - 2, -1, -1):
        final_colour = segments[:3, segment] + segments[3:, segment] * final_colour
        final_transmit = segments[3:, segment] * final_transmit
    rows_out = brick_l // n_view
    opacity = 1.0 - final_transmit.reshape(1, rows_out, brick_a)
    return jnp.concatenate([final_colour.reshape(3, rows_out, brick_a), opacity], axis=0)


def solution(mesh):
    in_specs = (
        P("light", "across", "view"),
        P("light", "across", "view"),
        P(None, "across", "view"),
        P(),
        P(),
        P(),
    )
    out_specs = P(None, ("light", "view"), "across")
    return jax.shard_map(shards, mesh=mesh, in_specs=in_specs, out_specs=out_specs, check_vma=False)
```

```python
import jax
import jax.numpy as jnp
from jax import lax
from jax.experimental import pallas as pl
from jax.experimental.pallas import tpu as pltpu
from jax.sharding import PartitionSpec as P

SLABS = 8


BLUR = 0.24
AMBIENT = 0.1
SOFTEN = 0.05


def padded_2(block, sides, width):
    for axis, dim in sides:
        count = lax.axis_size(axis)
        forward = [(i, i + 1) for i in range(count - 1)]
        backward = [(target, source) for source, target in forward]
        low = lax.ppermute(
            lax.slice_in_dim(block, block.shape[dim] - width, None, axis=dim), axis, forward
        )
        high = lax.ppermute(lax.slice_in_dim(block, 0, width, axis=dim), axis, backward)
        block = jnp.concatenate([low, block, high], axis=dim)
    return block


def from_behind(value, axis, steps):
    count = lax.axis_size(axis)
    leading, last = (max(0, -steps), min(count, count - steps))
    return lax.ppermute(value, axis, [(source, source + steps) for source in range(leading, last)])


def from_partner(block, axis, apart):
    count = lax.axis_size(axis)
    route = []
    for low in range(count):
        high = low | 1 << apart
        if high != low and high < count:
            route += [(low, high), (high, low)]
    return lax.ppermute(block, axis, route)


def smooth(field):
    centre = field[1:-1, 1:-1, 1:-1]
    return (
        2.0 * centre
        + field[2:, 1:-1, 1:-1]
        + field[:-2, 1:-1, 1:-1]
        + field[1:-1, 2:, 1:-1]
        + field[1:-1, :-2, 1:-1]
        + field[1:-1, 1:-1, 2:]
        + field[1:-1, 1:-1, :-2]
    ) * 0.125


def shade_from(window, inside):
    slope_light = (window[2:, 1:-1, 1:-1] - window[:-2, 1:-1, 1:-1]) * 0.5
    slope_across = (window[1:-1, 2:, 1:-1] - window[1:-1, :-2, 1:-1]) * 0.5
    slope_view = (window[1:-1, 1:-1, 2:] - window[1:-1, 1:-1, :-2]) * 0.5
    along = 0.8 * slope_light + 0.36 * slope_across + 0.48 * slope_view
    aligned = along * along * inside
    trace = (slope_light * slope_light + slope_across * slope_across + slope_view * slope_view) * inside
    return 0.25 + smooth(aligned) / (smooth(trace) + SOFTEN)


def rim_mask(position, devices, width, border):
    places = position * width - border + jnp.arange(width + 2 * border, dtype=jnp.int32)
    return ((places >= 0) & (places < devices * width)).astype(jnp.float32)


def halo(block, axis, dim, width):
    count = lax.axis_size(axis)
    size = block.shape[dim]
    lows, highs = [], []
    if count == 2:
        need = min(size, width)
        first = lax.axis_index(axis) == 0
        send = block
        if need < size:
            send = jnp.where(
                first,
                lax.slice_in_dim(block, size - need, None, axis=dim),
                lax.slice_in_dim(block, 0, need, axis=dim),
            )
        got = lax.ppermute(send, axis, [(0, 1), (1, 0)])
        lows = [jnp.where(first, jnp.zeros_like(got), got)]
        highs = [jnp.where(first, got, jnp.zeros_like(got))]
        count = 0
    for hop in range(1, count):
        need = min(size, width - (hop - 1) * size)
        if need <= 0:
            break
        forward = [(i, i + hop) for i in range(count - hop)]
        backward = [(target, source) for source, target in forward]
        low = lax.slice_in_dim(block, size - need, None, axis=dim)
        lows.insert(0, lax.ppermute(low, axis, forward))
        highs.append(lax.ppermute(lax.slice_in_dim(block, 0, need, axis=dim), axis, backward))
    block = jnp.concatenate(lows + [block] + highs, axis=dim)
    missing = width - sum(part.shape[dim] for part in lows)
    if missing > 0:
        widths = [(0, 0)] * block.ndim
        widths[dim] = (missing, missing)
        block = jnp.pad(block, widths)
    return block


def plane_mask(border, brick_a, brick_v):
    return (
        rim_mask(lax.axis_index("across"), lax.axis_size("across"), brick_a, border)[:, None]
        * rim_mask(lax.axis_index("view"), lax.axis_size("view"), brick_v, border)[None, :]
    )


def propagate(current, border_in, fade_rim, brick_a, brick_v):
    widest = (fade_rim.shape[2] - brick_a) // 2
    starts = []
    for slab_num in range(SLABS):
        border = border_in - slab_num
        starts.append(current[:, border : border + brick_a, border : border + brick_v])
        offset = widest - border
        fade_here = fade_rim[
            :,
            slab_num,
            offset : offset + brick_a + 2 * border,
            offset : offset + brick_v + 2 * border,
        ]
        current = current * fade_here
        centre = current[:, 1:-1, 1:-1]
        current = centre + BLUR * (
            current[:, :-2, 1:-1]
            + current[:, 2:, 1:-1]
            + current[:, 1:-1, :-2]
            + current[:, 1:-1, 2:]
            - 4.0 * centre
        )
    return (current, jnp.stack(starts, axis=1))


def fade_rim_of(extinction_table, density_rim, labels_rim, mask, light_step):
    rows, rim_a, rim_v = density_rim.shape
    layer_rows = rows // SLABS
    colours, materials = extinction_table.shape
    chunk = 8 if rim_a % 8 == 0 else rim_a

    def kernel(table_ref, density_ref, labels_ref, mask_ref, out_ref):
        def one_slab(slab_num, carry):
            for first in range(0, rim_a, chunk):
                part = slice(first, first + chunk)
                depth = [None] * colours
                for row in range(layer_rows):
                    row_num = slab_num * layer_rows + row
                    here = labels_ref[row_num, part, :]
                    cells = density_ref[row_num, part, :]
                    looked = [jnp.full(here.shape, table_ref[c, 0]) for c in range(colours)]
                    for material in range(1, materials):
                        match = here == float(material)
                        looked = [
                            jnp.where(match, table_ref[c, material], looked[c]) for c in range(colours)
                        ]
                    for c in range(colours):
                        term = looked[c] * cells
                        depth[c] = term if depth[c] is None else depth[c] + term
                for c in range(colours):
                    out_ref[c, slab_num, part, :] = (
                        jnp.exp(-light_step * depth[c]) * mask_ref[part, :]
                    )
            return carry

        lax.fori_loop(0, SLABS, one_slab, 0)

    return pl.pallas_call(
        kernel,
        out_shape=jax.ShapeDtypeStruct((colours, SLABS, rim_a, rim_v), jnp.float32),
        in_specs=[
            pl.BlockSpec(memory_space=pltpu.SMEM),
            pl.BlockSpec(memory_space=pltpu.VMEM),
            pl.BlockSpec(memory_space=pltpu.VMEM),
            pl.BlockSpec(memory_space=pltpu.VMEM),
        ],
        out_specs=pl.BlockSpec(memory_space=pltpu.VMEM),
    )(extinction_table, density_rim, labels_rim, mask)


def shards(density, labels, sunlight, opacity_table, extinction_table, albedo_table):
    brick_l, brick_a, brick_v = density.shape
    n_light = lax.axis_size("light")
    n_view = lax.axis_size("view")
    n_across = lax.axis_size("across")
    full_l = brick_l * n_light
    full_v = brick_v * n_view
    light_step = 10.0 / full_l
    view_step = 2.0 / full_v
    layer_rows = brick_l // SLABS
    light_idx = lax.axis_index("light")
    view_idx = lax.axis_index("view")
    across_idx = lax.axis_index("across")
    widest = SLABS * n_light
    stack = jnp.concatenate([density, labels.astype(jnp.float32), sunlight], axis=0)
    stack_rim = halo(halo(stack, "across", 1, widest), "view", 2, widest)
    density_rim = stack_rim[:brick_l]
    labels_rim = stack_rim[brick_l : 2 * brick_l]
    sun_rim = stack_rim[2 * brick_l :]
    density_side = density_rim[
        :, widest - 2 : widest + brick_a + 2, widest - 2 : widest + brick_v + 2
    ]
    table_all = jnp.concatenate([opacity_table[None], extinction_table, albedo_table], axis=0)
    looked = jnp.broadcast_to(table_all[:, 0, None, None, None], (7,) + labels.shape)
    for material in range(1, table_all.shape[1]):
        looked = jnp.where(
            (labels == material)[None], table_all[:, material, None, None, None], looked
        )
    extinct = looked[1:4] * density[None]
    extinct_slabs = extinct.reshape(3, SLABS, layer_rows, brick_a, brick_v)
    running = jnp.cumsum(extinct_slabs, axis=2) - extinct_slabs
    fade_rim = fade_rim_of(
        extinction_table, density_rim, labels_rim, plane_mask(widest, brick_a, brick_v), light_step
    )
    starts = None
    incoming = sun_rim
    for section_num in range(n_light):
        border = SLABS * (n_light - section_num)
        outgoing, starts = propagate(
            incoming, border, fade_rim, brick_a, brick_v
        )
        if section_num == 0:
            outgoing, density_side = lax.optimization_barrier((outgoing, density_side))
        if section_num + 1 < n_light:
            arrived = from_behind(outgoing, "light", 1)
            cut = widest - border + SLABS
            sun_here = sun_rim[:, cut : cut + brick_a + 2 * (border - SLABS), cut : cut + brick_v + 2 * (border - SLABS)]
            incoming = jnp.where(light_idx == 0, sun_here, arrived)
    padded = padded_2(density_side, (("light", 0),), 2)
    inside = (
        rim_mask(light_idx, n_light, brick_l, 1)[:, None, None]
        * rim_mask(across_idx, n_across, brick_a, 1)[None, :, None]
        * rim_mask(view_idx, n_view, brick_v, 1)[None, None, :]
    )
    shading = shade_from(padded, inside)
    lighting = (starts[:, :, None] * jnp.exp(-light_step * running)).reshape(
        3, brick_l, brick_a, brick_v
    )
    optical = looked[0] * density * view_step
    colour = (1.0 - jnp.exp(-optical))[None] * looked[4:7] * (shading[None] * lighting + AMBIENT)
    upper = (jnp.arange(brick_v)[:, None] < jnp.arange(brick_v)[None, :]).astype(jnp.float32)
    before = jnp.dot(optical.reshape(-1, brick_v), upper, precision=lax.Precision.HIGHEST).reshape(
        brick_l, brick_a, brick_v
    )
    colour_sum = jnp.sum(colour * jnp.exp(-before)[None], axis=-1)
    transmit = jnp.exp(-jnp.sum(optical, axis=-1))
    pixels = brick_l * brick_a
    piece_len = pixels // n_view
    image_now = jnp.concatenate(
        [colour_sum.reshape(3, n_view, piece_len), transmit.reshape(1, n_view, piece_len)], axis=0
    )
    bit_count = n_view.bit_length() - 1
    for bit_num in range(bit_count):
        kept = image_now.shape[1]
        pairs = image_now.reshape(4, kept // 2, 2, piece_len)
        my_bit = view_idx // 2**bit_num % 2
        first_half = my_bit == 0
        keep = jnp.where(first_half, pairs[:, :, 0], pairs[:, :, 1])
        send = jnp.where(first_half, pairs[:, :, 1], pairs[:, :, 0])
        got = from_partner(send, "view", bit_num)
        front = jnp.where(first_half, keep, got)
        back = jnp.where(first_half, got, keep)
        image_now = jnp.concatenate(
            [front[:3] + front[3:] * back[:3], keep[3:] * got[3:]], axis=0
        )
    final_colour = image_now[:3, 0]
    final_transmit = image_now[3:, 0]
    rows_out = brick_l // n_view
    opacity = 1.0 - final_transmit.reshape(1, rows_out, brick_a)
    return jnp.concatenate([final_colour.reshape(3, rows_out, brick_a), opacity], axis=0)


def solution(mesh):
    in_specs = (
        P("light", "across", "view"),
        P("light", "across", "view"),
        P(None, "across", "view"),
        P(),
        P(),
        P(),
    )
    out_specs = P(None, ("light", "view"), "across")
    return jax.shard_map(shards, mesh=mesh, in_specs=in_specs, out_specs=out_specs, check_vma=False)
```

```python
import jax
import jax.numpy as jnp
from jax import lax
from jax.experimental import pallas as pl
from jax.experimental.pallas import tpu as pltpu
from jax.sharding import PartitionSpec as P

SLABS = 8


BLUR = 0.24
AMBIENT = 0.1
SOFTEN = 0.05


def padded_2(block, sides, width):
    for axis, dim in sides:
        count = lax.axis_size(axis)
        forward = [(i, i + 1) for i in range(count - 1)]
        backward = [(target, source) for source, target in forward]
        low = lax.ppermute(
            lax.slice_in_dim(block, block.shape[dim] - width, None, axis=dim), axis, forward
        )
        high = lax.ppermute(lax.slice_in_dim(block, 0, width, axis=dim), axis, backward)
        block = jnp.concatenate([low, block, high], axis=dim)
    return block


def from_behind(value, axis, steps):
    count = lax.axis_size(axis)
    leading, last = (max(0, -steps), min(count, count - steps))
    return lax.ppermute(value, axis, [(source, source + steps) for source in range(leading, last)])


def from_partner(block, axis, apart):
    count = lax.axis_size(axis)
    route = []
    for low in range(count):
        high = low | 1 << apart
        if high != low and high < count:
            route += [(low, high), (high, low)]
    return lax.ppermute(block, axis, route)


def smooth(field):
    centre = field[1:-1, 1:-1, 1:-1]
    return (
        2.0 * centre
        + field[2:, 1:-1, 1:-1]
        + field[:-2, 1:-1, 1:-1]
        + field[1:-1, 2:, 1:-1]
        + field[1:-1, :-2, 1:-1]
        + field[1:-1, 1:-1, 2:]
        + field[1:-1, 1:-1, :-2]
    ) * 0.125


def shade_from(window, inside):
    slope_light = (window[2:, 1:-1, 1:-1] - window[:-2, 1:-1, 1:-1]) * 0.5
    slope_across = (window[1:-1, 2:, 1:-1] - window[1:-1, :-2, 1:-1]) * 0.5
    slope_view = (window[1:-1, 1:-1, 2:] - window[1:-1, 1:-1, :-2]) * 0.5
    along = 0.8 * slope_light + 0.36 * slope_across + 0.48 * slope_view
    aligned = along * along * inside
    trace = (slope_light * slope_light + slope_across * slope_across + slope_view * slope_view) * inside
    return 0.25 + smooth(aligned) / (smooth(trace) + SOFTEN)


def rim_mask(position, devices, width, border):
    places = position * width - border + jnp.arange(width + 2 * border, dtype=jnp.int32)
    return ((places >= 0) & (places < devices * width)).astype(jnp.float32)


def halo(block, axis, dim, width):
    count = lax.axis_size(axis)
    size = block.shape[dim]
    lows, highs = [], []
    if count == 2:
        need = min(size, width)
        first = lax.axis_index(axis) == 0
        send = block
        if need < size:
            send = jnp.where(
                first,
                lax.slice_in_dim(block, size - need, None, axis=dim),
                lax.slice_in_dim(block, 0, need, axis=dim),
            )
        got = lax.ppermute(send, axis, [(0, 1), (1, 0)])
        lows = [jnp.where(first, jnp.zeros_like(got), got)]
        highs = [jnp.where(first, got, jnp.zeros_like(got))]
        count = 0
    for hop in range(1, count):
        need = min(size, width - (hop - 1) * size)
        if need <= 0:
            break
        forward = [(i, i + hop) for i in range(count - hop)]
        backward = [(target, source) for source, target in forward]
        low = lax.slice_in_dim(block, size - need, None, axis=dim)
        lows.insert(0, lax.ppermute(low, axis, forward))
        highs.append(lax.ppermute(lax.slice_in_dim(block, 0, need, axis=dim), axis, backward))
    block = jnp.concatenate(lows + [block] + highs, axis=dim)
    missing = width - sum(part.shape[dim] for part in lows)
    if missing > 0:
        widths = [(0, 0)] * block.ndim
        widths[dim] = (missing, missing)
        block = jnp.pad(block, widths)
    return block


def plane_mask(border, brick_a, brick_v):
    return (
        rim_mask(lax.axis_index("across"), lax.axis_size("across"), brick_a, border)[:, None]
        * rim_mask(lax.axis_index("view"), lax.axis_size("view"), brick_v, border)[None, :]
    )


def propagate(current, border_in, fade_rim, brick_a, brick_v):
    widest = (fade_rim.shape[2] - brick_a) // 2
    starts = []
    for slab_num in range(SLABS):
        border = border_in - slab_num
        starts.append(current[:, border : border + brick_a, border : border + brick_v])
        offset = widest - border
        fade_here = fade_rim[
            :,
            slab_num,
            offset : offset + brick_a + 2 * border,
            offset : offset + brick_v + 2 * border,
        ]
        current = current * fade_here
        centre = current[:, 1:-1, 1:-1]
        current = centre + BLUR * (
            current[:, :-2, 1:-1]
            + current[:, 2:, 1:-1]
            + current[:, 1:-1, :-2]
            + current[:, 1:-1, 2:]
            - 4.0 * centre
        )
    return (current, jnp.stack(starts, axis=1))


def fade_rim_of(extinction_table, stack_rim, rows, mask, light_step):
    _, rim_a, rim_v = stack_rim.shape
    layer_rows = rows // SLABS
    colours, materials = extinction_table.shape
    chunk = 8 if rim_a % 8 == 0 else rim_a

    def kernel(table_ref, stack_ref, mask_ref, out_ref):
        def one_slab(slab_num, carry):
            for first in range(0, rim_a, chunk):
                part = slice(first, first + chunk)
                depth = [None] * colours
                for row in range(layer_rows):
                    row_num = slab_num * layer_rows + row
                    here = stack_ref[rows + row_num, part, :]
                    cells = stack_ref[row_num, part, :]
                    looked = [jnp.full(here.shape, table_ref[c, 0]) for c in range(colours)]
                    for material in range(1, materials):
                        match = here == float(material)
                        looked = [
                            jnp.where(match, table_ref[c, material], looked[c]) for c in range(colours)
                        ]
                    for c in range(colours):
                        term = looked[c] * cells
                        depth[c] = term if depth[c] is None else depth[c] + term
                for c in range(colours):
                    out_ref[c, slab_num, part, :] = (
                        jnp.exp(-light_step * depth[c]) * mask_ref[part, :]
                    )
            return carry

        lax.fori_loop(0, SLABS, one_slab, 0)

    return pl.pallas_call(
        kernel,
        out_shape=jax.ShapeDtypeStruct((colours, SLABS, rim_a, rim_v), jnp.float32),
        in_specs=[
            pl.BlockSpec(memory_space=pltpu.SMEM),
            pl.BlockSpec(memory_space=pltpu.VMEM),
            pl.BlockSpec(memory_space=pltpu.VMEM),
        ],
        out_specs=pl.BlockSpec(memory_space=pltpu.VMEM),
    )(extinction_table, stack_rim, mask)


def shards(density, labels, sunlight, opacity_table, extinction_table, albedo_table):
    brick_l, brick_a, brick_v = density.shape
    n_light = lax.axis_size("light")
    n_view = lax.axis_size("view")
    n_across = lax.axis_size("across")
    full_l = brick_l * n_light
    full_v = brick_v * n_view
    light_step = 10.0 / full_l
    view_step = 2.0 / full_v
    layer_rows = brick_l // SLABS
    light_idx = lax.axis_index("light")
    view_idx = lax.axis_index("view")
    across_idx = lax.axis_index("across")
    widest = SLABS * n_light
    stack = jnp.concatenate([density, labels.astype(jnp.float32), sunlight], axis=0)
    stack_rim = halo(halo(stack, "across", 1, widest), "view", 2, widest)
    density_rim = stack_rim[:brick_l]
    sun_rim = stack_rim[2 * brick_l :]
    density_side = density_rim[
        :, widest - 2 : widest + brick_a + 2, widest - 2 : widest + brick_v + 2
    ]
    table_all = jnp.concatenate([opacity_table[None], extinction_table, albedo_table], axis=0)
    looked = jnp.broadcast_to(table_all[:, 0, None, None, None], (7,) + labels.shape)
    for material in range(1, table_all.shape[1]):
        looked = jnp.where(
            (labels == material)[None], table_all[:, material, None, None, None], looked
        )
    extinct = looked[1:4] * density[None]
    extinct_slabs = extinct.reshape(3, SLABS, layer_rows, brick_a, brick_v)
    running = jnp.cumsum(extinct_slabs, axis=2) - extinct_slabs
    fade_rim = fade_rim_of(
        extinction_table, stack_rim, brick_l, plane_mask(widest, brick_a, brick_v), light_step
    )
    starts = None
    incoming = sun_rim
    for section_num in range(n_light):
        border = SLABS * (n_light - section_num)
        outgoing, starts = propagate(
            incoming, border, fade_rim, brick_a, brick_v
        )
        if section_num == 0:
            outgoing, density_side = lax.optimization_barrier((outgoing, density_side))
        if section_num + 1 < n_light:
            arrived = from_behind(outgoing, "light", 1)
            cut = widest - border + SLABS
            sun_here = sun_rim[:, cut : cut + brick_a + 2 * (border - SLABS), cut : cut + brick_v + 2 * (border - SLABS)]
            incoming = jnp.where(light_idx == 0, sun_here, arrived)
    padded = padded_2(density_side, (("light", 0),), 2)
    inside = (
        rim_mask(light_idx, n_light, brick_l, 1)[:, None, None]
        * rim_mask(across_idx, n_across, brick_a, 1)[None, :, None]
        * rim_mask(view_idx, n_view, brick_v, 1)[None, None, :]
    )
    shading = shade_from(padded, inside)
    lighting = (starts[:, :, None] * jnp.exp(-light_step * running)).reshape(
        3, brick_l, brick_a, brick_v
    )
    optical = looked[0] * density * view_step
    colour = (1.0 - jnp.exp(-optical))[None] * looked[4:7] * (shading[None] * lighting + AMBIENT)
    upper = (jnp.arange(brick_v)[:, None] < jnp.arange(brick_v)[None, :]).astype(jnp.float32)
    before = jnp.dot(optical.reshape(-1, brick_v), upper, precision=lax.Precision.HIGHEST).reshape(
        brick_l, brick_a, brick_v
    )
    colour_sum = jnp.sum(colour * jnp.exp(-before)[None], axis=-1)
    transmit = jnp.exp(-jnp.sum(optical, axis=-1))
    pixels = brick_l * brick_a
    piece_len = pixels // n_view
    image_now = jnp.concatenate(
        [colour_sum.reshape(3, n_view, piece_len), transmit.reshape(1, n_view, piece_len)], axis=0
    )
    bit_count = n_view.bit_length() - 1
    for bit_num in range(bit_count):
        kept = image_now.shape[1]
        pairs = image_now.reshape(4, kept // 2, 2, piece_len)
        my_bit = view_idx // 2**bit_num % 2
        first_half = my_bit == 0
        keep = jnp.where(first_half, pairs[:, :, 0], pairs[:, :, 1])
        send = jnp.where(first_half, pairs[:, :, 1], pairs[:, :, 0])
        got = from_partner(send, "view", bit_num)
        front = jnp.where(first_half, keep, got)
        back = jnp.where(first_half, got, keep)
        image_now = jnp.concatenate(
            [front[:3] + front[3:] * back[:3], keep[3:] * got[3:]], axis=0
        )
    final_colour = image_now[:3, 0]
    final_transmit = image_now[3:, 0]
    rows_out = brick_l // n_view
    opacity = 1.0 - final_transmit.reshape(1, rows_out, brick_a)
    return jnp.concatenate([final_colour.reshape(3, rows_out, brick_a), opacity], axis=0)


def solution(mesh):
    in_specs = (
        P("light", "across", "view"),
        P("light", "across", "view"),
        P(None, "across", "view"),
        P(),
        P(),
        P(),
    )
    out_specs = P(None, ("light", "view"), "across")
    return jax.shard_map(shards, mesh=mesh, in_specs=in_specs, out_specs=out_specs, check_vma=False)
```

```python
import jax
import jax.numpy as jnp
from jax import lax
from jax.experimental import pallas as pl
from jax.experimental.pallas import tpu as pltpu
from jax.sharding import PartitionSpec as P

SLABS = 8


BLUR = 0.24
AMBIENT = 0.1
SOFTEN = 0.05


def padded_2(block, sides, width):
    for axis, dim in sides:
        count = lax.axis_size(axis)
        forward = [(i, i + 1) for i in range(count - 1)]
        backward = [(target, source) for source, target in forward]
        low = lax.ppermute(
            lax.slice_in_dim(block, block.shape[dim] - width, None, axis=dim), axis, forward
        )
        high = lax.ppermute(lax.slice_in_dim(block, 0, width, axis=dim), axis, backward)
        block = jnp.concatenate([low, block, high], axis=dim)
    return block


def from_behind(value, axis, steps):
    count = lax.axis_size(axis)
    leading, last = (max(0, -steps), min(count, count - steps))
    return lax.ppermute(value, axis, [(source, source + steps) for source in range(leading, last)])


def from_partner(block, axis, apart):
    count = lax.axis_size(axis)
    route = []
    for low in range(count):
        high = low | 1 << apart
        if high != low and high < count:
            route += [(low, high), (high, low)]
    return lax.ppermute(block, axis, route)


def smooth(field):
    centre = field[1:-1, 1:-1, 1:-1]
    return (
        2.0 * centre
        + field[2:, 1:-1, 1:-1]
        + field[:-2, 1:-1, 1:-1]
        + field[1:-1, 2:, 1:-1]
        + field[1:-1, :-2, 1:-1]
        + field[1:-1, 1:-1, 2:]
        + field[1:-1, 1:-1, :-2]
    ) * 0.125


def shade_from(window, inside):
    slope_light = (window[2:, 1:-1, 1:-1] - window[:-2, 1:-1, 1:-1]) * 0.5
    slope_across = (window[1:-1, 2:, 1:-1] - window[1:-1, :-2, 1:-1]) * 0.5
    slope_view = (window[1:-1, 1:-1, 2:] - window[1:-1, 1:-1, :-2]) * 0.5
    along = 0.8 * slope_light + 0.36 * slope_across + 0.48 * slope_view
    aligned = along * along * inside
    trace = (slope_light * slope_light + slope_across * slope_across + slope_view * slope_view) * inside
    return 0.25 + smooth(aligned) / (smooth(trace) + SOFTEN)


def rim_mask(position, devices, width, border):
    places = position * width - border + jnp.arange(width + 2 * border, dtype=jnp.int32)
    return ((places >= 0) & (places < devices * width)).astype(jnp.float32)


def halo(block, axis, dim, width):
    count = lax.axis_size(axis)
    size = block.shape[dim]
    lows, highs = [], []
    if count == 2:
        need = min(size, width)
        first = lax.axis_index(axis) == 0
        send = block
        if need < size:
            send = jnp.where(
                first,
                lax.slice_in_dim(block, size - need, None, axis=dim),
                lax.slice_in_dim(block, 0, need, axis=dim),
            )
        got = lax.ppermute(send, axis, [(0, 1), (1, 0)])
        lows = [jnp.where(first, jnp.zeros_like(got), got)]
        highs = [jnp.where(first, got, jnp.zeros_like(got))]
        count = 0
    for hop in range(1, count):
        need = min(size, width - (hop - 1) * size)
        if need <= 0:
            break
        forward = [(i, i + hop) for i in range(count - hop)]
        backward = [(target, source) for source, target in forward]
        low = lax.slice_in_dim(block, size - need, None, axis=dim)
        lows.insert(0, lax.ppermute(low, axis, forward))
        highs.append(lax.ppermute(lax.slice_in_dim(block, 0, need, axis=dim), axis, backward))
    block = jnp.concatenate(lows + [block] + highs, axis=dim)
    missing = width - sum(part.shape[dim] for part in lows)
    if missing > 0:
        widths = [(0, 0)] * block.ndim
        widths[dim] = (missing, missing)
        block = jnp.pad(block, widths)
    return block


def plane_mask(border, brick_a, brick_v):
    return (
        rim_mask(lax.axis_index("across"), lax.axis_size("across"), brick_a, border)[:, None]
        * rim_mask(lax.axis_index("view"), lax.axis_size("view"), brick_v, border)[None, :]
    )


def propagate(current, border_in, fade_rim, brick_a, brick_v):
    widest = (fade_rim.shape[2] - brick_a) // 2
    starts = []
    for slab_num in range(SLABS):
        border = border_in - slab_num
        starts.append(current[:, border : border + brick_a, border : border + brick_v])
        offset = widest - border
        fade_here = fade_rim[
            :,
            slab_num,
            offset : offset + brick_a + 2 * border,
            offset : offset + brick_v + 2 * border,
        ]
        current = current * fade_here
        centre = current[:, 1:-1, 1:-1]
        current = centre + BLUR * (
            current[:, :-2, 1:-1]
            + current[:, 2:, 1:-1]
            + current[:, 1:-1, :-2]
            + current[:, 1:-1, 2:]
            - 4.0 * centre
        )
    return (current, jnp.stack(starts, axis=1))


def fade_rim_of(extinction_table, stack_rim, rows, mask, light_step):
    _, rim_a, rim_v = stack_rim.shape
    layer_rows = rows // SLABS
    colours, materials = extinction_table.shape
    chunk = 8 if rim_a % 8 == 0 else rim_a
    lanes = 128
    windows = sorted(set(list(range(0, rim_v - lanes + 1, lanes)) + [rim_v - lanes]))
    table_lanes = jnp.pad(
        jnp.broadcast_to(extinction_table[:, None, :], (colours, chunk, materials)),
        ((0, 0), (0, 0), (0, lanes - materials)),
    )

    def kernel(table_ref, stack_ref, mask_ref, out_ref):
        tables = [table_ref[c] for c in range(colours)]

        def one_slab(slab_num, carry):
            for first in range(0, rim_a, chunk):
                part = slice(first, first + chunk)
                for low in windows:
                    window = slice(low, low + lanes)
                    depth = [None] * colours
                    for row in range(layer_rows):
                        row_num = slab_num * layer_rows + row
                        here = stack_ref[rows + row_num, part, window].astype(jnp.int32)
                        cells = stack_ref[row_num, part, window]
                        for c in range(colours):
                            looked = jnp.take_along_axis(
                                tables[c], here, axis=1, mode="promise_in_bounds"
                            )
                            term = looked * cells
                            depth[c] = term if depth[c] is None else depth[c] + term
                    for c in range(colours):
                        out_ref[c, slab_num, part, window] = (
                            jnp.exp(-light_step * depth[c]) * mask_ref[part, window]
                        )
            return carry

        lax.fori_loop(0, SLABS, one_slab, 0)

    return pl.pallas_call(
        kernel,
        out_shape=jax.ShapeDtypeStruct((colours, SLABS, rim_a, rim_v), jnp.float32),
        in_specs=[
            pl.BlockSpec(memory_space=pltpu.VMEM),
            pl.BlockSpec(memory_space=pltpu.VMEM),
            pl.BlockSpec(memory_space=pltpu.VMEM),
        ],
        out_specs=pl.BlockSpec(memory_space=pltpu.VMEM),
    )(table_lanes, stack_rim, mask)


def shards(density, labels, sunlight, opacity_table, extinction_table, albedo_table):
    brick_l, brick_a, brick_v = density.shape
    n_light = lax.axis_size("light")
    n_view = lax.axis_size("view")
    n_across = lax.axis_size("across")
    full_l = brick_l * n_light
    full_v = brick_v * n_view
    light_step = 10.0 / full_l
    view_step = 2.0 / full_v
    layer_rows = brick_l // SLABS
    light_idx = lax.axis_index("light")
    view_idx = lax.axis_index("view")
    across_idx = lax.axis_index("across")
    widest = SLABS * n_light
    stack = jnp.concatenate([density, labels.astype(jnp.float32), sunlight], axis=0)
    stack_rim = halo(halo(stack, "across", 1, widest), "view", 2, widest)
    density_rim = stack_rim[:brick_l]
    sun_rim = stack_rim[2 * brick_l :]
    density_side = density_rim[
        :, widest - 2 : widest + brick_a + 2, widest - 2 : widest + brick_v + 2
    ]
    table_all = jnp.concatenate([opacity_table[None], extinction_table, albedo_table], axis=0)
    looked = jnp.broadcast_to(table_all[:, 0, None, None, None], (7,) + labels.shape)
    for material in range(1, table_all.shape[1]):
        looked = jnp.where(
            (labels == material)[None], table_all[:, material, None, None, None], looked
        )
    extinct = looked[1:4] * density[None]
    extinct_slabs = extinct.reshape(3, SLABS, layer_rows, brick_a, brick_v)
    running = jnp.cumsum(extinct_slabs, axis=2) - extinct_slabs
    fade_rim = fade_rim_of(
        extinction_table, stack_rim, brick_l, plane_mask(widest, brick_a, brick_v), light_step
    )
    starts = None
    incoming = sun_rim
    for section_num in range(n_light):
        border = SLABS * (n_light - section_num)
        outgoing, starts = propagate(
            incoming, border, fade_rim, brick_a, brick_v
        )
        if section_num == 0:
            outgoing, density_side = lax.optimization_barrier((outgoing, density_side))
        if section_num + 1 < n_light:
            arrived = from_behind(outgoing, "light", 1)
            cut = widest - border + SLABS
            sun_here = sun_rim[:, cut : cut + brick_a + 2 * (border - SLABS), cut : cut + brick_v + 2 * (border - SLABS)]
            incoming = jnp.where(light_idx == 0, sun_here, arrived)
    padded = padded_2(density_side, (("light", 0),), 2)
    inside = (
        rim_mask(light_idx, n_light, brick_l, 1)[:, None, None]
        * rim_mask(across_idx, n_across, brick_a, 1)[None, :, None]
        * rim_mask(view_idx, n_view, brick_v, 1)[None, None, :]
    )
    shading = shade_from(padded, inside)
    lighting = (starts[:, :, None] * jnp.exp(-light_step * running)).reshape(
        3, brick_l, brick_a, brick_v
    )
    optical = looked[0] * density * view_step
    colour = (1.0 - jnp.exp(-optical))[None] * looked[4:7] * (shading[None] * lighting + AMBIENT)
    upper = (jnp.arange(brick_v)[:, None] < jnp.arange(brick_v)[None, :]).astype(jnp.float32)
    before = jnp.dot(optical.reshape(-1, brick_v), upper, precision=lax.Precision.HIGHEST).reshape(
        brick_l, brick_a, brick_v
    )
    colour_sum = jnp.sum(colour * jnp.exp(-before)[None], axis=-1)
    transmit = jnp.exp(-jnp.sum(optical, axis=-1))
    pixels = brick_l * brick_a
    piece_len = pixels // n_view
    image_now = jnp.concatenate(
        [colour_sum.reshape(3, n_view, piece_len), transmit.reshape(1, n_view, piece_len)], axis=0
    )
    bit_count = n_view.bit_length() - 1
    for bit_num in range(bit_count):
        kept = image_now.shape[1]
        pairs = image_now.reshape(4, kept // 2, 2, piece_len)
        my_bit = view_idx // 2**bit_num % 2
        first_half = my_bit == 0
        keep = jnp.where(first_half, pairs[:, :, 0], pairs[:, :, 1])
        send = jnp.where(first_half, pairs[:, :, 1], pairs[:, :, 0])
        got = from_partner(send, "view", bit_num)
        front = jnp.where(first_half, keep, got)
        back = jnp.where(first_half, got, keep)
        image_now = jnp.concatenate(
            [front[:3] + front[3:] * back[:3], keep[3:] * got[3:]], axis=0
        )
    final_colour = image_now[:3, 0]
    final_transmit = image_now[3:, 0]
    rows_out = brick_l // n_view
    opacity = 1.0 - final_transmit.reshape(1, rows_out, brick_a)
    return jnp.concatenate([final_colour.reshape(3, rows_out, brick_a), opacity], axis=0)


def solution(mesh):
    in_specs = (
        P("light", "across", "view"),
        P("light", "across", "view"),
        P(None, "across", "view"),
        P(),
        P(),
        P(),
    )
    out_specs = P(None, ("light", "view"), "across")
    return jax.shard_map(shards, mesh=mesh, in_specs=in_specs, out_specs=out_specs, check_vma=False)
```

```python
import jax
import jax.numpy as jnp
from jax import lax
from jax.experimental import pallas as pl
from jax.experimental.pallas import tpu as pltpu
from jax.sharding import PartitionSpec as P

SLABS = 8


BLUR = 0.24
AMBIENT = 0.1
SOFTEN = 0.05


def padded_2(block, sides, width):
    for axis, dim in sides:
        count = lax.axis_size(axis)
        forward = [(i, i + 1) for i in range(count - 1)]
        backward = [(target, source) for source, target in forward]
        low = lax.ppermute(
            lax.slice_in_dim(block, block.shape[dim] - width, None, axis=dim), axis, forward
        )
        high = lax.ppermute(lax.slice_in_dim(block, 0, width, axis=dim), axis, backward)
        block = jnp.concatenate([low, block, high], axis=dim)
    return block


def from_behind(value, axis, steps):
    count = lax.axis_size(axis)
    leading, last = (max(0, -steps), min(count, count - steps))
    return lax.ppermute(value, axis, [(source, source + steps) for source in range(leading, last)])


def from_partner(block, axis, apart):
    count = lax.axis_size(axis)
    route = []
    for low in range(count):
        high = low | 1 << apart
        if high != low and high < count:
            route += [(low, high), (high, low)]
    return lax.ppermute(block, axis, route)


def smooth(field):
    centre = field[1:-1, 1:-1, 1:-1]
    return (
        2.0 * centre
        + field[2:, 1:-1, 1:-1]
        + field[:-2, 1:-1, 1:-1]
        + field[1:-1, 2:, 1:-1]
        + field[1:-1, :-2, 1:-1]
        + field[1:-1, 1:-1, 2:]
        + field[1:-1, 1:-1, :-2]
    ) * 0.125


def shade_from(window, inside):
    slope_light = (window[2:, 1:-1, 1:-1] - window[:-2, 1:-1, 1:-1]) * 0.5
    slope_across = (window[1:-1, 2:, 1:-1] - window[1:-1, :-2, 1:-1]) * 0.5
    slope_view = (window[1:-1, 1:-1, 2:] - window[1:-1, 1:-1, :-2]) * 0.5
    along = 0.8 * slope_light + 0.36 * slope_across + 0.48 * slope_view
    aligned = along * along * inside
    trace = (slope_light * slope_light + slope_across * slope_across + slope_view * slope_view) * inside
    return 0.25 + smooth(aligned) / (smooth(trace) + SOFTEN)


def rim_mask(position, devices, width, border):
    places = position * width - border + jnp.arange(width + 2 * border, dtype=jnp.int32)
    return ((places >= 0) & (places < devices * width)).astype(jnp.float32)


def halo(block, axis, dim, width):
    count = lax.axis_size(axis)
    size = block.shape[dim]
    lows, highs = [], []
    if count == 2:
        need = min(size, width)
        first = lax.axis_index(axis) == 0
        send = block
        if need < size:
            send = jnp.where(
                first,
                lax.slice_in_dim(block, size - need, None, axis=dim),
                lax.slice_in_dim(block, 0, need, axis=dim),
            )
        got = lax.ppermute(send, axis, [(0, 1), (1, 0)])
        lows = [jnp.where(first, jnp.zeros_like(got), got)]
        highs = [jnp.where(first, got, jnp.zeros_like(got))]
        count = 0
    for hop in range(1, count):
        need = min(size, width - (hop - 1) * size)
        if need <= 0:
            break
        forward = [(i, i + hop) for i in range(count - hop)]
        backward = [(target, source) for source, target in forward]
        low = lax.slice_in_dim(block, size - need, None, axis=dim)
        lows.insert(0, lax.ppermute(low, axis, forward))
        highs.append(lax.ppermute(lax.slice_in_dim(block, 0, need, axis=dim), axis, backward))
    block = jnp.concatenate(lows + [block] + highs, axis=dim)
    missing = width - sum(part.shape[dim] for part in lows)
    if missing > 0:
        widths = [(0, 0)] * block.ndim
        widths[dim] = (missing, missing)
        block = jnp.pad(block, widths)
    return block


def plane_mask(border, brick_a, brick_v):
    return (
        rim_mask(lax.axis_index("across"), lax.axis_size("across"), brick_a, border)[:, None]
        * rim_mask(lax.axis_index("view"), lax.axis_size("view"), brick_v, border)[None, :]
    )


def propagate(current, border_in, fade_rim, brick_a, brick_v):
    widest = (fade_rim.shape[2] - brick_a) // 2
    starts = []
    for slab_num in range(SLABS):
        border = border_in - slab_num
        starts.append(current[:, border : border + brick_a, border : border + brick_v])
        offset = widest - border
        fade_here = fade_rim[
            :,
            slab_num,
            offset : offset + brick_a + 2 * border,
            offset : offset + brick_v + 2 * border,
        ]
        current = current * fade_here
        centre = current[:, 1:-1, 1:-1]
        current = centre + BLUR * (
            current[:, :-2, 1:-1]
            + current[:, 2:, 1:-1]
            + current[:, 1:-1, :-2]
            + current[:, 1:-1, 2:]
            - 4.0 * centre
        )
    return (current, jnp.stack(starts, axis=1))


def fade_rim_of(extinction_table, stack_rim, rows, mask, light_step):
    _, rim_a, rim_v = stack_rim.shape
    layer_rows = rows // SLABS
    colours, materials = extinction_table.shape
    chunk = 16 if rim_a % 16 == 0 else (8 if rim_a % 8 == 0 else rim_a)

    def kernel(table_ref, stack_ref, mask_ref, out_ref):
        def one_slab(slab_num, carry):
            for first in range(0, rim_a, chunk):
                part = slice(first, first + chunk)
                depth = [None] * colours
                for row in range(layer_rows):
                    row_num = slab_num * layer_rows + row
                    here = stack_ref[rows + row_num, part, :]
                    cells = stack_ref[row_num, part, :]
                    looked = [jnp.full(here.shape, table_ref[c, 0]) for c in range(colours)]
                    for material in range(1, materials):
                        match = here == float(material)
                        looked = [
                            jnp.where(match, table_ref[c, material], looked[c]) for c in range(colours)
                        ]
                    for c in range(colours):
                        term = looked[c] * cells
                        depth[c] = term if depth[c] is None else depth[c] + term
                for c in range(colours):
                    out_ref[c, slab_num, part, :] = (
                        jnp.exp(-light_step * depth[c]) * mask_ref[part, :]
                    )
            return carry

        lax.fori_loop(0, SLABS, one_slab, 0)

    return pl.pallas_call(
        kernel,
        out_shape=jax.ShapeDtypeStruct((colours, SLABS, rim_a, rim_v), jnp.float32),
        in_specs=[
            pl.BlockSpec(memory_space=pltpu.SMEM),
            pl.BlockSpec(memory_space=pltpu.VMEM),
            pl.BlockSpec(memory_space=pltpu.VMEM),
        ],
        out_specs=pl.BlockSpec(memory_space=pltpu.VMEM),
    )(extinction_table, stack_rim, mask)


def shards(density, labels, sunlight, opacity_table, extinction_table, albedo_table):
    brick_l, brick_a, brick_v = density.shape
    n_light = lax.axis_size("light")
    n_view = lax.axis_size("view")
    n_across = lax.axis_size("across")
    full_l = brick_l * n_light
    full_v = brick_v * n_view
    light_step = 10.0 / full_l
    view_step = 2.0 / full_v
    layer_rows = brick_l // SLABS
    light_idx = lax.axis_index("light")
    view_idx = lax.axis_index("view")
    across_idx = lax.axis_index("across")
    widest = SLABS * n_light
    stack = jnp.concatenate([density, labels.astype(jnp.float32), sunlight], axis=0)
    stack_rim = halo(halo(stack, "across", 1, widest), "view", 2, widest)
    density_rim = stack_rim[:brick_l]
    sun_rim = stack_rim[2 * brick_l :]
    density_side = density_rim[
        :, widest - 2 : widest + brick_a + 2, widest - 2 : widest + brick_v + 2
    ]
    table_all = jnp.concatenate([opacity_table[None], extinction_table, albedo_table], axis=0)
    looked = jnp.broadcast_to(table_all[:, 0, None, None, None], (7,) + labels.shape)
    for material in range(1, table_all.shape[1]):
        looked = jnp.where(
            (labels == material)[None], table_all[:, material, None, None, None], looked
        )
    extinct = looked[1:4] * density[None]
    extinct_slabs = extinct.reshape(3, SLABS, layer_rows, brick_a, brick_v)
    running = jnp.cumsum(extinct_slabs, axis=2) - extinct_slabs
    fade_rim = fade_rim_of(
        extinction_table, stack_rim, brick_l, plane_mask(widest, brick_a, brick_v), light_step
    )
    starts = None
    incoming = sun_rim
    for section_num in range(n_light):
        border = SLABS * (n_light - section_num)
        outgoing, starts = propagate(
            incoming, border, fade_rim, brick_a, brick_v
        )
        if section_num == 0:
            outgoing, density_side = lax.optimization_barrier((outgoing, density_side))
        if section_num + 1 < n_light:
            arrived = from_behind(outgoing, "light", 1)
            cut = widest - border + SLABS
            sun_here = sun_rim[:, cut : cut + brick_a + 2 * (border - SLABS), cut : cut + brick_v + 2 * (border - SLABS)]
            incoming = jnp.where(light_idx == 0, sun_here, arrived)
    padded = padded_2(density_side, (("light", 0),), 2)
    inside = (
        rim_mask(light_idx, n_light, brick_l, 1)[:, None, None]
        * rim_mask(across_idx, n_across, brick_a, 1)[None, :, None]
        * rim_mask(view_idx, n_view, brick_v, 1)[None, None, :]
    )
    shading = shade_from(padded, inside)
    lighting = (starts[:, :, None] * jnp.exp(-light_step * running)).reshape(
        3, brick_l, brick_a, brick_v
    )
    optical = looked[0] * density * view_step
    colour = (1.0 - jnp.exp(-optical))[None] * looked[4:7] * (shading[None] * lighting + AMBIENT)
    upper = (jnp.arange(brick_v)[:, None] < jnp.arange(brick_v)[None, :]).astype(jnp.float32)
    before = jnp.dot(optical.reshape(-1, brick_v), upper, precision=lax.Precision.HIGHEST).reshape(
        brick_l, brick_a, brick_v
    )
    colour_sum = jnp.sum(colour * jnp.exp(-before)[None], axis=-1)
    transmit = jnp.exp(-jnp.sum(optical, axis=-1))
    pixels = brick_l * brick_a
    piece_len = pixels // n_view
    image_now = jnp.concatenate(
        [colour_sum.reshape(3, n_view, piece_len), transmit.reshape(1, n_view, piece_len)], axis=0
    )
    bit_count = n_view.bit_length() - 1
    for bit_num in range(bit_count):
        kept = image_now.shape[1]
        pairs = image_now.reshape(4, kept // 2, 2, piece_len)
        my_bit = view_idx // 2**bit_num % 2
        first_half = my_bit == 0
        keep = jnp.where(first_half, pairs[:, :, 0], pairs[:, :, 1])
        send = jnp.where(first_half, pairs[:, :, 1], pairs[:, :, 0])
        got = from_partner(send, "view", bit_num)
        front = jnp.where(first_half, keep, got)
        back = jnp.where(first_half, got, keep)
        image_now = jnp.concatenate(
            [front[:3] + front[3:] * back[:3], keep[3:] * got[3:]], axis=0
        )
    final_colour = image_now[:3, 0]
    final_transmit = image_now[3:, 0]
    rows_out = brick_l // n_view
    opacity = 1.0 - final_transmit.reshape(1, rows_out, brick_a)
    return jnp.concatenate([final_colour.reshape(3, rows_out, brick_a), opacity], axis=0)


def solution(mesh):
    in_specs = (
        P("light", "across", "view"),
        P("light", "across", "view"),
        P(None, "across", "view"),
        P(),
        P(),
        P(),
    )
    out_specs = P(None, ("light", "view"), "across")
    return jax.shard_map(shards, mesh=mesh, in_specs=in_specs, out_specs=out_specs, check_vma=False)
```

```python
import jax
import jax.numpy as jnp
from jax import lax
from jax.experimental import pallas as pl
from jax.experimental.pallas import tpu as pltpu
from jax.sharding import PartitionSpec as P

SLABS = 8


BLUR = 0.24
AMBIENT = 0.1
SOFTEN = 0.05


def padded_2(block, sides, width):
    for axis, dim in sides:
        count = lax.axis_size(axis)
        forward = [(i, i + 1) for i in range(count - 1)]
        backward = [(target, source) for source, target in forward]
        low = lax.ppermute(
            lax.slice_in_dim(block, block.shape[dim] - width, None, axis=dim), axis, forward
        )
        high = lax.ppermute(lax.slice_in_dim(block, 0, width, axis=dim), axis, backward)
        block = jnp.concatenate([low, block, high], axis=dim)
    return block


def from_behind(value, axis, steps):
    count = lax.axis_size(axis)
    leading, last = (max(0, -steps), min(count, count - steps))
    return lax.ppermute(value, axis, [(source, source + steps) for source in range(leading, last)])


def from_partner(block, axis, apart):
    count = lax.axis_size(axis)
    route = []
    for low in range(count):
        high = low | 1 << apart
        if high != low and high < count:
            route += [(low, high), (high, low)]
    return lax.ppermute(block, axis, route)


def smooth(field):
    centre = field[1:-1, 1:-1, 1:-1]
    return (
        2.0 * centre
        + field[2:, 1:-1, 1:-1]
        + field[:-2, 1:-1, 1:-1]
        + field[1:-1, 2:, 1:-1]
        + field[1:-1, :-2, 1:-1]
        + field[1:-1, 1:-1, 2:]
        + field[1:-1, 1:-1, :-2]
    ) * 0.125


def shade_from(window, inside):
    slope_light = (window[2:, 1:-1, 1:-1] - window[:-2, 1:-1, 1:-1]) * 0.5
    slope_across = (window[1:-1, 2:, 1:-1] - window[1:-1, :-2, 1:-1]) * 0.5
    slope_view = (window[1:-1, 1:-1, 2:] - window[1:-1, 1:-1, :-2]) * 0.5
    along = 0.8 * slope_light + 0.36 * slope_across + 0.48 * slope_view
    aligned = along * along * inside
    trace = (slope_light * slope_light + slope_across * slope_across + slope_view * slope_view) * inside
    return 0.25 + smooth(aligned) / (smooth(trace) + SOFTEN)


def rim_mask(position, devices, width, border):
    places = position * width - border + jnp.arange(width + 2 * border, dtype=jnp.int32)
    return ((places >= 0) & (places < devices * width)).astype(jnp.float32)


def halo(block, axis, dim, width):
    count = lax.axis_size(axis)
    size = block.shape[dim]
    lows, highs = [], []
    if count == 2:
        need = min(size, width)
        first = lax.axis_index(axis) == 0
        send = block
        if need < size:
            send = jnp.where(
                first,
                lax.slice_in_dim(block, size - need, None, axis=dim),
                lax.slice_in_dim(block, 0, need, axis=dim),
            )
        got = lax.ppermute(send, axis, [(0, 1), (1, 0)])
        lows = [jnp.where(first, jnp.zeros_like(got), got)]
        highs = [jnp.where(first, got, jnp.zeros_like(got))]
        count = 0
    for hop in range(1, count):
        need = min(size, width - (hop - 1) * size)
        if need <= 0:
            break
        forward = [(i, i + hop) for i in range(count - hop)]
        backward = [(target, source) for source, target in forward]
        low = lax.slice_in_dim(block, size - need, None, axis=dim)
        lows.insert(0, lax.ppermute(low, axis, forward))
        highs.append(lax.ppermute(lax.slice_in_dim(block, 0, need, axis=dim), axis, backward))
    block = jnp.concatenate(lows + [block] + highs, axis=dim)
    missing = width - sum(part.shape[dim] for part in lows)
    if missing > 0:
        widths = [(0, 0)] * block.ndim
        widths[dim] = (missing, missing)
        block = jnp.pad(block, widths)
    return block


def plane_mask(border, brick_a, brick_v):
    return (
        rim_mask(lax.axis_index("across"), lax.axis_size("across"), brick_a, border)[:, None]
        * rim_mask(lax.axis_index("view"), lax.axis_size("view"), brick_v, border)[None, :]
    )


def propagate(current, border_in, fade_rim, brick_a, brick_v):
    colours, _, rim_a, _ = fade_rim.shape
    widest = (rim_a - brick_a) // 2
    border_out = border_in - SLABS

    def kernel(current_ref, fade_ref, out_ref, starts_ref):
        for c in range(colours):
            plane = current_ref[c]
            for slab_num in range(SLABS):
                border = border_in - slab_num
                starts_ref[c, slab_num] = plane[border : border + brick_a, border : border + brick_v]
                offset = widest - border
                fade_here = fade_ref[c, slab_num][
                    offset : offset + brick_a + 2 * border, offset : offset + brick_v + 2 * border
                ]
                plane = plane * fade_here
                centre = plane[1:-1, 1:-1]
                plane = centre + BLUR * (
                    plane[:-2, 1:-1] + plane[2:, 1:-1] + plane[1:-1, :-2] + plane[1:-1, 2:] - 4.0 * centre
                )
            out_ref[c] = plane

    return pl.pallas_call(
        kernel,
        out_shape=(
            jax.ShapeDtypeStruct(
                (colours, brick_a + 2 * border_out, brick_v + 2 * border_out), jnp.float32
            ),
            jax.ShapeDtypeStruct((colours, SLABS, brick_a, brick_v), jnp.float32),
        ),
        in_specs=[
            pl.BlockSpec(memory_space=pltpu.VMEM),
            pl.BlockSpec(memory_space=pltpu.VMEM),
        ],
        out_specs=(
            pl.BlockSpec(memory_space=pltpu.VMEM),
            pl.BlockSpec(memory_space=pltpu.VMEM),
        ),
    )(current, fade_rim)


def fade_rim_of(extinction_table, stack_rim, rows, mask, light_step):
    _, rim_a, rim_v = stack_rim.shape
    layer_rows = rows // SLABS
    colours, materials = extinction_table.shape
    chunk = 16 if rim_a % 16 == 0 else (8 if rim_a % 8 == 0 else rim_a)

    def kernel(table_ref, stack_ref, mask_ref, out_ref):
        def one_slab(slab_num, carry):
            for first in range(0, rim_a, chunk):
                part = slice(first, first + chunk)
                depth = [None] * colours
                for row in range(layer_rows):
                    row_num = slab_num * layer_rows + row
                    here = stack_ref[rows + row_num, part, :]
                    cells = stack_ref[row_num, part, :]
                    looked = [jnp.full(here.shape, table_ref[c, 0]) for c in range(colours)]
                    for material in range(1, materials):
                        match = here == float(material)
                        looked = [
                            jnp.where(match, table_ref[c, material], looked[c]) for c in range(colours)
                        ]
                    for c in range(colours):
                        term = looked[c] * cells
                        depth[c] = term if depth[c] is None else depth[c] + term
                for c in range(colours):
                    out_ref[c, slab_num, part, :] = (
                        jnp.exp(-light_step * depth[c]) * mask_ref[part, :]
                    )
            return carry

        lax.fori_loop(0, SLABS, one_slab, 0)

    return pl.pallas_call(
        kernel,
        out_shape=jax.ShapeDtypeStruct((colours, SLABS, rim_a, rim_v), jnp.float32),
        in_specs=[
            pl.BlockSpec(memory_space=pltpu.SMEM),
            pl.BlockSpec(memory_space=pltpu.VMEM),
            pl.BlockSpec(memory_space=pltpu.VMEM),
        ],
        out_specs=pl.BlockSpec(memory_space=pltpu.VMEM),
    )(extinction_table, stack_rim, mask)


def shards(density, labels, sunlight, opacity_table, extinction_table, albedo_table):
    brick_l, brick_a, brick_v = density.shape
    n_light = lax.axis_size("light")
    n_view = lax.axis_size("view")
    n_across = lax.axis_size("across")
    full_l = brick_l * n_light
    full_v = brick_v * n_view
    light_step = 10.0 / full_l
    view_step = 2.0 / full_v
    layer_rows = brick_l // SLABS
    light_idx = lax.axis_index("light")
    view_idx = lax.axis_index("view")
    across_idx = lax.axis_index("across")
    widest = SLABS * n_light
    stack = jnp.concatenate([density, labels.astype(jnp.float32), sunlight], axis=0)
    stack_rim = halo(halo(stack, "across", 1, widest), "view", 2, widest)
    density_rim = stack_rim[:brick_l]
    sun_rim = stack_rim[2 * brick_l :]
    density_side = density_rim[
        :, widest - 2 : widest + brick_a + 2, widest - 2 : widest + brick_v + 2
    ]
    table_all = jnp.concatenate([opacity_table[None], extinction_table, albedo_table], axis=0)
    looked = jnp.broadcast_to(table_all[:, 0, None, None, None], (7,) + labels.shape)
    for material in range(1, table_all.shape[1]):
        looked = jnp.where(
            (labels == material)[None], table_all[:, material, None, None, None], looked
        )
    extinct = looked[1:4] * density[None]
    extinct_slabs = extinct.reshape(3, SLABS, layer_rows, brick_a, brick_v)
    running = jnp.cumsum(extinct_slabs, axis=2) - extinct_slabs
    fade_rim = fade_rim_of(
        extinction_table, stack_rim, brick_l, plane_mask(widest, brick_a, brick_v), light_step
    )
    starts = None
    incoming = sun_rim
    for section_num in range(n_light):
        border = SLABS * (n_light - section_num)
        outgoing, starts = propagate(
            incoming, border, fade_rim, brick_a, brick_v
        )
        if section_num == 0:
            outgoing, density_side = lax.optimization_barrier((outgoing, density_side))
        if section_num + 1 < n_light:
            arrived = from_behind(outgoing, "light", 1)
            cut = widest - border + SLABS
            sun_here = sun_rim[:, cut : cut + brick_a + 2 * (border - SLABS), cut : cut + brick_v + 2 * (border - SLABS)]
            incoming = jnp.where(light_idx == 0, sun_here, arrived)
    padded = padded_2(density_side, (("light", 0),), 2)
    inside = (
        rim_mask(light_idx, n_light, brick_l, 1)[:, None, None]
        * rim_mask(across_idx, n_across, brick_a, 1)[None, :, None]
        * rim_mask(view_idx, n_view, brick_v, 1)[None, None, :]
    )
    shading = shade_from(padded, inside)
    lighting = (starts[:, :, None] * jnp.exp(-light_step * running)).reshape(
        3, brick_l, brick_a, brick_v
    )
    optical = looked[0] * density * view_step
    colour = (1.0 - jnp.exp(-optical))[None] * looked[4:7] * (shading[None] * lighting + AMBIENT)
    upper = (jnp.arange(brick_v)[:, None] < jnp.arange(brick_v)[None, :]).astype(jnp.float32)
    before = jnp.dot(optical.reshape(-1, brick_v), upper, precision=lax.Precision.HIGHEST).reshape(
        brick_l, brick_a, brick_v
    )
    colour_sum = jnp.sum(colour * jnp.exp(-before)[None], axis=-1)
    transmit = jnp.exp(-jnp.sum(optical, axis=-1))
    pixels = brick_l * brick_a
    piece_len = pixels // n_view
    image_now = jnp.concatenate(
        [colour_sum.reshape(3, n_view, piece_len), transmit.reshape(1, n_view, piece_len)], axis=0
    )
    bit_count = n_view.bit_length() - 1
    for bit_num in range(bit_count):
        kept = image_now.shape[1]
        pairs = image_now.reshape(4, kept // 2, 2, piece_len)
        my_bit = view_idx // 2**bit_num % 2
        first_half = my_bit == 0
        keep = jnp.where(first_half, pairs[:, :, 0], pairs[:, :, 1])
        send = jnp.where(first_half, pairs[:, :, 1], pairs[:, :, 0])
        got = from_partner(send, "view", bit_num)
        front = jnp.where(first_half, keep, got)
        back = jnp.where(first_half, got, keep)
        image_now = jnp.concatenate(
            [front[:3] + front[3:] * back[:3], keep[3:] * got[3:]], axis=0
        )
    final_colour = image_now[:3, 0]
    final_transmit = image_now[3:, 0]
    rows_out = brick_l // n_view
    opacity = 1.0 - final_transmit.reshape(1, rows_out, brick_a)
    return jnp.concatenate([final_colour.reshape(3, rows_out, brick_a), opacity], axis=0)


def solution(mesh):
    in_specs = (
        P("light", "across", "view"),
        P("light", "across", "view"),
        P(None, "across", "view"),
        P(),
        P(),
        P(),
    )
    out_specs = P(None, ("light", "view"), "across")
    return jax.shard_map(shards, mesh=mesh, in_specs=in_specs, out_specs=out_specs, check_vma=False)
```

```python
import jax
import jax.numpy as jnp
from jax import lax
from jax.experimental import pallas as pl
from jax.experimental.pallas import tpu as pltpu
from jax.sharding import PartitionSpec as P

SLABS = 8


BLUR = 0.24
AMBIENT = 0.1
SOFTEN = 0.05


def padded_2(block, sides, width):
    for axis, dim in sides:
        count = lax.axis_size(axis)
        forward = [(i, i + 1) for i in range(count - 1)]
        backward = [(target, source) for source, target in forward]
        low = lax.ppermute(
            lax.slice_in_dim(block, block.shape[dim] - width, None, axis=dim), axis, forward
        )
        high = lax.ppermute(lax.slice_in_dim(block, 0, width, axis=dim), axis, backward)
        block = jnp.concatenate([low, block, high], axis=dim)
    return block


def from_behind(value, axis, steps):
    count = lax.axis_size(axis)
    leading, last = (max(0, -steps), min(count, count - steps))
    return lax.ppermute(value, axis, [(source, source + steps) for source in range(leading, last)])


def from_partner(block, axis, apart):
    count = lax.axis_size(axis)
    route = []
    for low in range(count):
        high = low | 1 << apart
        if high != low and high < count:
            route += [(low, high), (high, low)]
    return lax.ppermute(block, axis, route)


def smooth(field):
    centre = field[1:-1, 1:-1, 1:-1]
    return (
        2.0 * centre
        + field[2:, 1:-1, 1:-1]
        + field[:-2, 1:-1, 1:-1]
        + field[1:-1, 2:, 1:-1]
        + field[1:-1, :-2, 1:-1]
        + field[1:-1, 1:-1, 2:]
        + field[1:-1, 1:-1, :-2]
    ) * 0.125


def shade_from(window, inside):
    slope_light = (window[2:, 1:-1, 1:-1] - window[:-2, 1:-1, 1:-1]) * 0.5
    slope_across = (window[1:-1, 2:, 1:-1] - window[1:-1, :-2, 1:-1]) * 0.5
    slope_view = (window[1:-1, 1:-1, 2:] - window[1:-1, 1:-1, :-2]) * 0.5
    along = 0.8 * slope_light + 0.36 * slope_across + 0.48 * slope_view
    aligned = along * along * inside
    trace = (slope_light * slope_light + slope_across * slope_across + slope_view * slope_view) * inside
    return 0.25 + smooth(aligned) / (smooth(trace) + SOFTEN)


def rim_mask(position, devices, width, border):
    places = position * width - border + jnp.arange(width + 2 * border, dtype=jnp.int32)
    return ((places >= 0) & (places < devices * width)).astype(jnp.float32)


def halo(block, axis, dim, width):
    count = lax.axis_size(axis)
    size = block.shape[dim]
    lows, highs = [], []
    if count == 2:
        need = min(size, width)
        first = lax.axis_index(axis) == 0
        send = block
        if need < size:
            send = jnp.where(
                first,
                lax.slice_in_dim(block, size - need, None, axis=dim),
                lax.slice_in_dim(block, 0, need, axis=dim),
            )
        got = lax.ppermute(send, axis, [(0, 1), (1, 0)])
        lows = [jnp.where(first, jnp.zeros_like(got), got)]
        highs = [jnp.where(first, got, jnp.zeros_like(got))]
        count = 0
    for hop in range(1, count):
        need = min(size, width - (hop - 1) * size)
        if need <= 0:
            break
        forward = [(i, i + hop) for i in range(count - hop)]
        backward = [(target, source) for source, target in forward]
        low = lax.slice_in_dim(block, size - need, None, axis=dim)
        lows.insert(0, lax.ppermute(low, axis, forward))
        highs.append(lax.ppermute(lax.slice_in_dim(block, 0, need, axis=dim), axis, backward))
    block = jnp.concatenate(lows + [block] + highs, axis=dim)
    missing = width - sum(part.shape[dim] for part in lows)
    if missing > 0:
        widths = [(0, 0)] * block.ndim
        widths[dim] = (missing, missing)
        block = jnp.pad(block, widths)
    return block


def plane_mask(border, brick_a, brick_v):
    return (
        rim_mask(lax.axis_index("across"), lax.axis_size("across"), brick_a, border)[:, None]
        * rim_mask(lax.axis_index("view"), lax.axis_size("view"), brick_v, border)[None, :]
    )


def halo_plane(stack, width):
    planes, size_a, size_v = stack.shape
    n_view = lax.axis_size("view")
    first = lax.axis_index("across") == 0

    def for_partner(block):
        if width >= size_a:
            return block
        return jnp.where(first, block[:, size_a - width :], block[:, :width])

    swap = [(0, 1), (1, 0)]
    forward = [(v, v + 1) for v in range(n_view - 1)]
    backward = [(target, source) for source, target in forward]
    diagonal_forward = [(v * 2 + a, (v + 1) * 2 + 1 - a) for a in range(2) for v in range(n_view - 1)]
    diagonal_backward = [(target, source) for source, target in diagonal_forward]
    left = stack[:, :, size_v - width :]
    right = stack[:, :, :width]
    centre_other = lax.ppermute(for_partner(stack), "across", swap)
    left_own = lax.ppermute(left, "view", forward)
    right_own = lax.ppermute(right, "view", backward)
    left_other = lax.ppermute(for_partner(left), ("view", "across"), diagonal_forward)
    right_other = lax.ppermute(for_partner(right), ("view", "across"), diagonal_backward)

    def column(own, other):
        empty = jnp.zeros_like(other)
        return jnp.concatenate(
            [jnp.where(first, empty, other), own, jnp.where(first, other, empty)], axis=1
        )

    return jnp.concatenate(
        [column(left_own, left_other), column(stack, centre_other), column(right_own, right_other)],
        axis=2,
    )


def propagate(current, border_in, fade_rim, brick_a, brick_v):
    widest = (fade_rim.shape[2] - brick_a) // 2
    starts = []
    for slab_num in range(SLABS):
        border = border_in - slab_num
        starts.append(current[:, border : border + brick_a, border : border + brick_v])
        offset = widest - border
        fade_here = fade_rim[
            :,
            slab_num,
            offset : offset + brick_a + 2 * border,
            offset : offset + brick_v + 2 * border,
        ]
        current = current * fade_here
        centre = current[:, 1:-1, 1:-1]
        current = centre + BLUR * (
            current[:, :-2, 1:-1]
            + current[:, 2:, 1:-1]
            + current[:, 1:-1, :-2]
            + current[:, 1:-1, 2:]
            - 4.0 * centre
        )
    return (current, jnp.stack(starts, axis=1))


def fade_rim_of(extinction_table, stack_rim, rows, mask, light_step):
    _, rim_a, rim_v = stack_rim.shape
    layer_rows = rows // SLABS
    colours, materials = extinction_table.shape
    chunk = 16 if rim_a % 16 == 0 else (8 if rim_a % 8 == 0 else rim_a)

    def kernel(table_ref, stack_ref, mask_ref, out_ref):
        def one_slab(slab_num, carry):
            for first in range(0, rim_a, chunk):
                part = slice(first, first + chunk)
                depth = [None] * colours
                for row in range(layer_rows):
                    row_num = slab_num * layer_rows + row
                    here = stack_ref[rows + row_num, part, :]
                    cells = stack_ref[row_num, part, :]
                    looked = [jnp.full(here.shape, table_ref[c, 0]) for c in range(colours)]
                    for material in range(1, materials):
                        match = here == float(material)
                        looked = [
                            jnp.where(match, table_ref[c, material], looked[c]) for c in range(colours)
                        ]
                    for c in range(colours):
                        term = looked[c] * cells
                        depth[c] = term if depth[c] is None else depth[c] + term
                for c in range(colours):
                    out_ref[c, slab_num, part, :] = (
                        jnp.exp(-light_step * depth[c]) * mask_ref[part, :]
                    )
            return carry

        lax.fori_loop(0, SLABS, one_slab, 0)

    return pl.pallas_call(
        kernel,
        out_shape=jax.ShapeDtypeStruct((colours, SLABS, rim_a, rim_v), jnp.float32),
        in_specs=[
            pl.BlockSpec(memory_space=pltpu.SMEM),
            pl.BlockSpec(memory_space=pltpu.VMEM),
            pl.BlockSpec(memory_space=pltpu.VMEM),
        ],
        out_specs=pl.BlockSpec(memory_space=pltpu.VMEM),
    )(extinction_table, stack_rim, mask)


def shards(density, labels, sunlight, opacity_table, extinction_table, albedo_table):
    brick_l, brick_a, brick_v = density.shape
    n_light = lax.axis_size("light")
    n_view = lax.axis_size("view")
    n_across = lax.axis_size("across")
    full_l = brick_l * n_light
    full_v = brick_v * n_view
    light_step = 10.0 / full_l
    view_step = 2.0 / full_v
    layer_rows = brick_l // SLABS
    light_idx = lax.axis_index("light")
    view_idx = lax.axis_index("view")
    across_idx = lax.axis_index("across")
    widest = SLABS * n_light
    stack = jnp.concatenate([density, labels.astype(jnp.float32), sunlight], axis=0)
    if n_across == 2 and widest <= brick_a and widest <= brick_v:
        stack_rim = halo_plane(stack, widest)
    else:
        stack_rim = halo(halo(stack, "across", 1, widest), "view", 2, widest)
    density_rim = stack_rim[:brick_l]
    sun_rim = stack_rim[2 * brick_l :]
    density_side = density_rim[
        :, widest - 2 : widest + brick_a + 2, widest - 2 : widest + brick_v + 2
    ]
    table_all = jnp.concatenate([opacity_table[None], extinction_table, albedo_table], axis=0)
    looked = jnp.broadcast_to(table_all[:, 0, None, None, None], (7,) + labels.shape)
    for material in range(1, table_all.shape[1]):
        looked = jnp.where(
            (labels == material)[None], table_all[:, material, None, None, None], looked
        )
    extinct = looked[1:4] * density[None]
    extinct_slabs = extinct.reshape(3, SLABS, layer_rows, brick_a, brick_v)
    running = jnp.cumsum(extinct_slabs, axis=2) - extinct_slabs
    fade_rim = fade_rim_of(
        extinction_table, stack_rim, brick_l, plane_mask(widest, brick_a, brick_v), light_step
    )
    starts = None
    incoming = sun_rim
    for section_num in range(n_light):
        border = SLABS * (n_light - section_num)
        outgoing, starts = propagate(
            incoming, border, fade_rim, brick_a, brick_v
        )
        if section_num == 0:
            outgoing, density_side = lax.optimization_barrier((outgoing, density_side))
        if section_num + 1 < n_light:
            arrived = from_behind(outgoing, "light", 1)
            cut = widest - border + SLABS
            sun_here = sun_rim[:, cut : cut + brick_a + 2 * (border - SLABS), cut : cut + brick_v + 2 * (border - SLABS)]
            incoming = jnp.where(light_idx == 0, sun_here, arrived)
    padded = padded_2(density_side, (("light", 0),), 2)
    inside = (
        rim_mask(light_idx, n_light, brick_l, 1)[:, None, None]
        * rim_mask(across_idx, n_across, brick_a, 1)[None, :, None]
        * rim_mask(view_idx, n_view, brick_v, 1)[None, None, :]
    )
    shading = shade_from(padded, inside)
    lighting = (starts[:, :, None] * jnp.exp(-light_step * running)).reshape(
        3, brick_l, brick_a, brick_v
    )
    optical = looked[0] * density * view_step
    colour = (1.0 - jnp.exp(-optical))[None] * looked[4:7] * (shading[None] * lighting + AMBIENT)
    upper = (jnp.arange(brick_v)[:, None] < jnp.arange(brick_v)[None, :]).astype(jnp.float32)
    before = jnp.dot(optical.reshape(-1, brick_v), upper, precision=lax.Precision.HIGHEST).reshape(
        brick_l, brick_a, brick_v
    )
    colour_sum = jnp.sum(colour * jnp.exp(-before)[None], axis=-1)
    transmit = jnp.exp(-jnp.sum(optical, axis=-1))
    pixels = brick_l * brick_a
    piece_len = pixels // n_view
    image_now = jnp.concatenate(
        [colour_sum.reshape(3, n_view, piece_len), transmit.reshape(1, n_view, piece_len)], axis=0
    )
    bit_count = n_view.bit_length() - 1
    for bit_num in range(bit_count):
        kept = image_now.shape[1]
        pairs = image_now.reshape(4, kept // 2, 2, piece_len)
        my_bit = view_idx // 2**bit_num % 2
        first_half = my_bit == 0
        keep = jnp.where(first_half, pairs[:, :, 0], pairs[:, :, 1])
        send = jnp.where(first_half, pairs[:, :, 1], pairs[:, :, 0])
        got = from_partner(send, "view", bit_num)
        front = jnp.where(first_half, keep, got)
        back = jnp.where(first_half, got, keep)
        image_now = jnp.concatenate(
            [front[:3] + front[3:] * back[:3], keep[3:] * got[3:]], axis=0
        )
    final_colour = image_now[:3, 0]
    final_transmit = image_now[3:, 0]
    rows_out = brick_l // n_view
    opacity = 1.0 - final_transmit.reshape(1, rows_out, brick_a)
    return jnp.concatenate([final_colour.reshape(3, rows_out, brick_a), opacity], axis=0)


def solution(mesh):
    in_specs = (
        P("light", "across", "view"),
        P("light", "across", "view"),
        P(None, "across", "view"),
        P(),
        P(),
        P(),
    )
    out_specs = P(None, ("light", "view"), "across")
    return jax.shard_map(shards, mesh=mesh, in_specs=in_specs, out_specs=out_specs, check_vma=False)
```

```python
import jax
import jax.numpy as jnp
from jax import lax
from jax.experimental import pallas as pl
from jax.experimental.pallas import tpu as pltpu
from jax.sharding import PartitionSpec as P

SLABS = 8


BLUR = 0.24
AMBIENT = 0.1
SOFTEN = 0.05


def padded_2(block, sides, width):
    for axis, dim in sides:
        count = lax.axis_size(axis)
        forward = [(i, i + 1) for i in range(count - 1)]
        backward = [(target, source) for source, target in forward]
        low = lax.ppermute(
            lax.slice_in_dim(block, block.shape[dim] - width, None, axis=dim), axis, forward
        )
        high = lax.ppermute(lax.slice_in_dim(block, 0, width, axis=dim), axis, backward)
        block = jnp.concatenate([low, block, high], axis=dim)
    return block


def from_behind(value, axis, steps):
    count = lax.axis_size(axis)
    leading, last = (max(0, -steps), min(count, count - steps))
    return lax.ppermute(value, axis, [(source, source + steps) for source in range(leading, last)])


def from_partner(block, axis, apart):
    count = lax.axis_size(axis)
    route = []
    for low in range(count):
        high = low | 1 << apart
        if high != low and high < count:
            route += [(low, high), (high, low)]
    return lax.ppermute(block, axis, route)


def smooth(field):
    centre = field[1:-1, 1:-1, 1:-1]
    return (
        2.0 * centre
        + field[2:, 1:-1, 1:-1]
        + field[:-2, 1:-1, 1:-1]
        + field[1:-1, 2:, 1:-1]
        + field[1:-1, :-2, 1:-1]
        + field[1:-1, 1:-1, 2:]
        + field[1:-1, 1:-1, :-2]
    ) * 0.125


def shade_from(window, inside):
    slope_light = (window[2:, 1:-1, 1:-1] - window[:-2, 1:-1, 1:-1]) * 0.5
    slope_across = (window[1:-1, 2:, 1:-1] - window[1:-1, :-2, 1:-1]) * 0.5
    slope_view = (window[1:-1, 1:-1, 2:] - window[1:-1, 1:-1, :-2]) * 0.5
    along = 0.8 * slope_light + 0.36 * slope_across + 0.48 * slope_view
    aligned = along * along * inside
    trace = (slope_light * slope_light + slope_across * slope_across + slope_view * slope_view) * inside
    return 0.25 + smooth(aligned) / (smooth(trace) + SOFTEN)


def rim_mask(position, devices, width, border):
    places = position * width - border + jnp.arange(width + 2 * border, dtype=jnp.int32)
    return ((places >= 0) & (places < devices * width)).astype(jnp.float32)


def halo(block, axis, dim, width):
    count = lax.axis_size(axis)
    size = block.shape[dim]
    lows, highs = [], []
    if count == 2:
        need = min(size, width)
        first = lax.axis_index(axis) == 0
        send = block
        if need < size:
            send = jnp.where(
                first,
                lax.slice_in_dim(block, size - need, None, axis=dim),
                lax.slice_in_dim(block, 0, need, axis=dim),
            )
        got = lax.ppermute(send, axis, [(0, 1), (1, 0)])
        lows = [jnp.where(first, jnp.zeros_like(got), got)]
        highs = [jnp.where(first, got, jnp.zeros_like(got))]
        count = 0
    for hop in range(1, count):
        need = min(size, width - (hop - 1) * size)
        if need <= 0:
            break
        forward = [(i, i + hop) for i in range(count - hop)]
        backward = [(target, source) for source, target in forward]
        low = lax.slice_in_dim(block, size - need, None, axis=dim)
        lows.insert(0, lax.ppermute(low, axis, forward))
        highs.append(lax.ppermute(lax.slice_in_dim(block, 0, need, axis=dim), axis, backward))
    block = jnp.concatenate(lows + [block] + highs, axis=dim)
    missing = width - sum(part.shape[dim] for part in lows)
    if missing > 0:
        widths = [(0, 0)] * block.ndim
        widths[dim] = (missing, missing)
        block = jnp.pad(block, widths)
    return block


def plane_mask(border, brick_a, brick_v):
    return (
        rim_mask(lax.axis_index("across"), lax.axis_size("across"), brick_a, border)[:, None]
        * rim_mask(lax.axis_index("view"), lax.axis_size("view"), brick_v, border)[None, :]
    )


def propagate(current, border_in, fade_rim, brick_a, brick_v):
    widest = (fade_rim.shape[2] - brick_a) // 2
    starts = []
    for slab_num in range(SLABS):
        border = border_in - slab_num
        starts.append(current[:, border : border + brick_a, border : border + brick_v])
        offset = widest - border
        fade_here = fade_rim[
            :,
            slab_num,
            offset : offset + brick_a + 2 * border,
            offset : offset + brick_v + 2 * border,
        ]
        current = current * fade_here
        centre = current[:, 1:-1, 1:-1]
        current = centre + BLUR * (
            current[:, :-2, 1:-1]
            + current[:, 2:, 1:-1]
            + current[:, 1:-1, :-2]
            + current[:, 1:-1, 2:]
            - 4.0 * centre
        )
    return (current, jnp.stack(starts, axis=1))


def fade_rim_of(extinction_table, stack_rim, rows, mask, light_step):
    _, rim_a, rim_v = stack_rim.shape
    layer_rows = rows // SLABS
    colours, materials = extinction_table.shape
    chunk = 16 if rim_a % 16 == 0 else (8 if rim_a % 8 == 0 else rim_a)

    def kernel(table_ref, stack_ref, mask_ref, out_ref):
        def one_slab(slab_num, carry):
            for first in range(0, rim_a, chunk):
                part = slice(first, first + chunk)
                depth = [None] * colours
                for row in range(layer_rows):
                    row_num = slab_num * layer_rows + row
                    here = stack_ref[rows + row_num, part, :]
                    cells = stack_ref[row_num, part, :]
                    looked = [jnp.full(here.shape, table_ref[c, 0]) for c in range(colours)]
                    for material in range(1, materials):
                        match = here == float(material)
                        looked = [
                            jnp.where(match, table_ref[c, material], looked[c]) for c in range(colours)
                        ]
                    for c in range(colours):
                        term = looked[c] * cells
                        depth[c] = term if depth[c] is None else depth[c] + term
                for c in range(colours):
                    out_ref[c, slab_num, part, :] = (
                        jnp.exp(-light_step * depth[c]) * mask_ref[part, :]
                    )
            return carry

        lax.fori_loop(0, SLABS, one_slab, 0)

    return pl.pallas_call(
        kernel,
        out_shape=jax.ShapeDtypeStruct((colours, SLABS, rim_a, rim_v), jnp.float32),
        in_specs=[
            pl.BlockSpec(memory_space=pltpu.SMEM),
            pl.BlockSpec(memory_space=pltpu.VMEM),
            pl.BlockSpec(memory_space=pltpu.VMEM),
        ],
        out_specs=pl.BlockSpec(memory_space=pltpu.VMEM),
    )(extinction_table, stack_rim, mask)


def shards(density, labels, sunlight, opacity_table, extinction_table, albedo_table):
    brick_l, brick_a, brick_v = density.shape
    n_light = lax.axis_size("light")
    n_view = lax.axis_size("view")
    n_across = lax.axis_size("across")
    full_l = brick_l * n_light
    full_v = brick_v * n_view
    light_step = 10.0 / full_l
    view_step = 2.0 / full_v
    layer_rows = brick_l // SLABS
    light_idx = lax.axis_index("light")
    view_idx = lax.axis_index("view")
    across_idx = lax.axis_index("across")
    widest = SLABS * n_light
    stack = jnp.concatenate([density, labels.astype(jnp.float32), sunlight], axis=0)
    stack_rim = halo(halo(stack, "across", 1, widest), "view", 2, widest)
    density_rim = stack_rim[:brick_l]
    sun_rim = stack_rim[2 * brick_l :]
    density_side = density_rim[
        :, widest - 2 : widest + brick_a + 2, widest - 2 : widest + brick_v + 2
    ]
    table_all = jnp.concatenate([opacity_table[None], extinction_table, albedo_table], axis=0)
    looked = jnp.broadcast_to(table_all[:, 0, None, None, None], (7,) + labels.shape)
    for material in range(1, table_all.shape[1]):
        looked = jnp.where(
            (labels == material)[None], table_all[:, material, None, None, None], looked
        )
    extinct = looked[1:4] * density[None]
    extinct_slabs = extinct.reshape(3, SLABS, layer_rows, brick_a, brick_v)
    running = jnp.cumsum(extinct_slabs, axis=2) - extinct_slabs
    fade_rim = fade_rim_of(
        extinction_table, stack_rim, brick_l, plane_mask(widest, brick_a, brick_v), light_step
    )
    starts = None
    incoming = sun_rim
    for section_num in range(n_light):
        border = SLABS * (n_light - section_num)
        outgoing, section_starts = propagate(
            incoming, border, fade_rim, brick_a, brick_v
        )
        if starts is None:
            starts = section_starts
        else:
            starts = jnp.where(light_idx == section_num, section_starts, starts)
        if section_num == 0:
            outgoing, density_side = lax.optimization_barrier((outgoing, density_side))
        if section_num + 1 < n_light:
            incoming = lax.ppermute(outgoing, "light", [(section_num, section_num + 1)])
    padded = padded_2(density_side, (("light", 0),), 2)
    inside = (
        rim_mask(light_idx, n_light, brick_l, 1)[:, None, None]
        * rim_mask(across_idx, n_across, brick_a, 1)[None, :, None]
        * rim_mask(view_idx, n_view, brick_v, 1)[None, None, :]
    )
    shading = shade_from(padded, inside)
    lighting = (starts[:, :, None] * jnp.exp(-light_step * running)).reshape(
        3, brick_l, brick_a, brick_v
    )
    optical = looked[0] * density * view_step
    colour = (1.0 - jnp.exp(-optical))[None] * looked[4:7] * (shading[None] * lighting + AMBIENT)
    upper = (jnp.arange(brick_v)[:, None] < jnp.arange(brick_v)[None, :]).astype(jnp.float32)
    before = jnp.dot(optical.reshape(-1, brick_v), upper, precision=lax.Precision.HIGHEST).reshape(
        brick_l, brick_a, brick_v
    )
    colour_sum = jnp.sum(colour * jnp.exp(-before)[None], axis=-1)
    transmit = jnp.exp(-jnp.sum(optical, axis=-1))
    pixels = brick_l * brick_a
    piece_len = pixels // n_view
    image_now = jnp.concatenate(
        [colour_sum.reshape(3, n_view, piece_len), transmit.reshape(1, n_view, piece_len)], axis=0
    )
    bit_count = n_view.bit_length() - 1
    for bit_num in range(bit_count):
        kept = image_now.shape[1]
        pairs = image_now.reshape(4, kept // 2, 2, piece_len)
        my_bit = view_idx // 2**bit_num % 2
        first_half = my_bit == 0
        keep = jnp.where(first_half, pairs[:, :, 0], pairs[:, :, 1])
        send = jnp.where(first_half, pairs[:, :, 1], pairs[:, :, 0])
        got = from_partner(send, "view", bit_num)
        front = jnp.where(first_half, keep, got)
        back = jnp.where(first_half, got, keep)
        image_now = jnp.concatenate(
            [front[:3] + front[3:] * back[:3], keep[3:] * got[3:]], axis=0
        )
    final_colour = image_now[:3, 0]
    final_transmit = image_now[3:, 0]
    rows_out = brick_l // n_view
    opacity = 1.0 - final_transmit.reshape(1, rows_out, brick_a)
    return jnp.concatenate([final_colour.reshape(3, rows_out, brick_a), opacity], axis=0)


def solution(mesh):
    in_specs = (
        P("light", "across", "view"),
        P("light", "across", "view"),
        P(None, "across", "view"),
        P(),
        P(),
        P(),
    )
    out_specs = P(None, ("light", "view"), "across")
    return jax.shard_map(shards, mesh=mesh, in_specs=in_specs, out_specs=out_specs, check_vma=False)
```

```python
import jax
import jax.numpy as jnp
from jax import lax
from jax.experimental import pallas as pl
from jax.experimental.pallas import tpu as pltpu
from jax.sharding import PartitionSpec as P

SLABS = 8


BLUR = 0.24
AMBIENT = 0.1
SOFTEN = 0.05


def padded_2(block, sides, width):
    for axis, dim in sides:
        count = lax.axis_size(axis)
        forward = [(i, i + 1) for i in range(count - 1)]
        backward = [(target, source) for source, target in forward]
        low = lax.ppermute(
            lax.slice_in_dim(block, block.shape[dim] - width, None, axis=dim), axis, forward
        )
        high = lax.ppermute(lax.slice_in_dim(block, 0, width, axis=dim), axis, backward)
        block = jnp.concatenate([low, block, high], axis=dim)
    return block


def from_behind(value, axis, steps):
    count = lax.axis_size(axis)
    leading, last = (max(0, -steps), min(count, count - steps))
    return lax.ppermute(value, axis, [(source, source + steps) for source in range(leading, last)])


def from_partner(block, axis, apart):
    count = lax.axis_size(axis)
    route = []
    for low in range(count):
        high = low | 1 << apart
        if high != low and high < count:
            route += [(low, high), (high, low)]
    return lax.ppermute(block, axis, route)


def smooth(field):
    centre = field[1:-1, 1:-1, 1:-1]
    return (
        2.0 * centre
        + field[2:, 1:-1, 1:-1]
        + field[:-2, 1:-1, 1:-1]
        + field[1:-1, 2:, 1:-1]
        + field[1:-1, :-2, 1:-1]
        + field[1:-1, 1:-1, 2:]
        + field[1:-1, 1:-1, :-2]
    ) * 0.125


def shade_from(window, inside):
    slope_light = (window[2:, 1:-1, 1:-1] - window[:-2, 1:-1, 1:-1]) * 0.5
    slope_across = (window[1:-1, 2:, 1:-1] - window[1:-1, :-2, 1:-1]) * 0.5
    slope_view = (window[1:-1, 1:-1, 2:] - window[1:-1, 1:-1, :-2]) * 0.5
    along = 0.8 * slope_light + 0.36 * slope_across + 0.48 * slope_view
    aligned = along * along * inside
    trace = (slope_light * slope_light + slope_across * slope_across + slope_view * slope_view) * inside
    return 0.25 + smooth(aligned) / (smooth(trace) + SOFTEN)


def rim_mask(position, devices, width, border):
    places = position * width - border + jnp.arange(width + 2 * border, dtype=jnp.int32)
    return ((places >= 0) & (places < devices * width)).astype(jnp.float32)


def halo(block, axis, dim, width):
    count = lax.axis_size(axis)
    size = block.shape[dim]
    lows, highs = [], []
    if count == 2:
        need = min(size, width)
        first = lax.axis_index(axis) == 0
        send = block
        if need < size:
            send = jnp.where(
                first,
                lax.slice_in_dim(block, size - need, None, axis=dim),
                lax.slice_in_dim(block, 0, need, axis=dim),
            )
        got = lax.ppermute(send, axis, [(0, 1), (1, 0)])
        lows = [jnp.where(first, jnp.zeros_like(got), got)]
        highs = [jnp.where(first, got, jnp.zeros_like(got))]
        count = 0
    for hop in range(1, count):
        need = min(size, width - (hop - 1) * size)
        if need <= 0:
            break
        forward = [(i, i + hop) for i in range(count - hop)]
        backward = [(target, source) for source, target in forward]
        low = lax.slice_in_dim(block, size - need, None, axis=dim)
        lows.insert(0, lax.ppermute(low, axis, forward))
        highs.append(lax.ppermute(lax.slice_in_dim(block, 0, need, axis=dim), axis, backward))
    block = jnp.concatenate(lows + [block] + highs, axis=dim)
    missing = width - sum(part.shape[dim] for part in lows)
    if missing > 0:
        widths = [(0, 0)] * block.ndim
        widths[dim] = (missing, missing)
        block = jnp.pad(block, widths)
    return block


def plane_mask(border, brick_a, brick_v):
    return (
        rim_mask(lax.axis_index("across"), lax.axis_size("across"), brick_a, border)[:, None]
        * rim_mask(lax.axis_index("view"), lax.axis_size("view"), brick_v, border)[None, :]
    )


def propagate(current, border_in, fade_rim, brick_a, brick_v):
    widest = (fade_rim.shape[2] - brick_a) // 2
    starts = []
    for slab_num in range(SLABS):
        border = border_in - slab_num
        starts.append(current[:, border : border + brick_a, border : border + brick_v])
        offset = widest - border
        fade_here = fade_rim[
            :,
            slab_num,
            offset : offset + brick_a + 2 * border,
            offset : offset + brick_v + 2 * border,
        ]
        current = current * fade_here
        centre = current[:, 1:-1, 1:-1]
        current = centre + BLUR * (
            current[:, :-2, 1:-1]
            + current[:, 2:, 1:-1]
            + current[:, 1:-1, :-2]
            + current[:, 1:-1, 2:]
            - 4.0 * centre
        )
    return (current, jnp.stack(starts, axis=1))


def fade_rim_of(extinction_table, stack_rim, rows, mask, light_step):
    _, rim_a, rim_v = stack_rim.shape
    layer_rows = rows // SLABS
    colours, materials = extinction_table.shape
    chunk = 16 if rim_a % 16 == 0 else (8 if rim_a % 8 == 0 else rim_a)

    def kernel(table_ref, stack_ref, mask_ref, out_ref):
        def one_slab(slab_num, carry):
            for first in range(0, rim_a, chunk):
                part = slice(first, first + chunk)
                depth = [None] * colours
                for row in range(layer_rows):
                    row_num = slab_num * layer_rows + row
                    here = stack_ref[rows + row_num, part, :]
                    cells = stack_ref[row_num, part, :]
                    looked = [jnp.full(here.shape, table_ref[c, 0]) for c in range(colours)]
                    for material in range(1, materials):
                        match = here == float(material)
                        looked = [
                            jnp.where(match, table_ref[c, material], looked[c]) for c in range(colours)
                        ]
                    for c in range(colours):
                        term = looked[c] * cells
                        depth[c] = term if depth[c] is None else depth[c] + term
                for c in range(colours):
                    out_ref[c, slab_num, part, :] = (
                        jnp.exp(-light_step * depth[c]) * mask_ref[part, :]
                    )
            return carry

        lax.fori_loop(0, SLABS, one_slab, 0)

    return pl.pallas_call(
        kernel,
        out_shape=jax.ShapeDtypeStruct((colours, SLABS, rim_a, rim_v), jnp.float32),
        in_specs=[
            pl.BlockSpec(memory_space=pltpu.SMEM),
            pl.BlockSpec(memory_space=pltpu.VMEM),
            pl.BlockSpec(memory_space=pltpu.VMEM),
        ],
        out_specs=pl.BlockSpec(memory_space=pltpu.VMEM),
    )(extinction_table, stack_rim, mask)


def shards(density, labels, sunlight, opacity_table, extinction_table, albedo_table):
    brick_l, brick_a, brick_v = density.shape
    n_light = lax.axis_size("light")
    n_view = lax.axis_size("view")
    n_across = lax.axis_size("across")
    full_l = brick_l * n_light
    full_v = brick_v * n_view
    light_step = 10.0 / full_l
    view_step = 2.0 / full_v
    layer_rows = brick_l // SLABS
    light_idx = lax.axis_index("light")
    view_idx = lax.axis_index("view")
    across_idx = lax.axis_index("across")
    widest = SLABS * n_light
    stack = jnp.concatenate([density, labels.astype(jnp.float32), sunlight], axis=0)
    stack_rim = halo(halo(stack, "across", 1, widest), "view", 2, widest)
    density_rim = stack_rim[:brick_l]
    sun_rim = stack_rim[2 * brick_l :]
    density_side = density_rim[
        :, widest - 2 : widest + brick_a + 2, widest - 2 : widest + brick_v + 2
    ]
    table_all = jnp.concatenate([opacity_table[None], extinction_table, albedo_table], axis=0)
    looked = jnp.broadcast_to(table_all[:, 0, None, None, None], (7,) + labels.shape)
    for material in range(1, table_all.shape[1]):
        looked = jnp.where(
            (labels == material)[None], table_all[:, material, None, None, None], looked
        )
    extinct = looked[1:4] * density[None]
    extinct_slabs = extinct.reshape(3, SLABS, layer_rows, brick_a, brick_v)
    running = jnp.cumsum(extinct_slabs, axis=2) - extinct_slabs
    fade_rim = fade_rim_of(
        extinction_table, stack_rim, brick_l, plane_mask(widest, brick_a, brick_v), light_step
    )
    starts = None
    incoming = sun_rim
    for section_num in range(n_light):
        border = SLABS * (n_light - section_num)
        outgoing, section_starts = propagate(
            incoming, border, fade_rim, brick_a, brick_v
        )
        if starts is None:
            starts = section_starts
        else:
            starts = jnp.where(light_idx == section_num, section_starts, starts)
        if section_num == max(0, n_light - 2):
            outgoing, density_side = lax.optimization_barrier((outgoing, density_side))
        if section_num + 1 < n_light:
            incoming = lax.ppermute(outgoing, "light", [(section_num, section_num + 1)])
    padded = padded_2(density_side, (("light", 0),), 2)
    inside = (
        rim_mask(light_idx, n_light, brick_l, 1)[:, None, None]
        * rim_mask(across_idx, n_across, brick_a, 1)[None, :, None]
        * rim_mask(view_idx, n_view, brick_v, 1)[None, None, :]
    )
    shading = shade_from(padded, inside)
    lighting = (starts[:, :, None] * jnp.exp(-light_step * running)).reshape(
        3, brick_l, brick_a, brick_v
    )
    optical = looked[0] * density * view_step
    colour = (1.0 - jnp.exp(-optical))[None] * looked[4:7] * (shading[None] * lighting + AMBIENT)
    upper = (jnp.arange(brick_v)[:, None] < jnp.arange(brick_v)[None, :]).astype(jnp.float32)
    before = jnp.dot(optical.reshape(-1, brick_v), upper, precision=lax.Precision.HIGHEST).reshape(
        brick_l, brick_a, brick_v
    )
    colour_sum = jnp.sum(colour * jnp.exp(-before)[None], axis=-1)
    transmit = jnp.exp(-jnp.sum(optical, axis=-1))
    pixels = brick_l * brick_a
    piece_len = pixels // n_view
    image_now = jnp.concatenate(
        [colour_sum.reshape(3, n_view, piece_len), transmit.reshape(1, n_view, piece_len)], axis=0
    )
    bit_count = n_view.bit_length() - 1
    for bit_num in range(bit_count):
        kept = image_now.shape[1]
        pairs = image_now.reshape(4, kept // 2, 2, piece_len)
        my_bit = view_idx // 2**bit_num % 2
        first_half = my_bit == 0
        keep = jnp.where(first_half, pairs[:, :, 0], pairs[:, :, 1])
        send = jnp.where(first_half, pairs[:, :, 1], pairs[:, :, 0])
        got = from_partner(send, "view", bit_num)
        front = jnp.where(first_half, keep, got)
        back = jnp.where(first_half, got, keep)
        image_now = jnp.concatenate(
            [front[:3] + front[3:] * back[:3], keep[3:] * got[3:]], axis=0
        )
    final_colour = image_now[:3, 0]
    final_transmit = image_now[3:, 0]
    rows_out = brick_l // n_view
    opacity = 1.0 - final_transmit.reshape(1, rows_out, brick_a)
    return jnp.concatenate([final_colour.reshape(3, rows_out, brick_a), opacity], axis=0)


def solution(mesh):
    in_specs = (
        P("light", "across", "view"),
        P("light", "across", "view"),
        P(None, "across", "view"),
        P(),
        P(),
        P(),
    )
    out_specs = P(None, ("light", "view"), "across")
    return jax.shard_map(shards, mesh=mesh, in_specs=in_specs, out_specs=out_specs, check_vma=False)
```

```python
import jax
import jax.numpy as jnp
from jax import lax
from jax.experimental import pallas as pl
from jax.experimental.pallas import tpu as pltpu
from jax.sharding import PartitionSpec as P

SLABS = 8


BLUR = 0.24
AMBIENT = 0.1
SOFTEN = 0.05


def padded_2(block, sides, width):
    for axis, dim in sides:
        count = lax.axis_size(axis)
        forward = [(i, i + 1) for i in range(count - 1)]
        backward = [(target, source) for source, target in forward]
        low = lax.ppermute(
            lax.slice_in_dim(block, block.shape[dim] - width, None, axis=dim), axis, forward
        )
        high = lax.ppermute(lax.slice_in_dim(block, 0, width, axis=dim), axis, backward)
        block = jnp.concatenate([low, block, high], axis=dim)
    return block


def from_behind(value, axis, steps):
    count = lax.axis_size(axis)
    leading, last = (max(0, -steps), min(count, count - steps))
    return lax.ppermute(value, axis, [(source, source + steps) for source in range(leading, last)])


def from_partner(block, axis, apart):
    count = lax.axis_size(axis)
    route = []
    for low in range(count):
        high = low | 1 << apart
        if high != low and high < count:
            route += [(low, high), (high, low)]
    return lax.ppermute(block, axis, route)


def smooth(field):
    centre = field[1:-1, 1:-1, 1:-1]
    return (
        2.0 * centre
        + field[2:, 1:-1, 1:-1]
        + field[:-2, 1:-1, 1:-1]
        + field[1:-1, 2:, 1:-1]
        + field[1:-1, :-2, 1:-1]
        + field[1:-1, 1:-1, 2:]
        + field[1:-1, 1:-1, :-2]
    ) * 0.125


def shade_from(window, inside):
    slope_light = (window[2:, 1:-1, 1:-1] - window[:-2, 1:-1, 1:-1]) * 0.5
    slope_across = (window[1:-1, 2:, 1:-1] - window[1:-1, :-2, 1:-1]) * 0.5
    slope_view = (window[1:-1, 1:-1, 2:] - window[1:-1, 1:-1, :-2]) * 0.5
    along = 0.8 * slope_light + 0.36 * slope_across + 0.48 * slope_view
    aligned = along * along * inside
    trace = (slope_light * slope_light + slope_across * slope_across + slope_view * slope_view) * inside
    return 0.25 + smooth(aligned) / (smooth(trace) + SOFTEN)


def rim_mask(position, devices, width, border):
    places = position * width - border + jnp.arange(width + 2 * border, dtype=jnp.int32)
    return ((places >= 0) & (places < devices * width)).astype(jnp.float32)


def halo(block, axis, dim, width):
    count = lax.axis_size(axis)
    size = block.shape[dim]
    lows, highs = [], []
    if count == 2:
        need = min(size, width)
        first = lax.axis_index(axis) == 0
        send = block
        if need < size:
            send = jnp.where(
                first,
                lax.slice_in_dim(block, size - need, None, axis=dim),
                lax.slice_in_dim(block, 0, need, axis=dim),
            )
        got = lax.ppermute(send, axis, [(0, 1), (1, 0)])
        lows = [jnp.where(first, jnp.zeros_like(got), got)]
        highs = [jnp.where(first, got, jnp.zeros_like(got))]
        count = 0
    for hop in range(1, count):
        need = min(size, width - (hop - 1) * size)
        if need <= 0:
            break
        forward = [(i, i + hop) for i in range(count - hop)]
        backward = [(target, source) for source, target in forward]
        low = lax.slice_in_dim(block, size - need, None, axis=dim)
        lows.insert(0, lax.ppermute(low, axis, forward))
        highs.append(lax.ppermute(lax.slice_in_dim(block, 0, need, axis=dim), axis, backward))
    block = jnp.concatenate(lows + [block] + highs, axis=dim)
    missing = width - sum(part.shape[dim] for part in lows)
    if missing > 0:
        widths = [(0, 0)] * block.ndim
        widths[dim] = (missing, missing)
        block = jnp.pad(block, widths)
    return block


def plane_mask(border, brick_a, brick_v):
    return (
        rim_mask(lax.axis_index("across"), lax.axis_size("across"), brick_a, border)[:, None]
        * rim_mask(lax.axis_index("view"), lax.axis_size("view"), brick_v, border)[None, :]
    )


def propagate(current, border_in, fade_rim, brick_a, brick_v):
    widest = (fade_rim.shape[2] - brick_a) // 2
    starts = []
    for slab_num in range(SLABS):
        border = border_in - slab_num
        starts.append(current[:, border : border + brick_a, border : border + brick_v])
        offset = widest - border
        fade_here = fade_rim[
            :,
            slab_num,
            offset : offset + brick_a + 2 * border,
            offset : offset + brick_v + 2 * border,
        ]
        current = current * fade_here
        centre = current[:, 1:-1, 1:-1]
        current = centre + BLUR * (
            current[:, :-2, 1:-1]
            + current[:, 2:, 1:-1]
            + current[:, 1:-1, :-2]
            + current[:, 1:-1, 2:]
            - 4.0 * centre
        )
    return (current, jnp.stack(starts, axis=1))


def fade_rim_of(extinction_table, stack_rim, rows, mask, light_step):
    _, rim_a, rim_v = stack_rim.shape
    layer_rows = rows // SLABS
    colours, materials = extinction_table.shape
    chunk = 16 if rim_a % 16 == 0 else (8 if rim_a % 8 == 0 else rim_a)

    def kernel(table_ref, stack_ref, mask_ref, out_ref):
        def one_slab(slab_num, carry):
            for first in range(0, rim_a, chunk):
                part = slice(first, first + chunk)
                depth = [None] * colours
                for row in range(layer_rows):
                    row_num = slab_num * layer_rows + row
                    here = stack_ref[rows + row_num, part, :]
                    cells = stack_ref[row_num, part, :]
                    looked = [jnp.full(here.shape, table_ref[c, 0]) for c in range(colours)]
                    for material in range(1, materials):
                        match = here == float(material)
                        looked = [
                            jnp.where(match, table_ref[c, material], looked[c]) for c in range(colours)
                        ]
                    for c in range(colours):
                        term = looked[c] * cells
                        depth[c] = term if depth[c] is None else depth[c] + term
                for c in range(colours):
                    out_ref[c, slab_num, part, :] = (
                        jnp.exp(-light_step * depth[c]) * mask_ref[part, :]
                    )
            return carry

        lax.fori_loop(0, SLABS, one_slab, 0)

    return pl.pallas_call(
        kernel,
        out_shape=jax.ShapeDtypeStruct((colours, SLABS, rim_a, rim_v), jnp.float32),
        in_specs=[
            pl.BlockSpec(memory_space=pltpu.SMEM),
            pl.BlockSpec(memory_space=pltpu.VMEM),
            pl.BlockSpec(memory_space=pltpu.VMEM),
        ],
        out_specs=pl.BlockSpec(memory_space=pltpu.VMEM),
    )(extinction_table, stack_rim, mask)


def shards(density, labels, sunlight, opacity_table, extinction_table, albedo_table):
    brick_l, brick_a, brick_v = density.shape
    n_light = lax.axis_size("light")
    n_view = lax.axis_size("view")
    n_across = lax.axis_size("across")
    full_l = brick_l * n_light
    full_v = brick_v * n_view
    light_step = 10.0 / full_l
    view_step = 2.0 / full_v
    layer_rows = brick_l // SLABS
    light_idx = lax.axis_index("light")
    view_idx = lax.axis_index("view")
    across_idx = lax.axis_index("across")
    widest = SLABS * n_light
    stack = jnp.concatenate([density, labels.astype(jnp.float32), sunlight], axis=0)
    stack_rim = halo(halo(stack, "across", 1, widest), "view", 2, widest)
    density_rim = stack_rim[:brick_l]
    sun_rim = stack_rim[2 * brick_l :]
    density_side = density_rim[
        :, widest - 2 : widest + brick_a + 2, widest - 2 : widest + brick_v + 2
    ]
    table_all = jnp.concatenate([opacity_table[None], extinction_table, albedo_table], axis=0)
    looked = jnp.broadcast_to(table_all[:, 0, None, None, None], (7,) + labels.shape)
    for material in range(1, table_all.shape[1]):
        looked = jnp.where(
            (labels == material)[None], table_all[:, material, None, None, None], looked
        )
    extinct = looked[1:4] * density[None]
    extinct_slabs = extinct.reshape(3, SLABS, layer_rows, brick_a, brick_v)
    running = jnp.cumsum(extinct_slabs, axis=2) - extinct_slabs
    fade_rim = fade_rim_of(
        extinction_table, stack_rim, brick_l, plane_mask(widest, brick_a, brick_v), light_step
    )
    starts = None
    incoming = sun_rim
    for section_num in range(n_light):
        border = SLABS * (n_light - section_num)
        outgoing, section_starts = propagate(
            incoming, border, fade_rim, brick_a, brick_v
        )
        if starts is None:
            starts = section_starts
        else:
            starts = jnp.where(light_idx == section_num, section_starts, starts)
        if section_num + 1 < n_light:
            incoming = lax.ppermute(outgoing, "light", [(section_num, section_num + 1)])
    padded = padded_2(density_side, (("light", 0),), 2)
    inside = (
        rim_mask(light_idx, n_light, brick_l, 1)[:, None, None]
        * rim_mask(across_idx, n_across, brick_a, 1)[None, :, None]
        * rim_mask(view_idx, n_view, brick_v, 1)[None, None, :]
    )
    shading = shade_from(padded, inside)
    lighting = (starts[:, :, None] * jnp.exp(-light_step * running)).reshape(
        3, brick_l, brick_a, brick_v
    )
    optical = looked[0] * density * view_step
    colour = (1.0 - jnp.exp(-optical))[None] * looked[4:7] * (shading[None] * lighting + AMBIENT)
    upper = (jnp.arange(brick_v)[:, None] < jnp.arange(brick_v)[None, :]).astype(jnp.float32)
    before = jnp.dot(optical.reshape(-1, brick_v), upper, precision=lax.Precision.HIGHEST).reshape(
        brick_l, brick_a, brick_v
    )
    colour_sum = jnp.sum(colour * jnp.exp(-before)[None], axis=-1)
    transmit = jnp.exp(-jnp.sum(optical, axis=-1))
    pixels = brick_l * brick_a
    piece_len = pixels // n_view
    image_now = jnp.concatenate(
        [colour_sum.reshape(3, n_view, piece_len), transmit.reshape(1, n_view, piece_len)], axis=0
    )
    bit_count = n_view.bit_length() - 1
    for bit_num in range(bit_count):
        kept = image_now.shape[1]
        pairs = image_now.reshape(4, kept // 2, 2, piece_len)
        my_bit = view_idx // 2**bit_num % 2
        first_half = my_bit == 0
        keep = jnp.where(first_half, pairs[:, :, 0], pairs[:, :, 1])
        send = jnp.where(first_half, pairs[:, :, 1], pairs[:, :, 0])
        got = from_partner(send, "view", bit_num)
        front = jnp.where(first_half, keep, got)
        back = jnp.where(first_half, got, keep)
        image_now = jnp.concatenate(
            [front[:3] + front[3:] * back[:3], keep[3:] * got[3:]], axis=0
        )
    final_colour = image_now[:3, 0]
    final_transmit = image_now[3:, 0]
    rows_out = brick_l // n_view
    opacity = 1.0 - final_transmit.reshape(1, rows_out, brick_a)
    return jnp.concatenate([final_colour.reshape(3, rows_out, brick_a), opacity], axis=0)


def solution(mesh):
    in_specs = (
        P("light", "across", "view"),
        P("light", "across", "view"),
        P(None, "across", "view"),
        P(),
        P(),
        P(),
    )
    out_specs = P(None, ("light", "view"), "across")
    return jax.shard_map(shards, mesh=mesh, in_specs=in_specs, out_specs=out_specs, check_vma=False)
```

```python
import jax
import jax.numpy as jnp
from jax import lax
from jax.experimental import pallas as pl
from jax.experimental.pallas import tpu as pltpu
from jax.sharding import PartitionSpec as P

SLABS = 8


BLUR = 0.24
AMBIENT = 0.1
SOFTEN = 0.05


def padded_2(block, sides, width):
    for axis, dim in sides:
        count = lax.axis_size(axis)
        forward = [(i, i + 1) for i in range(count - 1)]
        backward = [(target, source) for source, target in forward]
        low = lax.ppermute(
            lax.slice_in_dim(block, block.shape[dim] - width, None, axis=dim), axis, forward
        )
        high = lax.ppermute(lax.slice_in_dim(block, 0, width, axis=dim), axis, backward)
        block = jnp.concatenate([low, block, high], axis=dim)
    return block


def from_behind(value, axis, steps):
    count = lax.axis_size(axis)
    leading, last = (max(0, -steps), min(count, count - steps))
    return lax.ppermute(value, axis, [(source, source + steps) for source in range(leading, last)])


def from_partner(block, axis, apart):
    count = lax.axis_size(axis)
    route = []
    for low in range(count):
        high = low | 1 << apart
        if high != low and high < count:
            route += [(low, high), (high, low)]
    return lax.ppermute(block, axis, route)


def smooth(field):
    centre = field[1:-1, 1:-1, 1:-1]
    return (
        2.0 * centre
        + field[2:, 1:-1, 1:-1]
        + field[:-2, 1:-1, 1:-1]
        + field[1:-1, 2:, 1:-1]
        + field[1:-1, :-2, 1:-1]
        + field[1:-1, 1:-1, 2:]
        + field[1:-1, 1:-1, :-2]
    ) * 0.125


def shade_from(window, inside):
    slope_light = (window[2:, 1:-1, 1:-1] - window[:-2, 1:-1, 1:-1]) * 0.5
    slope_across = (window[1:-1, 2:, 1:-1] - window[1:-1, :-2, 1:-1]) * 0.5
    slope_view = (window[1:-1, 1:-1, 2:] - window[1:-1, 1:-1, :-2]) * 0.5
    along = 0.8 * slope_light + 0.36 * slope_across + 0.48 * slope_view
    aligned = along * along * inside
    trace = (slope_light * slope_light + slope_across * slope_across + slope_view * slope_view) * inside
    return 0.25 + smooth(aligned) / (smooth(trace) + SOFTEN)


def rim_mask(position, devices, width, border):
    places = position * width - border + jnp.arange(width + 2 * border, dtype=jnp.int32)
    return ((places >= 0) & (places < devices * width)).astype(jnp.float32)


def halo(block, axis, dim, width):
    count = lax.axis_size(axis)
    size = block.shape[dim]
    lows, highs = [], []
    if count == 2:
        need = min(size, width)
        first = lax.axis_index(axis) == 0
        send = block
        if need < size:
            send = jnp.where(
                first,
                lax.slice_in_dim(block, size - need, None, axis=dim),
                lax.slice_in_dim(block, 0, need, axis=dim),
            )
        got = lax.ppermute(send, axis, [(0, 1), (1, 0)])
        lows = [jnp.where(first, jnp.zeros_like(got), got)]
        highs = [jnp.where(first, got, jnp.zeros_like(got))]
        count = 0
    for hop in range(1, count):
        need = min(size, width - (hop - 1) * size)
        if need <= 0:
            break
        forward = [(i, i + hop) for i in range(count - hop)]
        backward = [(target, source) for source, target in forward]
        low = lax.slice_in_dim(block, size - need, None, axis=dim)
        lows.insert(0, lax.ppermute(low, axis, forward))
        highs.append(lax.ppermute(lax.slice_in_dim(block, 0, need, axis=dim), axis, backward))
    block = jnp.concatenate(lows + [block] + highs, axis=dim)
    missing = width - sum(part.shape[dim] for part in lows)
    if missing > 0:
        widths = [(0, 0)] * block.ndim
        widths[dim] = (missing, missing)
        block = jnp.pad(block, widths)
    return block


def plane_mask(border, brick_a, brick_v):
    return (
        rim_mask(lax.axis_index("across"), lax.axis_size("across"), brick_a, border)[:, None]
        * rim_mask(lax.axis_index("view"), lax.axis_size("view"), brick_v, border)[None, :]
    )


def propagate(current, border_in, fade_rim, brick_a, brick_v):
    widest = (fade_rim.shape[2] - brick_a) // 2
    starts = []
    for slab_num in range(SLABS):
        border = border_in - slab_num
        starts.append(current[:, border : border + brick_a, border : border + brick_v])
        offset = widest - border
        fade_here = fade_rim[
            :,
            slab_num,
            offset : offset + brick_a + 2 * border,
            offset : offset + brick_v + 2 * border,
        ]
        current = current * fade_here
        centre = current[:, 1:-1, 1:-1]
        current = centre + BLUR * (
            current[:, :-2, 1:-1]
            + current[:, 2:, 1:-1]
            + current[:, 1:-1, :-2]
            + current[:, 1:-1, 2:]
            - 4.0 * centre
        )
    return (current, jnp.stack(starts, axis=1))


def fade_rim_of(extinction_table, stack_rim, rows, mask, light_step):
    _, rim_a, rim_v = stack_rim.shape
    layer_rows = rows // SLABS
    colours, materials = extinction_table.shape
    chunk = 16 if rim_a % 16 == 0 else (8 if rim_a % 8 == 0 else rim_a)

    def kernel(table_ref, stack_ref, mask_ref, out_ref):
        def one_slab(slab_num, carry):
            for first in range(0, rim_a, chunk):
                part = slice(first, first + chunk)
                depth = [None] * colours
                for row in range(layer_rows):
                    row_num = slab_num * layer_rows + row
                    here = stack_ref[rows + row_num, part, :]
                    cells = stack_ref[row_num, part, :]
                    looked = [jnp.full(here.shape, table_ref[c, 0]) for c in range(colours)]
                    for material in range(1, materials):
                        match = here == float(material)
                        looked = [
                            jnp.where(match, table_ref[c, material], looked[c]) for c in range(colours)
                        ]
                    for c in range(colours):
                        term = looked[c] * cells
                        depth[c] = term if depth[c] is None else depth[c] + term
                for c in range(colours):
                    out_ref[c, slab_num, part, :] = (
                        jnp.exp(-light_step * depth[c]) * mask_ref[part, :]
                    )
            return carry

        lax.fori_loop(0, SLABS, one_slab, 0)

    return pl.pallas_call(
        kernel,
        out_shape=jax.ShapeDtypeStruct((colours, SLABS, rim_a, rim_v), jnp.float32),
        in_specs=[
            pl.BlockSpec(memory_space=pltpu.SMEM),
            pl.BlockSpec(memory_space=pltpu.VMEM),
            pl.BlockSpec(memory_space=pltpu.VMEM),
        ],
        out_specs=pl.BlockSpec(memory_space=pltpu.VMEM),
    )(extinction_table, stack_rim, mask)


def shards(density, labels, sunlight, opacity_table, extinction_table, albedo_table):
    brick_l, brick_a, brick_v = density.shape
    n_light = lax.axis_size("light")
    n_view = lax.axis_size("view")
    n_across = lax.axis_size("across")
    full_l = brick_l * n_light
    full_v = brick_v * n_view
    light_step = 10.0 / full_l
    view_step = 2.0 / full_v
    layer_rows = brick_l // SLABS
    light_idx = lax.axis_index("light")
    view_idx = lax.axis_index("view")
    across_idx = lax.axis_index("across")
    widest = SLABS * n_light
    stack = jnp.concatenate([density, labels.astype(jnp.float32), sunlight], axis=0)
    stack_rim = halo(halo(stack, "across", 1, widest), "view", 2, widest)
    density_rim = stack_rim[:brick_l]
    sun_rim = stack_rim[2 * brick_l :]
    density_side = density_rim[
        :, widest - 2 : widest + brick_a + 2, widest - 2 : widest + brick_v + 2
    ]
    table_all = jnp.concatenate([opacity_table[None], extinction_table, albedo_table], axis=0)
    looked = jnp.broadcast_to(table_all[:, 0, None, None, None], (7,) + labels.shape)
    for material in range(1, table_all.shape[1]):
        looked = jnp.where(
            (labels == material)[None], table_all[:, material, None, None, None], looked
        )
    extinct = looked[1:4] * density[None]
    extinct_slabs = extinct.reshape(3, SLABS, layer_rows, brick_a, brick_v)
    running = jnp.cumsum(extinct_slabs, axis=2) - extinct_slabs
    fade_rim = fade_rim_of(
        extinction_table, stack_rim, brick_l, plane_mask(widest, brick_a, brick_v), light_step
    )
    starts = None
    incoming = sun_rim
    for section_num in range(n_light):
        border = SLABS * (n_light - section_num)
        outgoing, section_starts = propagate(
            incoming, border, fade_rim, brick_a, brick_v
        )
        if starts is None:
            starts = section_starts
        else:
            starts = jnp.where(light_idx == section_num, section_starts, starts)
        if section_num + 1 < n_light:
            incoming = lax.ppermute(outgoing, "light", [(section_num, section_num + 1)])
    padded = padded_2(density_side, (("light", 0),), 2)
    inside = (
        rim_mask(light_idx, n_light, brick_l, 1)[:, None, None]
        * rim_mask(across_idx, n_across, brick_a, 1)[None, :, None]
        * rim_mask(view_idx, n_view, brick_v, 1)[None, None, :]
    )
    shading = shade_from(padded, inside)
    lighting = (starts[:, :, None] * jnp.exp(-light_step * running)).reshape(
        3, brick_l, brick_a, brick_v
    )
    optical = looked[0] * density * view_step
    colour = (1.0 - jnp.exp(-optical))[None] * looked[4:7] * (shading[None] * lighting + AMBIENT)
    upper = (jnp.arange(brick_v)[:, None] < jnp.arange(brick_v)[None, :]).astype(jnp.float32)
    before = jnp.dot(optical.reshape(-1, brick_v), upper, precision=lax.Precision.HIGHEST).reshape(
        brick_l, brick_a, brick_v
    )
    colour_sum = jnp.sum(colour * jnp.exp(-before)[None], axis=-1)
    transmit = jnp.exp(-jnp.sum(optical, axis=-1))
    pixels = brick_l * brick_a
    piece_len = pixels // n_view
    image_now = jnp.concatenate(
        [colour_sum.reshape(3, n_view, piece_len), transmit.reshape(1, n_view, piece_len)], axis=0
    )
    received = [image_now[:, :, None]]
    for shift in range(1, n_view):
        piece = lax.dynamic_slice_in_dim(image_now, (view_idx + shift) % n_view, 1, axis=1)
        route = [(source, (source + shift) % n_view) for source in range(n_view)]
        received.append(lax.ppermute(piece, "view", route)[:, :, None])
    own = lax.dynamic_slice_in_dim(image_now, view_idx, 1, axis=1)
    received[0] = own[:, :, None]
    by_shift = jnp.concatenate(received, axis=2)[:, 0]
    order = (view_idx - jnp.arange(n_view)) % n_view
    segments = jnp.take(by_shift, order, axis=1)
    final_colour = segments[:3, n_view - 1]
    final_transmit = segments[3:, n_view - 1]
    for segment in range(n_view - 2, -1, -1):
        final_colour = segments[:3, segment] + segments[3:, segment] * final_colour
        final_transmit = segments[3:, segment] * final_transmit
    rows_out = brick_l // n_view
    opacity = 1.0 - final_transmit.reshape(1, rows_out, brick_a)
    return jnp.concatenate([final_colour.reshape(3, rows_out, brick_a), opacity], axis=0)


def solution(mesh):
    in_specs = (
        P("light", "across", "view"),
        P("light", "across", "view"),
        P(None, "across", "view"),
        P(),
        P(),
        P(),
    )
    out_specs = P(None, ("light", "view"), "across")
    return jax.shard_map(shards, mesh=mesh, in_specs=in_specs, out_specs=out_specs, check_vma=False)
```

```python
import jax
import jax.numpy as jnp
from jax import lax
from jax.experimental import pallas as pl
from jax.experimental.pallas import tpu as pltpu
from jax.sharding import PartitionSpec as P

SLABS = 8


BLUR = 0.24
AMBIENT = 0.1
SOFTEN = 0.05


def padded_2(block, sides, width):
    for axis, dim in sides:
        count = lax.axis_size(axis)
        forward = [(i, i + 1) for i in range(count - 1)]
        backward = [(target, source) for source, target in forward]
        low = lax.ppermute(
            lax.slice_in_dim(block, block.shape[dim] - width, None, axis=dim), axis, forward
        )
        high = lax.ppermute(lax.slice_in_dim(block, 0, width, axis=dim), axis, backward)
        block = jnp.concatenate([low, block, high], axis=dim)
    return block


def from_behind(value, axis, steps):
    count = lax.axis_size(axis)
    leading, last = (max(0, -steps), min(count, count - steps))
    return lax.ppermute(value, axis, [(source, source + steps) for source in range(leading, last)])


def from_partner(block, axis, apart):
    count = lax.axis_size(axis)
    route = []
    for low in range(count):
        high = low | 1 << apart
        if high != low and high < count:
            route += [(low, high), (high, low)]
    return lax.ppermute(block, axis, route)


def smooth(field):
    centre = field[1:-1, 1:-1, 1:-1]
    return (
        2.0 * centre
        + field[2:, 1:-1, 1:-1]
        + field[:-2, 1:-1, 1:-1]
        + field[1:-1, 2:, 1:-1]
        + field[1:-1, :-2, 1:-1]
        + field[1:-1, 1:-1, 2:]
        + field[1:-1, 1:-1, :-2]
    ) * 0.125


def shade_from(window, inside):
    slope_light = (window[2:, 1:-1, 1:-1] - window[:-2, 1:-1, 1:-1]) * 0.5
    slope_across = (window[1:-1, 2:, 1:-1] - window[1:-1, :-2, 1:-1]) * 0.5
    slope_view = (window[1:-1, 1:-1, 2:] - window[1:-1, 1:-1, :-2]) * 0.5
    along = 0.8 * slope_light + 0.36 * slope_across + 0.48 * slope_view
    aligned = along * along * inside
    trace = (slope_light * slope_light + slope_across * slope_across + slope_view * slope_view) * inside
    return 0.25 + smooth(aligned) / (smooth(trace) + SOFTEN)


def rim_mask(position, devices, width, border):
    places = position * width - border + jnp.arange(width + 2 * border, dtype=jnp.int32)
    return ((places >= 0) & (places < devices * width)).astype(jnp.float32)


def halo(block, axis, dim, width):
    count = lax.axis_size(axis)
    size = block.shape[dim]
    lows, highs = [], []
    if count == 2:
        need = min(size, width)
        first = lax.axis_index(axis) == 0
        send = block
        if need < size:
            send = jnp.where(
                first,
                lax.slice_in_dim(block, size - need, None, axis=dim),
                lax.slice_in_dim(block, 0, need, axis=dim),
            )
        got = lax.ppermute(send, axis, [(0, 1), (1, 0)])
        lows = [jnp.where(first, jnp.zeros_like(got), got)]
        highs = [jnp.where(first, got, jnp.zeros_like(got))]
        count = 0
    for hop in range(1, count):
        need = min(size, width - (hop - 1) * size)
        if need <= 0:
            break
        forward = [(i, i + hop) for i in range(count - hop)]
        backward = [(target, source) for source, target in forward]
        low = lax.slice_in_dim(block, size - need, None, axis=dim)
        lows.insert(0, lax.ppermute(low, axis, forward))
        highs.append(lax.ppermute(lax.slice_in_dim(block, 0, need, axis=dim), axis, backward))
    block = jnp.concatenate(lows + [block] + highs, axis=dim)
    missing = width - sum(part.shape[dim] for part in lows)
    if missing > 0:
        widths = [(0, 0)] * block.ndim
        widths[dim] = (missing, missing)
        block = jnp.pad(block, widths)
    return block


def plane_mask(border, brick_a, brick_v):
    return (
        rim_mask(lax.axis_index("across"), lax.axis_size("across"), brick_a, border)[:, None]
        * rim_mask(lax.axis_index("view"), lax.axis_size("view"), brick_v, border)[None, :]
    )


def propagate(current, border_in, fade_rim, brick_a, brick_v):
    widest = (fade_rim.shape[2] - brick_a) // 2
    starts = []
    for slab_num in range(SLABS):
        border = border_in - slab_num
        starts.append(current[:, border : border + brick_a, border : border + brick_v])
        offset = widest - border
        fade_here = fade_rim[
            :,
            slab_num,
            offset : offset + brick_a + 2 * border,
            offset : offset + brick_v + 2 * border,
        ]
        current = current * fade_here
        centre = current[:, 1:-1, 1:-1]
        current = centre + BLUR * (
            current[:, :-2, 1:-1]
            + current[:, 2:, 1:-1]
            + current[:, 1:-1, :-2]
            + current[:, 1:-1, 2:]
            - 4.0 * centre
        )
    return (current, jnp.stack(starts, axis=1))


def fade_rim_of(extinction_table, stack_rim, rows, mask, light_step):
    _, rim_a, rim_v = stack_rim.shape
    layer_rows = rows // SLABS
    colours, materials = extinction_table.shape
    chunk = 16 if rim_a % 16 == 0 else (8 if rim_a % 8 == 0 else rim_a)

    def kernel(table_ref, stack_ref, mask_ref, out_ref):
        def one_slab(slab_num, carry):
            for first in range(0, rim_a, chunk):
                part = slice(first, first + chunk)
                depth = [None] * colours
                for row in range(layer_rows):
                    row_num = slab_num * layer_rows + row
                    here = stack_ref[rows + row_num, part, :]
                    cells = stack_ref[row_num, part, :]
                    looked = [jnp.full(here.shape, table_ref[c, 0]) for c in range(colours)]
                    for material in range(1, materials):
                        match = here == float(material)
                        looked = [
                            jnp.where(match, table_ref[c, material], looked[c]) for c in range(colours)
                        ]
                    for c in range(colours):
                        term = looked[c] * cells
                        depth[c] = term if depth[c] is None else depth[c] + term
                for c in range(colours):
                    out_ref[c, slab_num, part, :] = (
                        jnp.exp(-light_step * depth[c]) * mask_ref[part, :]
                    )
            return carry

        lax.fori_loop(0, SLABS, one_slab, 0)

    return pl.pallas_call(
        kernel,
        out_shape=jax.ShapeDtypeStruct((colours, SLABS, rim_a, rim_v), jnp.float32),
        in_specs=[
            pl.BlockSpec(memory_space=pltpu.SMEM),
            pl.BlockSpec(memory_space=pltpu.VMEM),
            pl.BlockSpec(memory_space=pltpu.VMEM),
        ],
        out_specs=pl.BlockSpec(memory_space=pltpu.VMEM),
    )(extinction_table, stack_rim, mask)


def shards(density, labels, sunlight, opacity_table, extinction_table, albedo_table):
    brick_l, brick_a, brick_v = density.shape
    n_light = lax.axis_size("light")
    n_view = lax.axis_size("view")
    n_across = lax.axis_size("across")
    full_l = brick_l * n_light
    full_v = brick_v * n_view
    light_step = 10.0 / full_l
    view_step = 2.0 / full_v
    layer_rows = brick_l // SLABS
    light_idx = lax.axis_index("light")
    view_idx = lax.axis_index("view")
    across_idx = lax.axis_index("across")
    widest = SLABS * n_light
    stack = jnp.concatenate([density, labels.astype(jnp.float32), sunlight], axis=0)
    stack_rim = halo(halo(stack, "across", 1, widest), "view", 2, widest)
    density_rim = stack_rim[:brick_l]
    sun_rim = stack_rim[2 * brick_l :]
    density_side = density_rim[
        :, widest - 2 : widest + brick_a + 2, widest - 2 : widest + brick_v + 2
    ]
    table_all = jnp.concatenate([opacity_table[None], extinction_table, albedo_table], axis=0)
    looked = jnp.broadcast_to(table_all[:, 0, None, None, None], (7,) + labels.shape)
    for material in range(1, table_all.shape[1]):
        looked = jnp.where(
            (labels == material)[None], table_all[:, material, None, None, None], looked
        )
    extinct = looked[1:4] * density[None]
    extinct_slabs = extinct.reshape(3, SLABS, layer_rows, brick_a, brick_v)
    running = jnp.cumsum(extinct_slabs, axis=2) - extinct_slabs
    fade_rim = fade_rim_of(
        extinction_table, stack_rim, brick_l, plane_mask(widest, brick_a, brick_v), light_step
    )
    starts = None
    incoming = sun_rim
    for section_num in range(n_light):
        border = SLABS * (n_light - section_num)
        outgoing, section_starts = propagate(
            incoming, border, fade_rim, brick_a, brick_v
        )
        if starts is None:
            starts = section_starts
        else:
            starts = jnp.where(light_idx == section_num, section_starts, starts)
        if section_num + 1 < n_light:
            incoming = lax.ppermute(outgoing, "light", [(section_num, section_num + 1)])
    padded = padded_2(density_side, (("light", 0),), 2)
    inside = (
        rim_mask(light_idx, n_light, brick_l, 1)[:, None, None]
        * rim_mask(across_idx, n_across, brick_a, 1)[None, :, None]
        * rim_mask(view_idx, n_view, brick_v, 1)[None, None, :]
    )
    shading = shade_from(padded, inside)
    optical = looked[0] * density * view_step
    upper = (jnp.arange(brick_v)[:, None] < jnp.arange(brick_v)[None, :]).astype(jnp.float32)
    before = jnp.dot(optical.reshape(-1, brick_v), upper, precision=lax.Precision.HIGHEST).reshape(
        brick_l, brick_a, brick_v
    )
    weight = (1.0 - jnp.exp(-optical))[None] * looked[4:7] * jnp.exp(-before)[None]
    lit = (weight * shading[None]).reshape(3, SLABS, layer_rows, brick_a, brick_v) * jnp.exp(
        -light_step * running
    )
    ambient_sum = AMBIENT * jnp.sum(weight, axis=-1)
    lit, ambient_sum = lax.optimization_barrier((lit, ambient_sum))
    colour_sum = (
        jnp.sum((lit * starts[:, :, None]).reshape(3, brick_l, brick_a, brick_v), axis=-1)
        + ambient_sum
    )
    transmit = jnp.exp(-jnp.sum(optical, axis=-1))
    pixels = brick_l * brick_a
    piece_len = pixels // n_view
    image_now = jnp.concatenate(
        [colour_sum.reshape(3, n_view, piece_len), transmit.reshape(1, n_view, piece_len)], axis=0
    )
    bit_count = n_view.bit_length() - 1
    for bit_num in range(bit_count):
        kept = image_now.shape[1]
        pairs = image_now.reshape(4, kept // 2, 2, piece_len)
        my_bit = view_idx // 2**bit_num % 2
        first_half = my_bit == 0
        keep = jnp.where(first_half, pairs[:, :, 0], pairs[:, :, 1])
        send = jnp.where(first_half, pairs[:, :, 1], pairs[:, :, 0])
        got = from_partner(send, "view", bit_num)
        front = jnp.where(first_half, keep, got)
        back = jnp.where(first_half, got, keep)
        image_now = jnp.concatenate(
            [front[:3] + front[3:] * back[:3], keep[3:] * got[3:]], axis=0
        )
    final_colour = image_now[:3, 0]
    final_transmit = image_now[3:, 0]
    rows_out = brick_l // n_view
    opacity = 1.0 - final_transmit.reshape(1, rows_out, brick_a)
    return jnp.concatenate([final_colour.reshape(3, rows_out, brick_a), opacity], axis=0)


def solution(mesh):
    in_specs = (
        P("light", "across", "view"),
        P("light", "across", "view"),
        P(None, "across", "view"),
        P(),
        P(),
        P(),
    )
    out_specs = P(None, ("light", "view"), "across")
    return jax.shard_map(shards, mesh=mesh, in_specs=in_specs, out_specs=out_specs, check_vma=False)
```

```python
import jax
import jax.numpy as jnp
from jax import lax
from jax.experimental import pallas as pl
from jax.experimental.pallas import tpu as pltpu
from jax.sharding import PartitionSpec as P

SLABS = 8


BLUR = 0.24
AMBIENT = 0.1
SOFTEN = 0.05


def padded_2(block, sides, width):
    for axis, dim in sides:
        count = lax.axis_size(axis)
        forward = [(i, i + 1) for i in range(count - 1)]
        backward = [(target, source) for source, target in forward]
        low = lax.ppermute(
            lax.slice_in_dim(block, block.shape[dim] - width, None, axis=dim), axis, forward
        )
        high = lax.ppermute(lax.slice_in_dim(block, 0, width, axis=dim), axis, backward)
        block = jnp.concatenate([low, block, high], axis=dim)
    return block


def from_behind(value, axis, steps):
    count = lax.axis_size(axis)
    leading, last = (max(0, -steps), min(count, count - steps))
    return lax.ppermute(value, axis, [(source, source + steps) for source in range(leading, last)])


def from_partner(block, axis, apart):
    count = lax.axis_size(axis)
    route = []
    for low in range(count):
        high = low | 1 << apart
        if high != low and high < count:
            route += [(low, high), (high, low)]
    return lax.ppermute(block, axis, route)


def smooth(field):
    centre = field[1:-1, 1:-1, 1:-1]
    return (
        2.0 * centre
        + field[2:, 1:-1, 1:-1]
        + field[:-2, 1:-1, 1:-1]
        + field[1:-1, 2:, 1:-1]
        + field[1:-1, :-2, 1:-1]
        + field[1:-1, 1:-1, 2:]
        + field[1:-1, 1:-1, :-2]
    ) * 0.125


def shade_from(window, inside):
    slope_light = (window[2:, 1:-1, 1:-1] - window[:-2, 1:-1, 1:-1]) * 0.5
    slope_across = (window[1:-1, 2:, 1:-1] - window[1:-1, :-2, 1:-1]) * 0.5
    slope_view = (window[1:-1, 1:-1, 2:] - window[1:-1, 1:-1, :-2]) * 0.5
    along = 0.8 * slope_light + 0.36 * slope_across + 0.48 * slope_view
    aligned = along * along * inside
    trace = (slope_light * slope_light + slope_across * slope_across + slope_view * slope_view) * inside
    return 0.25 + smooth(aligned) / (smooth(trace) + SOFTEN)


def rim_mask(position, devices, width, border):
    places = position * width - border + jnp.arange(width + 2 * border, dtype=jnp.int32)
    return ((places >= 0) & (places < devices * width)).astype(jnp.float32)


def halo(block, axis, dim, width):
    count = lax.axis_size(axis)
    size = block.shape[dim]
    lows, highs = [], []
    if count == 2:
        need = min(size, width)
        first = lax.axis_index(axis) == 0
        send = block
        if need < size:
            send = jnp.where(
                first,
                lax.slice_in_dim(block, size - need, None, axis=dim),
                lax.slice_in_dim(block, 0, need, axis=dim),
            )
        half = send.shape[0] // 2
        got = jnp.concatenate(
            [
                lax.ppermute(send[:half], axis, [(0, 1), (1, 0)]),
                lax.ppermute(send[half:], axis, [(0, 1), (1, 0)]),
            ],
            axis=0,
        )
        lows = [jnp.where(first, jnp.zeros_like(got), got)]
        highs = [jnp.where(first, got, jnp.zeros_like(got))]
        count = 0
    for hop in range(1, count):
        need = min(size, width - (hop - 1) * size)
        if need <= 0:
            break
        forward = [(i, i + hop) for i in range(count - hop)]
        backward = [(target, source) for source, target in forward]
        low = lax.slice_in_dim(block, size - need, None, axis=dim)
        lows.insert(0, lax.ppermute(low, axis, forward))
        highs.append(lax.ppermute(lax.slice_in_dim(block, 0, need, axis=dim), axis, backward))
    block = jnp.concatenate(lows + [block] + highs, axis=dim)
    missing = width - sum(part.shape[dim] for part in lows)
    if missing > 0:
        widths = [(0, 0)] * block.ndim
        widths[dim] = (missing, missing)
        block = jnp.pad(block, widths)
    return block


def plane_mask(border, brick_a, brick_v):
    return (
        rim_mask(lax.axis_index("across"), lax.axis_size("across"), brick_a, border)[:, None]
        * rim_mask(lax.axis_index("view"), lax.axis_size("view"), brick_v, border)[None, :]
    )


def propagate(current, border_in, fade_rim, brick_a, brick_v):
    widest = (fade_rim.shape[2] - brick_a) // 2
    starts = []
    for slab_num in range(SLABS):
        border = border_in - slab_num
        starts.append(current[:, border : border + brick_a, border : border + brick_v])
        offset = widest - border
        fade_here = fade_rim[
            :,
            slab_num,
            offset : offset + brick_a + 2 * border,
            offset : offset + brick_v + 2 * border,
        ]
        current = current * fade_here
        centre = current[:, 1:-1, 1:-1]
        current = centre + BLUR * (
            current[:, :-2, 1:-1]
            + current[:, 2:, 1:-1]
            + current[:, 1:-1, :-2]
            + current[:, 1:-1, 2:]
            - 4.0 * centre
        )
    return (current, jnp.stack(starts, axis=1))


def fade_rim_of(extinction_table, stack_rim, rows, mask, light_step):
    _, rim_a, rim_v = stack_rim.shape
    layer_rows = rows // SLABS
    colours, materials = extinction_table.shape
    chunk = 16 if rim_a % 16 == 0 else (8 if rim_a % 8 == 0 else rim_a)

    def kernel(table_ref, stack_ref, mask_ref, out_ref):
        def one_slab(slab_num, carry):
            for first in range(0, rim_a, chunk):
                part = slice(first, first + chunk)
                depth = [None] * colours
                for row in range(layer_rows):
                    row_num = slab_num * layer_rows + row
                    here = stack_ref[rows + row_num, part, :]
                    cells = stack_ref[row_num, part, :]
                    looked = [jnp.full(here.shape, table_ref[c, 0]) for c in range(colours)]
                    for material in range(1, materials):
                        match = here == float(material)
                        looked = [
                            jnp.where(match, table_ref[c, material], looked[c]) for c in range(colours)
                        ]
                    for c in range(colours):
                        term = looked[c] * cells
                        depth[c] = term if depth[c] is None else depth[c] + term
                for c in range(colours):
                    out_ref[c, slab_num, part, :] = (
                        jnp.exp(-light_step * depth[c]) * mask_ref[part, :]
                    )
            return carry

        lax.fori_loop(0, SLABS, one_slab, 0)

    return pl.pallas_call(
        kernel,
        out_shape=jax.ShapeDtypeStruct((colours, SLABS, rim_a, rim_v), jnp.float32),
        in_specs=[
            pl.BlockSpec(memory_space=pltpu.SMEM),
            pl.BlockSpec(memory_space=pltpu.VMEM),
            pl.BlockSpec(memory_space=pltpu.VMEM),
        ],
        out_specs=pl.BlockSpec(memory_space=pltpu.VMEM),
    )(extinction_table, stack_rim, mask)


def shards(density, labels, sunlight, opacity_table, extinction_table, albedo_table):
    brick_l, brick_a, brick_v = density.shape
    n_light = lax.axis_size("light")
    n_view = lax.axis_size("view")
    n_across = lax.axis_size("across")
    full_l = brick_l * n_light
    full_v = brick_v * n_view
    light_step = 10.0 / full_l
    view_step = 2.0 / full_v
    layer_rows = brick_l // SLABS
    light_idx = lax.axis_index("light")
    view_idx = lax.axis_index("view")
    across_idx = lax.axis_index("across")
    widest = SLABS * n_light
    stack = jnp.concatenate([density, labels.astype(jnp.float32), sunlight], axis=0)
    stack_rim = halo(halo(stack, "across", 1, widest), "view", 2, widest)
    density_rim = stack_rim[:brick_l]
    sun_rim = stack_rim[2 * brick_l :]
    density_side = density_rim[
        :, widest - 2 : widest + brick_a + 2, widest - 2 : widest + brick_v + 2
    ]
    table_all = jnp.concatenate([opacity_table[None], extinction_table, albedo_table], axis=0)
    looked = jnp.broadcast_to(table_all[:, 0, None, None, None], (7,) + labels.shape)
    for material in range(1, table_all.shape[1]):
        looked = jnp.where(
            (labels == material)[None], table_all[:, material, None, None, None], looked
        )
    extinct = looked[1:4] * density[None]
    extinct_slabs = extinct.reshape(3, SLABS, layer_rows, brick_a, brick_v)
    running = jnp.cumsum(extinct_slabs, axis=2) - extinct_slabs
    fade_rim = fade_rim_of(
        extinction_table, stack_rim, brick_l, plane_mask(widest, brick_a, brick_v), light_step
    )
    starts = None
    incoming = sun_rim
    for section_num in range(n_light):
        border = SLABS * (n_light - section_num)
        outgoing, section_starts = propagate(
            incoming, border, fade_rim, brick_a, brick_v
        )
        if starts is None:
            starts = section_starts
        else:
            starts = jnp.where(light_idx == section_num, section_starts, starts)
        if section_num + 1 < n_light:
            incoming = lax.ppermute(outgoing, "light", [(section_num, section_num + 1)])
    padded = padded_2(density_side, (("light", 0),), 2)
    inside = (
        rim_mask(light_idx, n_light, brick_l, 1)[:, None, None]
        * rim_mask(across_idx, n_across, brick_a, 1)[None, :, None]
        * rim_mask(view_idx, n_view, brick_v, 1)[None, None, :]
    )
    shading = shade_from(padded, inside)
    lighting = (starts[:, :, None] * jnp.exp(-light_step * running)).reshape(
        3, brick_l, brick_a, brick_v
    )
    optical = looked[0] * density * view_step
    colour = (1.0 - jnp.exp(-optical))[None] * looked[4:7] * (shading[None] * lighting + AMBIENT)
    upper = (jnp.arange(brick_v)[:, None] < jnp.arange(brick_v)[None, :]).astype(jnp.float32)
    before = jnp.dot(optical.reshape(-1, brick_v), upper, precision=lax.Precision.HIGHEST).reshape(
        brick_l, brick_a, brick_v
    )
    colour_sum = jnp.sum(colour * jnp.exp(-before)[None], axis=-1)
    transmit = jnp.exp(-jnp.sum(optical, axis=-1))
    pixels = brick_l * brick_a
    piece_len = pixels // n_view
    image_now = jnp.concatenate(
        [colour_sum.reshape(3, n_view, piece_len), transmit.reshape(1, n_view, piece_len)], axis=0
    )
    bit_count = n_view.bit_length() - 1
    for bit_num in range(bit_count):
        kept = image_now.shape[1]
        pairs = image_now.reshape(4, kept // 2, 2, piece_len)
        my_bit = view_idx // 2**bit_num % 2
        first_half = my_bit == 0
        keep = jnp.where(first_half, pairs[:, :, 0], pairs[:, :, 1])
        send = jnp.where(first_half, pairs[:, :, 1], pairs[:, :, 0])
        got = from_partner(send, "view", bit_num)
        front = jnp.where(first_half, keep, got)
        back = jnp.where(first_half, got, keep)
        image_now = jnp.concatenate(
            [front[:3] + front[3:] * back[:3], keep[3:] * got[3:]], axis=0
        )
    final_colour = image_now[:3, 0]
    final_transmit = image_now[3:, 0]
    rows_out = brick_l // n_view
    opacity = 1.0 - final_transmit.reshape(1, rows_out, brick_a)
    return jnp.concatenate([final_colour.reshape(3, rows_out, brick_a), opacity], axis=0)


def solution(mesh):
    in_specs = (
        P("light", "across", "view"),
        P("light", "across", "view"),
        P(None, "across", "view"),
        P(),
        P(),
        P(),
    )
    out_specs = P(None, ("light", "view"), "across")
    return jax.shard_map(shards, mesh=mesh, in_specs=in_specs, out_specs=out_specs, check_vma=False)
```

```python
import jax
import jax.numpy as jnp
from jax import lax
from jax.experimental import pallas as pl
from jax.experimental.pallas import tpu as pltpu
from jax.sharding import PartitionSpec as P

SLABS = 8


BLUR = 0.24
AMBIENT = 0.1
SOFTEN = 0.05


def padded_2(block, sides, width):
    for axis, dim in sides:
        count = lax.axis_size(axis)
        forward = [(i, i + 1) for i in range(count - 1)]
        backward = [(target, source) for source, target in forward]
        low = lax.ppermute(
            lax.slice_in_dim(block, block.shape[dim] - width, None, axis=dim), axis, forward
        )
        high = lax.ppermute(lax.slice_in_dim(block, 0, width, axis=dim), axis, backward)
        block = jnp.concatenate([low, block, high], axis=dim)
    return block


def from_behind(value, axis, steps):
    count = lax.axis_size(axis)
    leading, last = (max(0, -steps), min(count, count - steps))
    return lax.ppermute(value, axis, [(source, source + steps) for source in range(leading, last)])


def from_partner(block, axis, apart):
    count = lax.axis_size(axis)
    route = []
    for low in range(count):
        high = low | 1 << apart
        if high != low and high < count:
            route += [(low, high), (high, low)]
    return lax.ppermute(block, axis, route)


def smooth(field):
    centre = field[1:-1, 1:-1, 1:-1]
    return (
        2.0 * centre
        + field[2:, 1:-1, 1:-1]
        + field[:-2, 1:-1, 1:-1]
        + field[1:-1, 2:, 1:-1]
        + field[1:-1, :-2, 1:-1]
        + field[1:-1, 1:-1, 2:]
        + field[1:-1, 1:-1, :-2]
    ) * 0.125


def shade_from(window, inside):
    slope_light = (window[2:, 1:-1, 1:-1] - window[:-2, 1:-1, 1:-1]) * 0.5
    slope_across = (window[1:-1, 2:, 1:-1] - window[1:-1, :-2, 1:-1]) * 0.5
    slope_view = (window[1:-1, 1:-1, 2:] - window[1:-1, 1:-1, :-2]) * 0.5
    along = 0.8 * slope_light + 0.36 * slope_across + 0.48 * slope_view
    aligned = along * along * inside
    trace = (slope_light * slope_light + slope_across * slope_across + slope_view * slope_view) * inside
    return 0.25 + smooth(aligned) / (smooth(trace) + SOFTEN)


def rim_mask(position, devices, width, border):
    places = position * width - border + jnp.arange(width + 2 * border, dtype=jnp.int32)
    return ((places >= 0) & (places < devices * width)).astype(jnp.float32)


def halo(block, axis, dim, width):
    count = lax.axis_size(axis)
    size = block.shape[dim]
    lows, highs = [], []
    if count == 2:
        need = min(size, width)
        first = lax.axis_index(axis) == 0
        send = block
        if need < size:
            send = jnp.where(
                first,
                lax.slice_in_dim(block, size - need, None, axis=dim),
                lax.slice_in_dim(block, 0, need, axis=dim),
            )
        half = send.shape[0] // 2
        got = jnp.concatenate(
            [
                lax.ppermute(send[:half], axis, [(0, 1), (1, 0)]),
                lax.ppermute(send[half:], axis, [(0, 1), (1, 0)]),
            ],
            axis=0,
        )
        lows = [jnp.where(first, jnp.zeros_like(got), got)]
        highs = [jnp.where(first, got, jnp.zeros_like(got))]
        count = 0
    for hop in range(1, count):
        need = min(size, width - (hop - 1) * size)
        if need <= 0:
            break
        forward = [(i, i + hop) for i in range(count - hop)]
        backward = [(target, source) for source, target in forward]
        low = lax.slice_in_dim(block, size - need, None, axis=dim)
        lows.insert(0, lax.ppermute(low, axis, forward))
        highs.append(lax.ppermute(lax.slice_in_dim(block, 0, need, axis=dim), axis, backward))
    block = jnp.concatenate(lows + [block] + highs, axis=dim)
    missing = width - sum(part.shape[dim] for part in lows)
    if missing > 0:
        widths = [(0, 0)] * block.ndim
        widths[dim] = (missing, missing)
        block = jnp.pad(block, widths)
    return block


def plane_mask(border, brick_a, brick_v):
    return (
        rim_mask(lax.axis_index("across"), lax.axis_size("across"), brick_a, border)[:, None]
        * rim_mask(lax.axis_index("view"), lax.axis_size("view"), brick_v, border)[None, :]
    )


def propagate(current, border_in, fade_rim, brick_a, brick_v):
    widest = (fade_rim.shape[2] - brick_a) // 2
    starts = []
    for slab_num in range(SLABS):
        border = border_in - slab_num
        starts.append(current[:, border : border + brick_a, border : border + brick_v])
        offset = widest - border
        fade_here = fade_rim[
            :,
            slab_num,
            offset : offset + brick_a + 2 * border,
            offset : offset + brick_v + 2 * border,
        ]
        current = current * fade_here
        centre = current[:, 1:-1, 1:-1]
        current = centre + BLUR * (
            current[:, :-2, 1:-1]
            + current[:, 2:, 1:-1]
            + current[:, 1:-1, :-2]
            + current[:, 1:-1, 2:]
            - 4.0 * centre
        )
    return (current, jnp.stack(starts, axis=1))


def fade_rim_of(extinction_table, stack_rim, rows, mask, light_step):
    _, rim_a, rim_v = stack_rim.shape
    layer_rows = rows // SLABS
    colours, materials = extinction_table.shape
    chunk = 16 if rim_a % 16 == 0 else (8 if rim_a % 8 == 0 else rim_a)

    def kernel(table_ref, stack_ref, mask_ref, out_ref):
        def one_slab(slab_num, carry):
            for first in range(0, rim_a, chunk):
                part = slice(first, first + chunk)
                depth = [None] * colours
                for row in range(layer_rows):
                    row_num = slab_num * layer_rows + row
                    here = stack_ref[rows + row_num, part, :]
                    cells = stack_ref[row_num, part, :]
                    looked = [jnp.full(here.shape, table_ref[c, 0]) for c in range(colours)]
                    for material in range(1, materials):
                        match = here == float(material)
                        looked = [
                            jnp.where(match, table_ref[c, material], looked[c]) for c in range(colours)
                        ]
                    for c in range(colours):
                        term = looked[c] * cells
                        depth[c] = term if depth[c] is None else depth[c] + term
                for c in range(colours):
                    out_ref[c, slab_num, part, :] = (
                        jnp.exp(-light_step * depth[c]) * mask_ref[part, :]
                    )
            return carry

        lax.fori_loop(0, SLABS, one_slab, 0)

    return pl.pallas_call(
        kernel,
        out_shape=jax.ShapeDtypeStruct((colours, SLABS, rim_a, rim_v), jnp.float32),
        in_specs=[
            pl.BlockSpec(memory_space=pltpu.SMEM),
            pl.BlockSpec(memory_space=pltpu.VMEM),
            pl.BlockSpec(memory_space=pltpu.VMEM),
        ],
        out_specs=pl.BlockSpec(memory_space=pltpu.VMEM),
    )(extinction_table, stack_rim, mask)


def shards(density, labels, sunlight, opacity_table, extinction_table, albedo_table):
    brick_l, brick_a, brick_v = density.shape
    n_light = lax.axis_size("light")
    n_view = lax.axis_size("view")
    n_across = lax.axis_size("across")
    full_l = brick_l * n_light
    full_v = brick_v * n_view
    light_step = 10.0 / full_l
    view_step = 2.0 / full_v
    layer_rows = brick_l // SLABS
    light_idx = lax.axis_index("light")
    view_idx = lax.axis_index("view")
    across_idx = lax.axis_index("across")
    widest = SLABS * n_light
    stack = jnp.concatenate([density, labels.astype(jnp.float32), sunlight], axis=0)
    stack_rim = halo(halo(stack, "across", 1, widest), "view", 2, widest)
    density_rim = stack_rim[:brick_l]
    sun_rim = stack_rim[2 * brick_l :]
    density_side = density_rim[
        :, widest - 2 : widest + brick_a + 2, widest - 2 : widest + brick_v + 2
    ]
    table_all = jnp.concatenate([opacity_table[None], extinction_table, albedo_table], axis=0)
    looked = jnp.broadcast_to(table_all[:, 0, None, None, None], (7,) + labels.shape)
    for material in range(1, table_all.shape[1]):
        looked = jnp.where(
            (labels == material)[None], table_all[:, material, None, None, None], looked
        )
    extinct = looked[1:4] * density[None]
    extinct_slabs = extinct.reshape(3, SLABS, layer_rows, brick_a, brick_v)
    running = jnp.cumsum(extinct_slabs, axis=2) - extinct_slabs
    fade_rim = fade_rim_of(
        extinction_table, stack_rim, brick_l, plane_mask(widest, brick_a, brick_v), light_step
    )
    starts = None
    incoming = sun_rim
    for section_num in range(n_light):
        border = SLABS * (n_light - section_num)
        outgoing, section_starts = propagate(
            incoming, border, fade_rim, brick_a, brick_v
        )
        if starts is None:
            starts = section_starts
        else:
            starts = jnp.where(light_idx == section_num, section_starts, starts)
        if section_num + 1 < n_light:
            incoming = lax.ppermute(outgoing, "light", [(section_num, section_num + 1)])
    odd = light_idx % 2 == 1
    first_rows = density_side[:2]
    last_rows = density_side[brick_l - 2 :]
    pairs_a = [(i, i ^ 1) for i in range(n_light) if i ^ 1 < n_light]
    pairs_b = [(i, i + 1) for i in range(1, n_light - 1, 2)] + [(i + 1, i) for i in range(1, n_light - 1, 2)]
    got_a = lax.ppermute(jnp.where(odd, first_rows, last_rows), "light", pairs_a)
    got_b = lax.ppermute(jnp.where(odd, last_rows, first_rows), "light", pairs_b)
    padded = jnp.concatenate(
        [jnp.where(odd, got_a, got_b), density_side, jnp.where(odd, got_b, got_a)], axis=0
    )
    inside = (
        rim_mask(light_idx, n_light, brick_l, 1)[:, None, None]
        * rim_mask(across_idx, n_across, brick_a, 1)[None, :, None]
        * rim_mask(view_idx, n_view, brick_v, 1)[None, None, :]
    )
    shading = shade_from(padded, inside)
    lighting = (starts[:, :, None] * jnp.exp(-light_step * running)).reshape(
        3, brick_l, brick_a, brick_v
    )
    optical = looked[0] * density * view_step
    colour = (1.0 - jnp.exp(-optical))[None] * looked[4:7] * (shading[None] * lighting + AMBIENT)
    upper = (jnp.arange(brick_v)[:, None] < jnp.arange(brick_v)[None, :]).astype(jnp.float32)
    before = jnp.dot(optical.reshape(-1, brick_v), upper, precision=lax.Precision.HIGHEST).reshape(
        brick_l, brick_a, brick_v
    )
    colour_sum = jnp.sum(colour * jnp.exp(-before)[None], axis=-1)
    transmit = jnp.exp(-jnp.sum(optical, axis=-1))
    pixels = brick_l * brick_a
    piece_len = pixels // n_view
    image_now = jnp.concatenate(
        [colour_sum.reshape(3, n_view, piece_len), transmit.reshape(1, n_view, piece_len)], axis=0
    )
    bit_count = n_view.bit_length() - 1
    for bit_num in range(bit_count):
        kept = image_now.shape[1]
        pairs = image_now.reshape(4, kept // 2, 2, piece_len)
        my_bit = view_idx // 2**bit_num % 2
        first_half = my_bit == 0
        keep = jnp.where(first_half, pairs[:, :, 0], pairs[:, :, 1])
        send = jnp.where(first_half, pairs[:, :, 1], pairs[:, :, 0])
        got = from_partner(send, "view", bit_num)
        front = jnp.where(first_half, keep, got)
        back = jnp.where(first_half, got, keep)
        image_now = jnp.concatenate(
            [front[:3] + front[3:] * back[:3], keep[3:] * got[3:]], axis=0
        )
    final_colour = image_now[:3, 0]
    final_transmit = image_now[3:, 0]
    rows_out = brick_l // n_view
    opacity = 1.0 - final_transmit.reshape(1, rows_out, brick_a)
    return jnp.concatenate([final_colour.reshape(3, rows_out, brick_a), opacity], axis=0)


def solution(mesh):
    in_specs = (
        P("light", "across", "view"),
        P("light", "across", "view"),
        P(None, "across", "view"),
        P(),
        P(),
        P(),
    )
    out_specs = P(None, ("light", "view"), "across")
    return jax.shard_map(shards, mesh=mesh, in_specs=in_specs, out_specs=out_specs, check_vma=False)
```
